32 devices in a mesh: blk: 8 (over y, x, core), help: 4 (over z).
Axes of the slice: x: 2, y: 2, z: 4, core: 2. Of those that a mesh axis runs over, the one named last changes fastest.
Arguments:
- queries: bfloat16 [512, 8192], P('help', 'blk'), may hold values from -200 to 200
- query_key_value: bfloat16 [512, 2048], P('help'), may hold values from -8 to 8
- cached_key_value: bfloat16 [16384, 2048], P(('blk', 'help')), may hold values from -6 to 6
- selected: int32 [4, 64, 8], P('help'), may hold values from 0 to 15, as said below
Outputs:
- attended: float32 [512, 8192], P('help', 'blk')
The draws below stay inside these ranges and needn't reach their ends.
Inputs may be any that keep to these rules, and one draw needn't show every extreme that they name: `selected`: each query block and head selects 8 distinct context blocks, at most one of each run of 2 blocks c * 2 to (c + 1) * 2 - 1.
All inputs are finite; a program needn't handle non-finite values.
Results may differ from the reference program's by a relative error of at most 0.0058.
Values may be sent and summed in bfloat16 or wider, within the bound.
No kernel may reach another device: no remote copies, remote signals or barrier semaphores. Data moves between devices by JAX's collectives and lax.ppermute only.
A program may use at most 128 MiB of HBM per device.

```python
import math
import jax
import jax.numpy as jnp
from jax import lax

HEAD_SIZE = 128
QUERY_HEADS = 64
KEY_VALUE_HEADS = 8
BLOCK_TOKENS = 1024
QUERY_GROUP_ROWS = 128
TOPK = 8
KB = 2
QUERY_ROW_COUNT = 512
QUERY_BLOCK_COUNT = 4
CONTEXT_BLOCKS = 16
CONTEXT_TOKENS = 16384


def common_fields(key):
    base = jax.random.fold_in(key, 7)
    key_a, random_key_second = jax.random.split(base, 2)
    query = jax.random.normal(key_a, (QUERY_ROW_COUNT, QUERY_HEADS, HEAD_SIZE), jnp.float32)
    fresh_state = jnp.clip(jax.random.normal(random_key_second, (QUERY_ROW_COUNT, 2, KEY_VALUE_HEADS, HEAD_SIZE), jnp.float32), -4.0, 4.0)
    query = jnp.clip(query, -6.0, 6.0)
    return (query, fresh_state)


def draw_queries(key, part):
    query, fresh_state = common_fields(key)
    return query.reshape(QUERY_ROW_COUNT, QUERY_HEADS * HEAD_SIZE).astype(jnp.bfloat16)


def draw_query_key_value(key, part):
    query, fresh_state = common_fields(key)
    return fresh_state.reshape(QUERY_ROW_COUNT, 2 * KEY_VALUE_HEADS * HEAD_SIZE).astype(jnp.bfloat16)


def draw_selected(key, part):
    shards = CONTEXT_BLOCKS // KB
    base = jax.random.fold_in(key, 11)
    key_a, random_key_second = jax.random.split(base)
    noise = jax.random.randint(key_a, (QUERY_BLOCK_COUNT, QUERY_HEADS, shards), 0, 64)
    order = jnp.arange(shards, dtype=jnp.int32)
    bias = jnp.where((order == 0) | (order >= shards - 2), 48, 0).astype(jnp.int32)
    score = (noise + bias[None, None, :]) * shards + order[None, None, :]
    values, chosen = lax.top_k(score, TOPK)
    inner_loop = jax.random.randint(random_key_second, (QUERY_BLOCK_COUNT, QUERY_HEADS, TOPK), 0, KB)
    return (chosen.astype(jnp.int32) * KB + inner_loop).astype(jnp.int32)


def level_of(key, shape, cuts, least, high):
    factor_of = 1.0
    for axis_at, shards_of in cuts:
        heights = jax.random.uniform(jax.random.fold_in(jax.random.fold_in(key, 6), axis_at), (shards_of,), jnp.float32, least / len(cuts), high / len(cuts))
        factor_of = factor_of * jnp.repeat(jnp.exp(heights), shape[axis_at] // shards_of).reshape((-1,) + (1,) * (len(shape) - 1 - axis_at))
    return factor_of


def gaussian(stream_key, extent, width, bound, cuts=(), kind=jnp.bfloat16):
    gain = level_of(stream_key, extent, cuts, -0.22, 0.18) if cuts else 1.0
    array = jax.random.normal(stream_key, extent, jnp.float32) * width * gain
    return jnp.minimum(jnp.maximum(array, -bound), bound).astype(kind)


def setup_inputs(seed: int = 0) -> dict:
    seeds = jax.random.split(jax.random.key(seed), 5)
    queries = draw_queries(jax.random.fold_in(seeds[4], 71), 0)
    query_key_value = draw_query_key_value(jax.random.fold_in(seeds[4], 71), 0)
    cached_key_value = gaussian(seeds[2], (CONTEXT_TOKENS, 2 * KEY_VALUE_HEADS * HEAD_SIZE), 1.0, 6.0, ((0, 32),))
    selected = draw_selected(jax.random.fold_in(seeds[4], 71), 0)
    return {"queries": queries, "query_key_value": query_key_value, "cached_key_value": cached_key_value, "selected": selected}


def reference(queries, query_key_value, cached_key_value, selected):
    scale = 1.0 / math.sqrt(HEAD_SIZE)
    head_group = QUERY_HEADS // KEY_VALUE_HEADS
    selection_table = jnp.transpose(cached_key_value.reshape(CONTEXT_BLOCKS, BLOCK_TOKENS, 2, KEY_VALUE_HEADS, HEAD_SIZE), (0, 3, 2, 1, 4))
    fresh_state = query_key_value.reshape(QUERY_BLOCK_COUNT, QUERY_GROUP_ROWS, 2, KEY_VALUE_HEADS, HEAD_SIZE)
    quer = queries.reshape(QUERY_BLOCK_COUNT, QUERY_GROUP_ROWS, QUERY_HEADS, HEAD_SIZE)
    heads_kv = (jnp.arange(QUERY_HEADS) // head_group).astype(jnp.int32)
    causal = jnp.arange(QUERY_GROUP_ROWS)[:, None] >= jnp.arange(QUERY_GROUP_ROWS)[None, :]

    def one_block(args):
        query_block, own, picks = args
        qf = query_block.astype(jnp.float32)
        chosen = selection_table[picks, heads_kv[:, None]]
        key_rows = chosen[:, :, 0].reshape(QUERY_HEADS, TOPK * BLOCK_TOKENS, HEAD_SIZE).astype(jnp.float32)
        vals = chosen[:, :, 1].reshape(QUERY_HEADS, TOPK * BLOCK_TOKENS, HEAD_SIZE).astype(jnp.float32)
        own_k = own[:, 0][:, heads_kv].astype(jnp.float32)
        own_v = own[:, 1][:, heads_kv].astype(jnp.float32)
        far = jnp.einsum('qhd,hkd->hqk', qf, key_rows) * scale
        near = jnp.einsum('qhd,khd->hqk', qf, own_k) * scale
        near = jnp.where(causal[None], near, -jnp.inf)
        scores = jnp.concatenate([far, near], axis=-1)
        best = lax.optimization_barrier(jnp.max(scores, axis=-1, keepdims=True))
        weight = jnp.exp(scores - best)
        total = lax.optimization_barrier(jnp.sum(weight, axis=-1))
        light = lax.optimization_barrier(weight.astype(jnp.bfloat16)).astype(jnp.float32)
        mixed = jnp.einsum('hqk,hkd->hqd', light[..., :TOPK * BLOCK_TOKENS], vals)
        mixed = mixed + jnp.einsum('hqk,khd->hqd', light[..., TOPK * BLOCK_TOKENS:], own_v)
        out = mixed / total[..., None]
        return jnp.transpose(out, (1, 0, 2)).reshape(QUERY_GROUP_ROWS, QUERY_HEADS * HEAD_SIZE).astype(jnp.float32)
    result = lax.map(one_block, (quer, fresh_state, selected))
    return result.reshape(QUERY_ROW_COUNT, QUERY_HEADS * HEAD_SIZE)
```

```python
import functools
import math

import jax
import jax.numpy as jnp
import numpy as np
from jax import lax
from jax.experimental import pallas as pl
from jax.experimental.pallas import tpu as pltpu
from jax.sharding import PartitionSpec as P

HEAD_SIZE = 128
QUERY_HEADS = 64
KEY_VALUE_HEADS = 8
BLOCK_TOKENS = 1024
QUERY_GROUP_ROWS = 128


def attend_kernel(sel_ref, home_ref, q_ref, kv_ref, own_ref, acc_ref, m_ref, l_ref,
                  s_buf, own_buf, m_scr, l_scr, acc_scr, *, groups, heads, scale):
    b = pl.program_id(0)
    rows = QUERY_GROUP_ROWS
    is_home = b == home_ref[0]
    causal = lax.broadcasted_iota(jnp.int32, (rows, rows), 0) >= lax.broadcasted_iota(
        jnp.int32, (rows, rows), 1)
    contract_last = (((1,), (1,)), ((), ()))

    for h in range(heads):
        q = q_ref[0, :, h * HEAD_SIZE:(h + 1) * HEAD_SIZE]
        base = (b * heads + h) * groups
        m_scr[...] = jnp.full(m_scr.shape, -jnp.inf, jnp.float32)
        l_scr[...] = jnp.zeros(l_scr.shape, jnp.float32)
        acc_scr[...] = jnp.zeros(acc_scr.shape, jnp.float32)

        def scores(g, carry):
            @pl.when(sel_ref[base + g] != 0)
            def _():
                s = lax.dot_general(q, kv_ref[g, 0], contract_last,
                                    preferred_element_type=jnp.float32)
                s_buf[g] = s
                m_scr[...] = jnp.maximum(m_scr[...], jnp.max(s, axis=1, keepdims=True))
            return carry

        lax.fori_loop(0, groups, scores, 0)

        @pl.when(is_home)
        def _():
            s = lax.dot_general(q, own_ref[0], contract_last, preferred_element_type=jnp.float32)
            s = jnp.where(causal, s, -jnp.inf)
            own_buf[...] = s
            m_scr[...] = jnp.maximum(m_scr[...], jnp.max(s, axis=1, keepdims=True))

        def mix(g, carry):
            @pl.when(sel_ref[base + g] != 0)
            def _():
                p = jnp.exp((s_buf[g] - m_scr[...]) * scale)
                l_scr[...] += jnp.sum(p, axis=1, keepdims=True)
                acc_scr[...] += jnp.dot(p.astype(jnp.bfloat16), kv_ref[g, 1],
                                        preferred_element_type=jnp.float32)
            return carry

        lax.fori_loop(0, groups, mix, 0)

        @pl.when(is_home)
        def _():
            p = jnp.exp((own_buf[...] - m_scr[...]) * scale)
            l_scr[...] += jnp.sum(p, axis=1, keepdims=True)
            acc_scr[...] += jnp.dot(p.astype(jnp.bfloat16), own_ref[1],
                                    preferred_element_type=jnp.float32)

        acc_ref[0, :, h * HEAD_SIZE:(h + 1) * HEAD_SIZE] = acc_scr[...]
        m_ref[0, :, h:h + 1] = m_scr[...] * scale
        l_ref[0, :, h:h + 1] = l_scr[...]


def local(queries, query_key_value, cached_key_value, selected):
    rows = queries.shape[0]
    heads = queries.shape[1] // HEAD_SIZE
    head_group = QUERY_HEADS // KEY_VALUE_HEADS
    scale = 1.0 / math.sqrt(HEAD_SIZE)
    groups = lax.axis_size("blk")
    helpers = lax.axis_size("help")
    worker = lax.axis_index("blk")
    helper = lax.axis_index("help")
    piece = cached_key_value.shape[0]
    assert rows == QUERY_GROUP_ROWS and head_group % heads == 0
    assert BLOCK_TOKENS % piece == 0
    per_group = piece * helpers // BLOCK_TOKENS
    query_blocks = helpers

    kv = cached_key_value.reshape(piece, 2, KEY_VALUE_HEADS, HEAD_SIZE)
    kv = jnp.transpose(kv, (2, 1, 0, 3))
    wanted = np.array([(t * heads) // head_group for t in range(groups)], np.int32)
    if not np.array_equal(wanted, np.arange(KEY_VALUE_HEADS)):
        kv = jnp.take(kv, wanted, axis=0)
    held = lax.all_to_all(kv, "blk", 0, 0, tiled=True)

    q_all = lax.all_gather(queries.reshape(1, rows, heads * HEAD_SIZE), "help", axis=0, tiled=True)
    sel_all = lax.all_gather(selected, "help", axis=0, tiled=True)

    kv_head = (worker * heads) // head_group
    own = query_key_value.reshape(rows, 2, KEY_VALUE_HEADS, HEAD_SIZE)
    own = lax.dynamic_index_in_dim(own, kv_head, axis=2, keepdims=False)
    own = jnp.transpose(own, (1, 0, 2))

    my_heads = lax.dynamic_slice_in_dim(sel_all, worker * heads, heads, axis=1)
    piece_block = per_group * jnp.arange(groups, dtype=jnp.int32) + (helper * piece) // BLOCK_TOKENS
    hit = jnp.any(my_heads[:, :, None, :] == piece_block[None, None, :, None], axis=3)
    sel_flat = hit.astype(jnp.int32).reshape(-1)
    home = helper.reshape(1).astype(jnp.int32)

    kernel = functools.partial(attend_kernel, groups=groups, heads=heads, scale=scale)
    width = heads * HEAD_SIZE
    acc, m, l = pl.pallas_call(
        kernel,
        grid_spec=pltpu.PrefetchScalarGridSpec(
            num_scalar_prefetch=2,
            grid=(query_blocks,),
            in_specs=[
                pl.BlockSpec((1, rows, width), lambda b, s, h: (b, 0, 0)),
                pl.BlockSpec((groups, 2, piece, HEAD_SIZE), lambda b, s, h: (0, 0, 0, 0)),
                pl.BlockSpec((2, rows, HEAD_SIZE), lambda b, s, h: (0, 0, 0)),
            ],
            out_specs=[
                pl.BlockSpec((1, rows, width), lambda b, s, h: (b, 0, 0)),
                pl.BlockSpec((1, rows, heads), lambda b, s, h: (b, 0, 0)),
                pl.BlockSpec((1, rows, heads), lambda b, s, h: (b, 0, 0)),
            ],
            scratch_shapes=[
                pltpu.VMEM((groups, rows, piece), jnp.float32),
                pltpu.VMEM((rows, rows), jnp.float32),
                pltpu.VMEM((rows, 1), jnp.float32),
                pltpu.VMEM((rows, 1), jnp.float32),
                pltpu.VMEM((rows, HEAD_SIZE), jnp.float32),
            ],
        ),
        out_shape=[
            jax.ShapeDtypeStruct((query_blocks, rows, width), jnp.float32),
            jax.ShapeDtypeStruct((query_blocks, rows, heads), jnp.float32),
            jax.ShapeDtypeStruct((query_blocks, rows, heads), jnp.float32),
        ],
    )(sel_flat, home, q_all, held, own)

    top = lax.pmax(m, "help")
    fade = jnp.exp(m - top)
    acc = acc.reshape(query_blocks, rows, heads, HEAD_SIZE) * fade[..., None]
    acc = lax.psum_scatter(acc, "help", scatter_dimension=0, tiled=True)
    total = lax.psum_scatter(l * fade, "help", scatter_dimension=0, tiled=True)
    result = acc / total[..., None]
    return result.reshape(rows, width)


def solution(mesh):
    in_specs = (P("help", "blk"), P("help", None), P(("blk", "help"), None), P("help", None, None))
    out_specs = P("help", "blk")
    return jax.shard_map(local, mesh=mesh, in_specs=in_specs, out_specs=out_specs, check_vma=False)
```

```python
import functools
import math

import jax
import jax.numpy as jnp
import numpy as np
from jax import lax
from jax.experimental import pallas as pl
from jax.experimental.pallas import tpu as pltpu
from jax.sharding import PartitionSpec as P

HEAD_SIZE = 128
QUERY_HEADS = 64
KEY_VALUE_HEADS = 8
BLOCK_TOKENS = 1024
QUERY_GROUP_ROWS = 128


def attend_kernel(sel_ref, home_ref, q_ref, kt_ref, v_ref, own_ref, acc_ref, m_ref, l_ref,
                  p_buf, m_scr, l_scr, acc_scr, *, groups, heads, scale):
    b = pl.program_id(0)
    rows = QUERY_GROUP_ROWS
    q = q_ref[0].reshape(heads * rows, HEAD_SIZE)
    m_scr[...] = jnp.full(m_scr.shape, -jnp.inf, jnp.float32)
    l_scr[...] = jnp.zeros(l_scr.shape, jnp.float32)
    acc_scr[...] = jnp.zeros(acc_scr.shape, jnp.float32)

    def update(s, value, bias_of):
        for h in range(heads):
            s_h = s[h * rows:(h + 1) * rows] * scale + bias_of(h)
            m_old = m_scr[h]
            m_new = jnp.maximum(m_old, jnp.max(s_h, axis=1, keepdims=True))
            m_safe = jnp.where(m_new == -jnp.inf, 0.0, m_new)
            alpha = jnp.exp(m_old - m_safe)
            p = jnp.exp(s_h - m_safe)
            l_scr[h] = alpha * l_scr[h] + jnp.sum(p, axis=1, keepdims=True)
            m_scr[h] = m_new
            acc_scr[h] = alpha * acc_scr[h]
            p_buf[h * rows:(h + 1) * rows, :s.shape[1]] = p.astype(jnp.bfloat16)
        width = s.shape[1]
        pv = jnp.dot(p_buf[:, :width], value, preferred_element_type=jnp.float32)
        for h in range(heads):
            acc_scr[h] += pv[h * rows:(h + 1) * rows]

    def piece(g, carry):
        base = b * heads * groups + g

        def bias_of(h):
            return jnp.where(sel_ref[base + h * groups] != 0, 0.0, -jnp.inf)

        s = jnp.dot(q, kt_ref[g], preferred_element_type=jnp.float32)
        update(s, v_ref[g], bias_of)
        return carry

    lax.fori_loop(0, groups, piece, 0)

    @pl.when(b == home_ref[0])
    def _():
        causal = lax.broadcasted_iota(jnp.int32, (rows, rows), 0) >= lax.broadcasted_iota(
            jnp.int32, (rows, rows), 1)
        mask = jnp.where(causal, 0.0, -jnp.inf)
        s = jnp.dot(q, own_ref[0], preferred_element_type=jnp.float32)
        update(s, own_ref[1], lambda h: mask)

    for h in range(heads):
        acc_ref[0, :, h * HEAD_SIZE:(h + 1) * HEAD_SIZE] = acc_scr[h]
        m_ref[0, :, h:h + 1] = m_scr[h]
        l_ref[0, :, h:h + 1] = l_scr[h]


def join(a, b):
    acc_a, m_a, l_a = a
    acc_b, m_b, l_b = b
    m = jnp.maximum(m_a, m_b)
    m_safe = jnp.where(m == -jnp.inf, 0.0, m)
    f_a = jnp.exp(m_a - m_safe)
    f_b = jnp.exp(m_b - m_safe)
    acc = acc_a * f_a[..., None] + acc_b * f_b[..., None]
    return acc, m, l_a * f_a + l_b * f_b


def local(queries, query_key_value, cached_key_value, selected):
    rows = queries.shape[0]
    heads = queries.shape[1] // HEAD_SIZE
    head_group = QUERY_HEADS // KEY_VALUE_HEADS
    scale = 1.0 / math.sqrt(HEAD_SIZE)
    groups = lax.axis_size("blk")
    helpers = lax.axis_size("help")
    worker = lax.axis_index("blk")
    helper = lax.axis_index("help")
    piece = cached_key_value.shape[0]
    picks = selected.shape[1] * selected.shape[2]
    assert rows == QUERY_GROUP_ROWS and head_group % heads == 0 and selected.shape[0] == 1
    assert BLOCK_TOKENS % piece == 0 and picks % HEAD_SIZE == 0 and picks // HEAD_SIZE <= rows
    per_group = piece * helpers // BLOCK_TOKENS
    query_blocks = helpers

    kv = cached_key_value.reshape(piece, 2, KEY_VALUE_HEADS, HEAD_SIZE)
    wanted = np.array([(t * heads) // head_group for t in range(groups)], np.int32)
    keys = jnp.transpose(kv[:, 0], (1, 2, 0))
    values = jnp.transpose(kv[:, 1], (1, 0, 2))
    if not np.array_equal(wanted, np.arange(KEY_VALUE_HEADS)):
        keys = jnp.take(keys, wanted, axis=0)
        values = jnp.take(values, wanted, axis=0)
    keys = lax.all_to_all(keys, "blk", 0, 0, tiled=True)
    values = lax.all_to_all(values, "blk", 0, 0, tiled=True)

    q = jnp.transpose(queries.reshape(rows, heads, HEAD_SIZE), (1, 0, 2))
    sel_rows = selected.reshape(picks // HEAD_SIZE, HEAD_SIZE).astype(jnp.bfloat16)
    sel_rows = jnp.pad(sel_rows, ((0, rows - picks // HEAD_SIZE), (0, 0)))
    q = jnp.concatenate([q, sel_rows[None]], axis=0)
    q_all = lax.all_gather(q[None], "help", axis=0, tiled=True)
    sel_all = q_all[:, heads, :picks // HEAD_SIZE].astype(jnp.int32).reshape(
        query_blocks, selected.shape[1], selected.shape[2])

    kv_head = (worker * heads) // head_group
    own = query_key_value.reshape(rows, 2, KEY_VALUE_HEADS, HEAD_SIZE)
    own = lax.dynamic_index_in_dim(own, kv_head, axis=2, keepdims=False)
    own = jnp.stack([own[:, 0].T, own[:, 1]])

    my_heads = lax.dynamic_slice_in_dim(sel_all, worker * heads, heads, axis=1)
    piece_block = per_group * jnp.arange(groups, dtype=jnp.int32) + (helper * piece) // BLOCK_TOKENS
    hit = jnp.any(my_heads[:, :, None, :] == piece_block[None, None, :, None], axis=3)
    sel_flat = hit.astype(jnp.int32).reshape(-1)
    home = helper.reshape(1).astype(jnp.int32)

    kernel = functools.partial(attend_kernel, groups=groups, heads=heads, scale=scale)
    width = heads * HEAD_SIZE
    acc, m, l = pl.pallas_call(
        kernel,
        grid_spec=pltpu.PrefetchScalarGridSpec(
            num_scalar_prefetch=2,
            grid=(query_blocks,),
            in_specs=[
                pl.BlockSpec((1, heads, rows, HEAD_SIZE), lambda b, s, h: (b, 0, 0, 0)),
                pl.BlockSpec((groups, HEAD_SIZE, piece), lambda b, s, h: (0, 0, 0)),
                pl.BlockSpec((groups, piece, HEAD_SIZE), lambda b, s, h: (0, 0, 0)),
                pl.BlockSpec((2, rows, HEAD_SIZE), lambda b, s, h: (0, 0, 0)),
            ],
            out_specs=[
                pl.BlockSpec((1, rows, width), lambda b, s, h: (b, 0, 0)),
                pl.BlockSpec((1, rows, heads), lambda b, s, h: (b, 0, 0)),
                pl.BlockSpec((1, rows, heads), lambda b, s, h: (b, 0, 0)),
            ],
            scratch_shapes=[
                pltpu.VMEM((heads * rows, max(piece, rows)), jnp.bfloat16),
                pltpu.VMEM((heads, rows, 1), jnp.float32),
                pltpu.VMEM((heads, rows, 1), jnp.float32),
                pltpu.VMEM((heads, rows, HEAD_SIZE), jnp.float32),
            ],
        ),
        out_shape=[
            jax.ShapeDtypeStruct((query_blocks, rows, width), jnp.float32),
            jax.ShapeDtypeStruct((query_blocks, rows, heads), jnp.float32),
            jax.ShapeDtypeStruct((query_blocks, rows, heads), jnp.float32),
        ],
    )(sel_flat, home, q_all, keys, values, own)

    acc = acc.reshape(query_blocks, rows, heads, HEAD_SIZE)
    state = (acc, m, l)

    def pick(t):
        t = jnp.clip(t, 0, query_blocks - 1)
        return tuple(lax.dynamic_index_in_dim(x, t, axis=0, keepdims=False) for x in state)

    def put(t, part, valid):
        t = jnp.clip(t, 0, query_blocks - 1)
        old = pick(t)
        part = (part[0], jnp.where(valid, part[1], -jnp.inf), part[2])
        new = join(old, part)
        return tuple(lax.dynamic_update_index_in_dim(x, y, t, axis=0) for x, y in zip(state, new))

    for r in range(1, helpers):
        right = lax.ppermute(pick(helper + helpers - r), "help",
                             [(z, z + 1) for z in range(0, r)])
        left = lax.ppermute(pick(helper - helpers + r), "help",
                            [(z, z - 1) for z in range(helpers - r, helpers)])
        from_left = (helper >= 1) & (helper <= r)
        state = put(helper - 1 + helpers - r, right, from_left)
        from_right = (helper >= helpers - r - 1) & (helper <= helpers - 2)
        state = put(helper + 1 - helpers + r, left, from_right)

    acc, m, l = pick(helper)
    result = acc / l[..., None]
    return result.reshape(rows, width)


def solution(mesh):
    in_specs = (P("help", "blk"), P("help", None), P(("blk", "help"), None), P("help", None, None))
    out_specs = P("help", "blk")
    return jax.shard_map(local, mesh=mesh, in_specs=in_specs, out_specs=out_specs, check_vma=False)
```

```python
import functools
import math

import jax
import jax.numpy as jnp
import numpy as np
from jax import lax
from jax.experimental import pallas as pl
from jax.experimental.pallas import tpu as pltpu
from jax.sharding import PartitionSpec as P

HEAD_SIZE = 128
QUERY_HEADS = 64
KEY_VALUE_HEADS = 8
BLOCK_TOKENS = 1024
QUERY_GROUP_ROWS = 128


def attend_kernel(sel_ref, home_ref, q_ref, kv_ref, own_ref, acc_ref, m_ref, l_ref,
                  p_buf, m_scr, l_scr, acc_scr, *, groups, heads, chunks, factor):
    b = pl.program_id(0)
    rows = QUERY_GROUP_ROWS
    q = q_ref[0].reshape(heads * rows, HEAD_SIZE)
    m_scr[...] = jnp.full(m_scr.shape, -jnp.inf, jnp.float32)
    l_scr[...] = jnp.zeros(l_scr.shape, jnp.float32)
    acc_scr[...] = jnp.zeros(acc_scr.shape, jnp.float32)

    def update(s, value, on_of, mask):
        width = s.shape[1]
        for h in range(heads):
            on = on_of(h)

            @pl.when(on)
            def _():
                s_h = s[h * rows:(h + 1) * rows] * factor
                if mask is not None:
                    s_h = jnp.where(mask, s_h, -jnp.inf)
                m_old = m_scr[h]
                m_new = jnp.maximum(m_old, jnp.max(s_h, axis=1, keepdims=True))
                m_safe = jnp.where(m_new == -jnp.inf, 0.0, m_new)
                alpha = jnp.exp2(m_old - m_safe)
                p = jnp.exp2(s_h - m_safe)
                l_scr[h] = alpha * l_scr[h] + jnp.sum(p, axis=1, keepdims=True)
                m_scr[h] = m_new
                acc_scr[h] = alpha * acc_scr[h]
                p_buf[h * rows:(h + 1) * rows, :width] = p.astype(jnp.bfloat16)

            @pl.when(jnp.logical_not(on))
            def _():
                p_buf[h * rows:(h + 1) * rows, :width] = jnp.zeros((rows, width), jnp.bfloat16)

        pv = jnp.dot(p_buf[:, :width], value, preferred_element_type=jnp.float32)
        for h in range(heads):
            @pl.when(on_of(h))
            def _():
                acc_scr[h] += pv[h * rows:(h + 1) * rows]

    def piece(g, carry):
        base = b * heads * groups + g
        if chunks == 1:
            s = jnp.dot(q, kv_ref[g, 0, 0], preferred_element_type=jnp.float32)
        else:
            s = jnp.concatenate(
                [jnp.dot(q, kv_ref[g, 0, c], preferred_element_type=jnp.float32)
                 for c in range(chunks)], axis=1)
        value = kv_ref[g, 1].reshape(chunks * HEAD_SIZE, HEAD_SIZE)
        update(s, value, lambda h: sel_ref[base + h * groups] != 0, None)
        return carry

    lax.fori_loop(0, groups, piece, 0)

    @pl.when(b == home_ref[0])
    def _():
        causal = lax.broadcasted_iota(jnp.int32, (rows, rows), 0) >= lax.broadcasted_iota(
            jnp.int32, (rows, rows), 1)
        s = jnp.dot(q, own_ref[0], preferred_element_type=jnp.float32)
        update(s, own_ref[1], lambda h: True, causal)

    for h in range(heads):
        acc_ref[0, :, h * HEAD_SIZE:(h + 1) * HEAD_SIZE] = acc_scr[h]
        m_ref[0, :, h:h + 1] = m_scr[h]
        l_ref[0, :, h:h + 1] = l_scr[h]


def join(a, b):
    acc_a, m_a, l_a = a
    acc_b, m_b, l_b = b
    m = jnp.maximum(m_a, m_b)
    m_safe = jnp.where(m == -jnp.inf, 0.0, m)
    f_a = jnp.exp2(m_a - m_safe)
    f_b = jnp.exp2(m_b - m_safe)
    acc = acc_a * f_a[..., None] + acc_b * f_b[..., None]
    return acc, m, l_a * f_a + l_b * f_b


def local(queries, query_key_value, cached_key_value, selected):
    rows = queries.shape[0]
    heads = queries.shape[1] // HEAD_SIZE
    head_group = QUERY_HEADS // KEY_VALUE_HEADS
    scale = 1.0 / math.sqrt(HEAD_SIZE)
    groups = lax.axis_size("blk")
    helpers = lax.axis_size("help")
    worker = lax.axis_index("blk")
    helper = lax.axis_index("help")
    piece = cached_key_value.shape[0]
    picks = selected.shape[1] * selected.shape[2]
    assert rows == QUERY_GROUP_ROWS and head_group % heads == 0 and selected.shape[0] == 1
    assert BLOCK_TOKENS % piece == 0 and piece % HEAD_SIZE == 0 and picks % HEAD_SIZE == 0 and picks // HEAD_SIZE <= rows
    per_group = piece * helpers // BLOCK_TOKENS
    query_blocks = helpers

    kv = cached_key_value.reshape(piece, 2, KEY_VALUE_HEADS, HEAD_SIZE)
    wanted = np.array([(t * heads) // head_group for t in range(groups)], np.int32)
    if not np.array_equal(wanted, np.arange(KEY_VALUE_HEADS)):
        kv = jnp.take(kv, wanted, axis=2)
    chunks = piece // HEAD_SIZE
    kv = kv.reshape(chunks, HEAD_SIZE, 2, groups, HEAD_SIZE)
    keys = jnp.transpose(kv[:, :, 0], (2, 0, 3, 1))
    values = jnp.transpose(kv[:, :, 1], (2, 0, 1, 3))
    held = lax.all_to_all(jnp.stack([keys, values], axis=1), "blk", 0, 0, tiled=True)

    q = jnp.transpose(queries.reshape(rows, heads, HEAD_SIZE), (1, 0, 2))
    sel_rows = selected.reshape(picks // HEAD_SIZE, HEAD_SIZE).astype(jnp.bfloat16)
    sel_rows = jnp.pad(sel_rows, ((0, rows - picks // HEAD_SIZE), (0, 0)))
    q = jnp.concatenate([q, sel_rows[None]], axis=0)
    q_all = lax.all_gather(q[None], "help", axis=0, tiled=True)
    sel_all = q_all[:, heads, :picks // HEAD_SIZE].astype(jnp.int32).reshape(
        query_blocks, selected.shape[1], selected.shape[2])

    kv_head = (worker * heads) // head_group
    own = query_key_value.reshape(rows, 2, KEY_VALUE_HEADS, HEAD_SIZE)
    own = lax.dynamic_index_in_dim(own, kv_head, axis=2, keepdims=False)
    own = jnp.stack([own[:, 0].T, own[:, 1]])

    my_heads = lax.dynamic_slice_in_dim(sel_all, worker * heads, heads, axis=1)
    piece_block = per_group * jnp.arange(groups, dtype=jnp.int32) + (helper * piece) // BLOCK_TOKENS
    hit = jnp.any(my_heads[:, :, None, :] == piece_block[None, None, :, None], axis=3)
    sel_flat = hit.astype(jnp.int32).reshape(-1)
    home = helper.reshape(1).astype(jnp.int32)

    kernel = functools.partial(attend_kernel, groups=groups, heads=heads, chunks=chunks,
                               factor=scale * math.log2(math.e))
    width = heads * HEAD_SIZE
    acc, m, l = pl.pallas_call(
        kernel,
        grid_spec=pltpu.PrefetchScalarGridSpec(
            num_scalar_prefetch=2,
            grid=(query_blocks,),
            in_specs=[
                pl.BlockSpec((1, heads, rows, HEAD_SIZE), lambda b, s, h: (b, 0, 0, 0)),
                pl.BlockSpec((groups, 2, chunks, HEAD_SIZE, HEAD_SIZE), lambda b, s, h: (0, 0, 0, 0, 0)),
                pl.BlockSpec((2, rows, HEAD_SIZE), lambda b, s, h: (0, 0, 0)),
            ],
            out_specs=[
                pl.BlockSpec((1, rows, width), lambda b, s, h: (b, 0, 0)),
                pl.BlockSpec((1, rows, heads), lambda b, s, h: (b, 0, 0)),
                pl.BlockSpec((1, rows, heads), lambda b, s, h: (b, 0, 0)),
            ],
            scratch_shapes=[
                pltpu.VMEM((heads * rows, max(piece, rows)), jnp.bfloat16),
                pltpu.VMEM((heads, rows, 1), jnp.float32),
                pltpu.VMEM((heads, rows, 1), jnp.float32),
                pltpu.VMEM((heads, rows, HEAD_SIZE), jnp.float32),
            ],
        ),
        out_shape=[
            jax.ShapeDtypeStruct((query_blocks, rows, width), jnp.float32),
            jax.ShapeDtypeStruct((query_blocks, rows, heads), jnp.float32),
            jax.ShapeDtypeStruct((query_blocks, rows, heads), jnp.float32),
        ],
    )(sel_flat, home, q_all, held, own)

    acc = acc.reshape(query_blocks, rows, heads, HEAD_SIZE)
    state = (acc, m, l)

    def pick(t):
        t = jnp.clip(t, 0, query_blocks - 1)
        return tuple(lax.dynamic_index_in_dim(x, t, axis=0, keepdims=False) for x in state)

    def put(t, part, valid):
        t = jnp.clip(t, 0, query_blocks - 1)
        old = pick(t)
        part = (part[0], jnp.where(valid, part[1], -jnp.inf), part[2])
        new = join(old, part)
        return tuple(lax.dynamic_update_index_in_dim(x, y, t, axis=0) for x, y in zip(state, new))

    for r in range(1, helpers):
        right = lax.ppermute(pick(helper + helpers - r), "help",
                             [(z, z + 1) for z in range(0, r)])
        left = lax.ppermute(pick(helper - helpers + r), "help",
                            [(z, z - 1) for z in range(helpers - r, helpers)])
        from_left = (helper >= 1) & (helper <= r)
        state = put(helper - 1 + helpers - r, right, from_left)
        from_right = (helper >= helpers - r - 1) & (helper <= helpers - 2)
        state = put(helper + 1 - helpers + r, left, from_right)

    acc, m, l = pick(helper)
    result = acc / l[..., None]
    return result.reshape(rows, width)


def solution(mesh):
    in_specs = (P("help", "blk"), P("help", None), P(("blk", "help"), None), P("help", None, None))
    out_specs = P("help", "blk")
    return jax.shard_map(local, mesh=mesh, in_specs=in_specs, out_specs=out_specs, check_vma=False)
```

```python
import functools
import math

import jax
import jax.numpy as jnp
import numpy as np
from jax import lax
from jax.experimental import pallas as pl
from jax.experimental.pallas import tpu as pltpu
from jax.sharding import PartitionSpec as P

HEAD_SIZE = 128
QUERY_HEADS = 64
KEY_VALUE_HEADS = 8
BLOCK_TOKENS = 1024
QUERY_GROUP_ROWS = 128


def attend_kernel(sel_ref, home_ref, q_ref, kv_ref, own_ref, out_ref,
                  p_buf, m_scr, l_scr, acc_scr, *, groups, heads, first, all_heads, chunks, factor):
    b = pl.program_id(0)
    rows = QUERY_GROUP_ROWS
    q = q_ref[0].reshape(heads * rows, HEAD_SIZE)
    m_scr[...] = jnp.full(m_scr.shape, -jnp.inf, jnp.float32)
    l_scr[...] = jnp.zeros(l_scr.shape, jnp.float32)
    acc_scr[...] = jnp.zeros(acc_scr.shape, jnp.float32)

    def update(s, value, on_of, mask):
        width = s.shape[1]
        for h in range(heads):
            on = on_of(h)

            @pl.when(on)
            def _():
                s_h = s[h * rows:(h + 1) * rows] * factor
                if mask is not None:
                    s_h = jnp.where(mask, s_h, -jnp.inf)
                m_old = m_scr[h]
                m_new = jnp.maximum(m_old, jnp.max(s_h, axis=1, keepdims=True))
                m_safe = jnp.where(m_new == -jnp.inf, 0.0, m_new)
                alpha = jnp.exp2(m_old - m_safe)
                p = jnp.exp2(s_h - m_safe)
                l_scr[h] = alpha * l_scr[h] + jnp.sum(p, axis=1, keepdims=True)
                m_scr[h] = m_new
                acc_scr[h] = alpha * acc_scr[h]
                p_buf[h * rows:(h + 1) * rows, :width] = p.astype(jnp.bfloat16)

            @pl.when(jnp.logical_not(on))
            def _():
                p_buf[h * rows:(h + 1) * rows, :width] = jnp.zeros((rows, width), jnp.bfloat16)

        pv = jnp.dot(p_buf[:, :width], value, preferred_element_type=jnp.float32)
        for h in range(heads):
            @pl.when(on_of(h))
            def _():
                acc_scr[h] += pv[h * rows:(h + 1) * rows]

    def piece(g, carry):
        base = (b * all_heads + first) * groups + g
        if chunks == 1:
            s = jnp.dot(q, kv_ref[g, 0, 0], preferred_element_type=jnp.float32)
        else:
            s = jnp.concatenate(
                [jnp.dot(q, kv_ref[g, 0, c], preferred_element_type=jnp.float32)
                 for c in range(chunks)], axis=1)
        value = kv_ref[g, 1].reshape(chunks * HEAD_SIZE, HEAD_SIZE)
        update(s, value, lambda h: sel_ref[base + h * groups] != 0, None)
        return carry

    lax.fori_loop(0, groups, piece, 0)

    @pl.when(b == home_ref[0])
    def _():
        causal = lax.broadcasted_iota(jnp.int32, (rows, rows), 0) >= lax.broadcasted_iota(
            jnp.int32, (rows, rows), 1)
        s = jnp.dot(q, own_ref[0], preferred_element_type=jnp.float32)
        update(s, own_ref[1], lambda h: True, causal)

    stats = heads * HEAD_SIZE
    out_ref[0, :, stats:] = jnp.zeros((rows, HEAD_SIZE), jnp.float32)
    for h in range(heads):
        out_ref[0, :, h * HEAD_SIZE:(h + 1) * HEAD_SIZE] = acc_scr[h]
        out_ref[0, :, stats + h:stats + h + 1] = m_scr[h]
        out_ref[0, :, stats + heads + h:stats + heads + h + 1] = l_scr[h]


def join(a, b):
    acc_a, m_a, l_a = a
    acc_b, m_b, l_b = b
    m = jnp.maximum(m_a, m_b)
    m_safe = jnp.where(m == -jnp.inf, 0.0, m)
    f_a = jnp.exp2(m_a - m_safe)
    f_b = jnp.exp2(m_b - m_safe)
    acc = acc_a * f_a[..., None] + acc_b * f_b[..., None]
    return acc, m, l_a * f_a + l_b * f_b


def local(queries, query_key_value, cached_key_value, selected):
    rows = queries.shape[0]
    heads = queries.shape[1] // HEAD_SIZE
    head_group = QUERY_HEADS // KEY_VALUE_HEADS
    scale = 1.0 / math.sqrt(HEAD_SIZE)
    groups = lax.axis_size("blk")
    helpers = lax.axis_size("help")
    worker = lax.axis_index("blk")
    helper = lax.axis_index("help")
    piece = cached_key_value.shape[0]
    picks = selected.shape[1] * selected.shape[2]
    assert rows == QUERY_GROUP_ROWS and head_group % heads == 0 and selected.shape[0] == 1
    assert BLOCK_TOKENS % piece == 0 and piece % HEAD_SIZE == 0 and picks % HEAD_SIZE == 0 and picks // HEAD_SIZE <= rows
    per_group = piece * helpers // BLOCK_TOKENS
    query_blocks = helpers

    kv = cached_key_value.reshape(piece, 2, KEY_VALUE_HEADS, HEAD_SIZE)
    wanted = np.array([(t * heads) // head_group for t in range(groups)], np.int32)
    if not np.array_equal(wanted, np.arange(KEY_VALUE_HEADS)):
        kv = jnp.take(kv, wanted, axis=2)
    chunks = piece // HEAD_SIZE
    kv = kv.reshape(chunks, HEAD_SIZE, 2, groups, HEAD_SIZE)
    keys = jnp.transpose(kv[:, :, 0], (2, 0, 3, 1))
    values = jnp.transpose(kv[:, :, 1], (2, 0, 1, 3))
    held = lax.all_to_all(jnp.stack([keys, values], axis=1), "blk", 0, 0, tiled=True)

    q = jnp.transpose(queries.reshape(rows, heads, HEAD_SIZE), (1, 0, 2))
    sel_rows = selected.reshape(picks // HEAD_SIZE, HEAD_SIZE).astype(jnp.bfloat16)
    sel_rows = jnp.pad(sel_rows, ((0, rows - picks // HEAD_SIZE), (0, 0)))
    q = jnp.concatenate([q, sel_rows[None]], axis=0)
    q_all = lax.all_gather(q[None], "help", axis=0, tiled=True)
    sel_all = q_all[:, heads, :picks // HEAD_SIZE].astype(jnp.int32).reshape(
        query_blocks, selected.shape[1], selected.shape[2])

    kv_head = (worker * heads) // head_group
    own = query_key_value.reshape(rows, 2, KEY_VALUE_HEADS, HEAD_SIZE)
    own = lax.dynamic_index_in_dim(own, kv_head, axis=2, keepdims=False)
    own = jnp.stack([own[:, 0].T, own[:, 1]])

    my_heads = lax.dynamic_slice_in_dim(sel_all, worker * heads, heads, axis=1)
    piece_block = per_group * jnp.arange(groups, dtype=jnp.int32) + (helper * piece) // BLOCK_TOKENS
    hit = jnp.any(my_heads[:, :, None, :] == piece_block[None, None, :, None], axis=3)
    sel_flat = hit.astype(jnp.int32).reshape(-1)
    home = helper.reshape(1).astype(jnp.int32)

    slices = min(4, heads)
    part = heads // slices
    assert part * slices == heads and 2 * part <= HEAD_SIZE
    width = (part + 1) * HEAD_SIZE
    outs = []
    for c in range(slices):
        kernel = functools.partial(attend_kernel, groups=groups, heads=part, first=c * part,
                                   all_heads=heads, chunks=chunks, factor=scale * math.log2(math.e))
        partial = pl.pallas_call(
            kernel,
            grid_spec=pltpu.PrefetchScalarGridSpec(
                num_scalar_prefetch=2,
                grid=(query_blocks,),
                in_specs=[
                    pl.BlockSpec((1, part, rows, HEAD_SIZE), lambda b, s, h, c=c: (b, c, 0, 0)),
                    pl.BlockSpec((groups, 2, chunks, HEAD_SIZE, HEAD_SIZE),
                                 lambda b, s, h: (0, 0, 0, 0, 0)),
                    pl.BlockSpec((2, rows, HEAD_SIZE), lambda b, s, h: (0, 0, 0)),
                ],
                out_specs=pl.BlockSpec((1, rows, width), lambda b, s, h: (b, 0, 0)),
                scratch_shapes=[
                    pltpu.VMEM((part * rows, max(piece, rows)), jnp.bfloat16),
                    pltpu.VMEM((part, rows, 1), jnp.float32),
                    pltpu.VMEM((part, rows, 1), jnp.float32),
                    pltpu.VMEM((part, rows, HEAD_SIZE), jnp.float32),
                ],
            ),
            out_shape=jax.ShapeDtypeStruct((query_blocks, rows, width), jnp.float32),
            cost_estimate=pl.CostEstimate(
                flops=4 * query_blocks * part * rows * groups * piece * HEAD_SIZE,
                transcendentals=query_blocks * part * rows * groups * piece,
                bytes_accessed=2 * groups * 2 * piece * HEAD_SIZE + 4 * query_blocks * rows * width),
        )(sel_flat, home, q_all, held, own)
        got = lax.all_to_all(partial, "help", 0, 0, tiled=True)
        acc = got[:, :, :part * HEAD_SIZE].reshape(helpers, rows, part, HEAD_SIZE)
        m = got[:, :, part * HEAD_SIZE:part * HEAD_SIZE + part]
        l = got[:, :, part * HEAD_SIZE + part:part * HEAD_SIZE + 2 * part]
        top = jnp.max(m, axis=0)
        fade = jnp.exp2(m - jnp.where(top == -jnp.inf, 0.0, top))
        total = jnp.sum(l * fade, axis=0)
        acc = jnp.sum(acc * fade[..., None], axis=0)
        outs.append((acc / total[..., None]).reshape(rows, part * HEAD_SIZE))
    return jnp.concatenate(outs, axis=1)


def solution(mesh):
    in_specs = (P("help", "blk"), P("help", None), P(("blk", "help"), None), P("help", None, None))
    out_specs = P("help", "blk")
    return jax.shard_map(local, mesh=mesh, in_specs=in_specs, out_specs=out_specs, check_vma=False)
```

```python
import functools
import math

import jax
import jax.numpy as jnp
import numpy as np
from jax import lax
from jax.experimental import pallas as pl
from jax.experimental.pallas import tpu as pltpu
from jax.sharding import PartitionSpec as P

HEAD_SIZE = 128
QUERY_HEADS = 64
KEY_VALUE_HEADS = 8
BLOCK_TOKENS = 1024
QUERY_GROUP_ROWS = 128


def attend_kernel(sel_ref, home_ref, q_ref, kv_ref, own_ref, out_ref,
                  p_buf, m_scr, l_scr, acc_scr, *, groups, heads, first, all_heads, blocks, chunks,
                  factor):
    rows = QUERY_GROUP_ROWS
    slots = blocks * heads
    q = q_ref[...].reshape(slots * rows, HEAD_SIZE)
    m_scr[...] = jnp.full(m_scr.shape, -jnp.inf, jnp.float32)
    l_scr[...] = jnp.zeros(l_scr.shape, jnp.float32)
    acc_scr[...] = jnp.zeros(acc_scr.shape, jnp.float32)

    def soften(s_h, slot, mask):
        s_h = s_h * factor
        if mask is not None:
            s_h = jnp.where(mask, s_h, -jnp.inf)
        m_old = m_scr[slot]
        m_new = jnp.maximum(m_old, jnp.max(s_h, axis=1, keepdims=True))
        m_safe = jnp.where(m_new == -jnp.inf, 0.0, m_new)
        alpha = jnp.exp2(m_old - m_safe)
        p = jnp.exp2(s_h - m_safe)
        l_scr[slot] = alpha * l_scr[slot] + jnp.sum(p, axis=1, keepdims=True)
        m_scr[slot] = m_new
        acc_scr[slot] = alpha * acc_scr[slot]
        return p.astype(jnp.bfloat16)

    def piece(g, carry):
        if chunks == 1:
            s = jnp.dot(q, kv_ref[g, 0, 0], preferred_element_type=jnp.float32)
        else:
            s = jnp.concatenate(
                [jnp.dot(q, kv_ref[g, 0, c], preferred_element_type=jnp.float32)
                 for c in range(chunks)], axis=1)
        width = s.shape[1]
        ons = []
        for slot in range(slots):
            b, h = divmod(slot, heads)
            on = sel_ref[(b * all_heads + first + h) * groups + g] != 0
            ons.append(on)

            @pl.when(on)
            def _():
                p_buf[slot * rows:(slot + 1) * rows, :width] = soften(
                    s[slot * rows:(slot + 1) * rows], slot, None)

            @pl.when(jnp.logical_not(on))
            def _():
                p_buf[slot * rows:(slot + 1) * rows, :width] = jnp.zeros((rows, width), jnp.bfloat16)

        value = kv_ref[g, 1].reshape(chunks * HEAD_SIZE, HEAD_SIZE)
        pv = jnp.dot(p_buf[:, :width], value, preferred_element_type=jnp.float32)
        for slot in range(slots):
            @pl.when(ons[slot])
            def _():
                acc_scr[slot] += pv[slot * rows:(slot + 1) * rows]
        return carry

    lax.fori_loop(0, groups, piece, 0)

    home = home_ref[0]
    causal = lax.broadcasted_iota(jnp.int32, (rows, rows), 0) >= lax.broadcasted_iota(
        jnp.int32, (rows, rows), 1)
    q_home = q_ref[home].reshape(heads * rows, HEAD_SIZE)
    s = jnp.dot(q_home, own_ref[0], preferred_element_type=jnp.float32)
    for h in range(heads):
        slot = home * heads + h
        p = soften(s[h * rows:(h + 1) * rows], slot, causal)
        acc_scr[slot] += jnp.dot(p, own_ref[1], preferred_element_type=jnp.float32)

    stats = heads * HEAD_SIZE
    for b in range(blocks):
        out_ref[b, :, stats:] = jnp.zeros((rows, HEAD_SIZE), jnp.float32)
        for h in range(heads):
            slot = b * heads + h
            out_ref[b, :, h * HEAD_SIZE:(h + 1) * HEAD_SIZE] = acc_scr[slot]
            out_ref[b, :, stats + h:stats + h + 1] = m_scr[slot]
            out_ref[b, :, stats + heads + h:stats + heads + h + 1] = l_scr[slot]


def join(a, b):
    acc_a, m_a, l_a = a
    acc_b, m_b, l_b = b
    m = jnp.maximum(m_a, m_b)
    m_safe = jnp.where(m == -jnp.inf, 0.0, m)
    f_a = jnp.exp2(m_a - m_safe)
    f_b = jnp.exp2(m_b - m_safe)
    acc = acc_a * f_a[..., None] + acc_b * f_b[..., None]
    return acc, m, l_a * f_a + l_b * f_b


def local(queries, query_key_value, cached_key_value, selected):
    rows = queries.shape[0]
    heads = queries.shape[1] // HEAD_SIZE
    head_group = QUERY_HEADS // KEY_VALUE_HEADS
    scale = 1.0 / math.sqrt(HEAD_SIZE)
    groups = lax.axis_size("blk")
    helpers = lax.axis_size("help")
    worker = lax.axis_index("blk")
    helper = lax.axis_index("help")
    piece = cached_key_value.shape[0]
    picks = selected.shape[1] * selected.shape[2]
    assert rows == QUERY_GROUP_ROWS and head_group % heads == 0 and selected.shape[0] == 1
    assert BLOCK_TOKENS % piece == 0 and piece % HEAD_SIZE == 0 and picks % HEAD_SIZE == 0 and picks // HEAD_SIZE <= rows
    per_group = piece * helpers // BLOCK_TOKENS
    query_blocks = helpers

    kv = cached_key_value.reshape(piece, 2, KEY_VALUE_HEADS, HEAD_SIZE)
    wanted = np.array([(t * heads) // head_group for t in range(groups)], np.int32)
    if not np.array_equal(wanted, np.arange(KEY_VALUE_HEADS)):
        kv = jnp.take(kv, wanted, axis=2)
    chunks = piece // HEAD_SIZE
    kv = kv.reshape(chunks, HEAD_SIZE, 2, groups, HEAD_SIZE)
    keys = jnp.transpose(kv[:, :, 0], (2, 0, 3, 1))
    values = jnp.transpose(kv[:, :, 1], (2, 0, 1, 3))
    held = lax.all_to_all(jnp.stack([keys, values], axis=1), "blk", 0, 0, tiled=True)

    q = jnp.transpose(queries.reshape(rows, heads, HEAD_SIZE), (1, 0, 2))
    sel_rows = selected.reshape(picks // HEAD_SIZE, HEAD_SIZE).astype(jnp.bfloat16)
    sel_rows = jnp.pad(sel_rows, ((0, rows - picks // HEAD_SIZE), (0, 0)))
    q = jnp.concatenate([q, sel_rows[None]], axis=0)
    q_all = lax.all_gather(q[None], "help", axis=0, tiled=True)
    sel_all = q_all[:, heads, :picks // HEAD_SIZE].astype(jnp.int32).reshape(
        query_blocks, selected.shape[1], selected.shape[2])

    kv_head = (worker * heads) // head_group
    own = query_key_value.reshape(rows, 2, KEY_VALUE_HEADS, HEAD_SIZE)
    own = lax.dynamic_index_in_dim(own, kv_head, axis=2, keepdims=False)
    own = jnp.stack([own[:, 0].T, own[:, 1]])

    my_heads = lax.dynamic_slice_in_dim(sel_all, worker * heads, heads, axis=1)
    piece_block = per_group * jnp.arange(groups, dtype=jnp.int32) + (helper * piece) // BLOCK_TOKENS
    hit = jnp.any(my_heads[:, :, None, :] == piece_block[None, None, :, None], axis=3)
    sel_flat = hit.astype(jnp.int32).reshape(-1)
    home = helper.reshape(1).astype(jnp.int32)

    slices = min(4, heads)
    part = heads // slices
    assert part * slices == heads and 2 * part <= HEAD_SIZE
    width = (part + 1) * HEAD_SIZE
    outs = []
    for c in range(slices):
        kernel = functools.partial(attend_kernel, groups=groups, heads=part, first=c * part,
                                   all_heads=heads, blocks=query_blocks, chunks=chunks,
                                   factor=scale * math.log2(math.e))
        slots = query_blocks * part
        partial = pl.pallas_call(
            kernel,
            grid_spec=pltpu.PrefetchScalarGridSpec(
                num_scalar_prefetch=2,
                grid=(1,),
                in_specs=[
                    pl.BlockSpec((query_blocks, part, rows, HEAD_SIZE),
                                 lambda i, s, h, c=c: (0, c, 0, 0)),
                    pl.BlockSpec((groups, 2, chunks, HEAD_SIZE, HEAD_SIZE),
                                 lambda i, s, h: (0, 0, 0, 0, 0)),
                    pl.BlockSpec((2, rows, HEAD_SIZE), lambda i, s, h: (0, 0, 0)),
                ],
                out_specs=pl.BlockSpec((query_blocks, rows, width), lambda i, s, h: (0, 0, 0)),
                scratch_shapes=[
                    pltpu.VMEM((slots * rows, piece), jnp.bfloat16),
                    pltpu.VMEM((slots, rows, 1), jnp.float32),
                    pltpu.VMEM((slots, rows, 1), jnp.float32),
                    pltpu.VMEM((slots, rows, HEAD_SIZE), jnp.float32),
                ],
            ),
            out_shape=jax.ShapeDtypeStruct((query_blocks, rows, width), jnp.float32),
            cost_estimate=pl.CostEstimate(
                flops=4 * query_blocks * part * rows * groups * piece * HEAD_SIZE,
                transcendentals=query_blocks * part * rows * groups * piece,
                bytes_accessed=2 * groups * 2 * piece * HEAD_SIZE + 4 * query_blocks * rows * width),
        )(sel_flat, home, q_all, held, own)
        got = lax.all_to_all(partial, "help", 0, 0, tiled=True)
        acc = got[:, :, :part * HEAD_SIZE].reshape(helpers, rows, part, HEAD_SIZE)
        m = got[:, :, part * HEAD_SIZE:part * HEAD_SIZE + part]
        l = got[:, :, part * HEAD_SIZE + part:part * HEAD_SIZE + 2 * part]
        top = jnp.max(m, axis=0)
        fade = jnp.exp2(m - jnp.where(top == -jnp.inf, 0.0, top))
        total = jnp.sum(l * fade, axis=0)
        acc = jnp.sum(acc * fade[..., None], axis=0)
        outs.append((acc / total[..., None]).reshape(rows, part * HEAD_SIZE))
    return jnp.concatenate(outs, axis=1)


def solution(mesh):
    in_specs = (P("help", "blk"), P("help", None), P(("blk", "help"), None), P("help", None, None))
    out_specs = P("help", "blk")
    return jax.shard_map(local, mesh=mesh, in_specs=in_specs, out_specs=out_specs, check_vma=False)
```

```python
import functools
import math

import jax
import jax.numpy as jnp
import numpy as np
from jax import lax
from jax.experimental import pallas as pl
from jax.experimental.pallas import tpu as pltpu
from jax.sharding import PartitionSpec as P

HEAD_SIZE = 128
QUERY_HEADS = 64
KEY_VALUE_HEADS = 8
BLOCK_TOKENS = 1024
QUERY_GROUP_ROWS = 128


def attend_kernel(sel_ref, home_ref, q_ref, kv_ref, own_ref, out_ref,
                  p_buf, m_scr, l_scr, acc_scr, *, groups, heads, first, all_heads, blocks, chunks,
                  factor):
    rows = QUERY_GROUP_ROWS
    slots = blocks * heads
    q = q_ref[...].reshape(slots * rows, HEAD_SIZE)
    m_scr[...] = jnp.full(m_scr.shape, -jnp.inf, jnp.float32)
    l_scr[...] = jnp.zeros(l_scr.shape, jnp.float32)
    acc_scr[...] = jnp.zeros(acc_scr.shape, jnp.float32)

    def soften(s_h, slot, mask):
        if mask is not None:
            s_h = jnp.where(mask, s_h, -jnp.inf)
        m_old = m_scr[slot]
        m_new = jnp.maximum(m_old, jnp.max(s_h, axis=1, keepdims=True) * factor)
        m_safe = jnp.where(m_new == -jnp.inf, 0.0, m_new)
        alpha = jnp.exp2(m_old - m_safe)
        p = jnp.exp2(s_h * factor - m_safe)
        l_scr[slot] = alpha * l_scr[slot] + jnp.sum(p, axis=1, keepdims=True)
        m_scr[slot] = m_new
        acc_scr[slot] = alpha * acc_scr[slot]
        return p.astype(jnp.bfloat16)

    def piece(g, carry):
        if chunks == 1:
            s = jnp.dot(q, kv_ref[g, 0, 0], preferred_element_type=jnp.float32)
        else:
            s = jnp.concatenate(
                [jnp.dot(q, kv_ref[g, 0, c], preferred_element_type=jnp.float32)
                 for c in range(chunks)], axis=1)
        width = s.shape[1]
        ons = []
        for slot in range(slots):
            b, h = divmod(slot, heads)
            on = sel_ref[(b * all_heads + first + h) * groups + g] != 0
            ons.append(on)

            @pl.when(on)
            def _():
                p_buf[slot * rows:(slot + 1) * rows, :width] = soften(
                    s[slot * rows:(slot + 1) * rows], slot, None)

            @pl.when(jnp.logical_not(on))
            def _():
                p_buf[slot * rows:(slot + 1) * rows, :width] = jnp.zeros((rows, width), jnp.bfloat16)

        value = kv_ref[g, 1].reshape(chunks * HEAD_SIZE, HEAD_SIZE)
        pv = jnp.dot(p_buf[:, :width], value, preferred_element_type=jnp.float32)
        for slot in range(slots):
            @pl.when(ons[slot])
            def _():
                acc_scr[slot] += pv[slot * rows:(slot + 1) * rows]
        return carry

    lax.fori_loop(0, groups, piece, 0)

    home = home_ref[0]
    causal = lax.broadcasted_iota(jnp.int32, (rows, rows), 0) >= lax.broadcasted_iota(
        jnp.int32, (rows, rows), 1)
    q_home = q_ref[home].reshape(heads * rows, HEAD_SIZE)
    s = jnp.dot(q_home, own_ref[0], preferred_element_type=jnp.float32)
    for h in range(heads):
        slot = home * heads + h
        p = soften(s[h * rows:(h + 1) * rows], slot, causal)
        acc_scr[slot] += jnp.dot(p, own_ref[1], preferred_element_type=jnp.float32)

    stats = heads * HEAD_SIZE
    for b in range(blocks):
        out_ref[b, :, stats:] = jnp.zeros((rows, HEAD_SIZE), jnp.float32)
        for h in range(heads):
            slot = b * heads + h
            out_ref[b, :, h * HEAD_SIZE:(h + 1) * HEAD_SIZE] = acc_scr[slot]
            out_ref[b, :, stats + h:stats + h + 1] = m_scr[slot]
            out_ref[b, :, stats + heads + h:stats + heads + h + 1] = l_scr[slot]


def join_kernel(got_ref, out_ref, *, sources, heads):
    stats = heads * HEAD_SIZE
    for h in range(heads):
        ms = [got_ref[s, :, stats + h:stats + h + 1] for s in range(sources)]
        top = ms[0]
        for m in ms[1:]:
            top = jnp.maximum(top, m)
        top = jnp.where(top == -jnp.inf, 0.0, top)
        total = None
        acc = None
        for s in range(sources):
            fade = jnp.exp2(ms[s] - top)
            part_total = fade * got_ref[s, :, stats + heads + h:stats + heads + h + 1]
            part_acc = fade * got_ref[s, :, h * HEAD_SIZE:(h + 1) * HEAD_SIZE]
            total = part_total if total is None else total + part_total
            acc = part_acc if acc is None else acc + part_acc
        out_ref[:, h * HEAD_SIZE:(h + 1) * HEAD_SIZE] = acc / total


def join(a, b):
    acc_a, m_a, l_a = a
    acc_b, m_b, l_b = b
    m = jnp.maximum(m_a, m_b)
    m_safe = jnp.where(m == -jnp.inf, 0.0, m)
    f_a = jnp.exp2(m_a - m_safe)
    f_b = jnp.exp2(m_b - m_safe)
    acc = acc_a * f_a[..., None] + acc_b * f_b[..., None]
    return acc, m, l_a * f_a + l_b * f_b


def local(queries, query_key_value, cached_key_value, selected):
    rows = queries.shape[0]
    heads = queries.shape[1] // HEAD_SIZE
    head_group = QUERY_HEADS // KEY_VALUE_HEADS
    scale = 1.0 / math.sqrt(HEAD_SIZE)
    groups = lax.axis_size("blk")
    helpers = lax.axis_size("help")
    worker = lax.axis_index("blk")
    helper = lax.axis_index("help")
    piece = cached_key_value.shape[0]
    picks = selected.shape[1] * selected.shape[2]
    assert rows == QUERY_GROUP_ROWS and head_group % heads == 0 and selected.shape[0] == 1
    assert BLOCK_TOKENS % piece == 0 and piece % HEAD_SIZE == 0 and picks % HEAD_SIZE == 0 and picks // HEAD_SIZE <= rows
    per_group = piece * helpers // BLOCK_TOKENS
    query_blocks = helpers

    kv = cached_key_value.reshape(piece, 2, KEY_VALUE_HEADS, HEAD_SIZE)
    wanted = np.array([(t * heads) // head_group for t in range(groups)], np.int32)
    if not np.array_equal(wanted, np.arange(KEY_VALUE_HEADS)):
        kv = jnp.take(kv, wanted, axis=2)
    chunks = piece // HEAD_SIZE
    kv = kv.reshape(chunks, HEAD_SIZE, 2, groups, HEAD_SIZE)
    keys = jnp.transpose(kv[:, :, 0], (2, 0, 3, 1))
    values = jnp.transpose(kv[:, :, 1], (2, 0, 1, 3))
    held = lax.all_to_all(jnp.stack([keys, values], axis=1), "blk", 0, 0, tiled=True)

    q = jnp.transpose(queries.reshape(rows, heads, HEAD_SIZE), (1, 0, 2))
    sel_rows = selected.reshape(picks // HEAD_SIZE, HEAD_SIZE).astype(jnp.bfloat16)
    sel_rows = jnp.pad(sel_rows, ((0, rows - picks // HEAD_SIZE), (0, 0)))
    q = jnp.concatenate([q, sel_rows[None]], axis=0)
    q_all = lax.all_gather(q[None], "help", axis=0, tiled=True)
    sel_all = q_all[:, heads, :picks // HEAD_SIZE].astype(jnp.int32).reshape(
        query_blocks, selected.shape[1], selected.shape[2])

    kv_head = (worker * heads) // head_group
    own = query_key_value.reshape(rows, 2, KEY_VALUE_HEADS, HEAD_SIZE)
    own = lax.dynamic_index_in_dim(own, kv_head, axis=2, keepdims=False)
    own = jnp.stack([own[:, 0].T, own[:, 1]])

    my_heads = lax.dynamic_slice_in_dim(sel_all, worker * heads, heads, axis=1)
    piece_block = per_group * jnp.arange(groups, dtype=jnp.int32) + (helper * piece) // BLOCK_TOKENS
    hit = jnp.any(my_heads[:, :, None, :] == piece_block[None, None, :, None], axis=3)
    sel_flat = hit.astype(jnp.int32).reshape(-1)
    home = helper.reshape(1).astype(jnp.int32)

    slices = min(4, heads)
    part = heads // slices
    assert part * slices == heads and 2 * part <= HEAD_SIZE
    width = (part + 1) * HEAD_SIZE
    outs = []
    for c in range(slices):
        kernel = functools.partial(attend_kernel, groups=groups, heads=part, first=c * part,
                                   all_heads=heads, blocks=query_blocks, chunks=chunks,
                                   factor=scale * math.log2(math.e))
        slots = query_blocks * part
        partial = pl.pallas_call(
            kernel,
            grid_spec=pltpu.PrefetchScalarGridSpec(
                num_scalar_prefetch=2,
                grid=(1,),
                in_specs=[
                    pl.BlockSpec((query_blocks, part, rows, HEAD_SIZE),
                                 lambda i, s, h, c=c: (0, c, 0, 0)),
                    pl.BlockSpec((groups, 2, chunks, HEAD_SIZE, HEAD_SIZE),
                                 lambda i, s, h: (0, 0, 0, 0, 0)),
                    pl.BlockSpec((2, rows, HEAD_SIZE), lambda i, s, h: (0, 0, 0)),
                ],
                out_specs=pl.BlockSpec((query_blocks, rows, width), lambda i, s, h: (0, 0, 0)),
                scratch_shapes=[
                    pltpu.VMEM((slots * rows, piece), jnp.bfloat16),
                    pltpu.VMEM((slots, rows, 1), jnp.float32),
                    pltpu.VMEM((slots, rows, 1), jnp.float32),
                    pltpu.VMEM((slots, rows, HEAD_SIZE), jnp.float32),
                ],
            ),
            out_shape=jax.ShapeDtypeStruct((query_blocks, rows, width), jnp.float32),
            cost_estimate=pl.CostEstimate(
                flops=4 * query_blocks * part * rows * groups * piece * HEAD_SIZE,
                transcendentals=query_blocks * part * rows * groups * piece,
                bytes_accessed=2 * groups * 2 * piece * HEAD_SIZE + 4 * query_blocks * rows * width),
        )(sel_flat, home, q_all, held, own)
        got = lax.all_to_all(partial, "help", 0, 0, tiled=True)
        outs.append(pl.pallas_call(
            functools.partial(join_kernel, sources=helpers, heads=part),
            in_specs=[pl.BlockSpec(memory_space=pltpu.VMEM)],
            out_specs=pl.BlockSpec(memory_space=pltpu.VMEM),
            out_shape=jax.ShapeDtypeStruct((rows, part * HEAD_SIZE), jnp.float32),
        )(got))
    return jnp.concatenate(outs, axis=1)


def solution(mesh):
    in_specs = (P("help", "blk"), P("help", None), P(("blk", "help"), None), P("help", None, None))
    out_specs = P("help", "blk")
    return jax.shard_map(local, mesh=mesh, in_specs=in_specs, out_specs=out_specs, check_vma=False)
```

```python
import functools
import math

import jax
import jax.numpy as jnp
import numpy as np
from jax import lax
from jax.experimental import pallas as pl
from jax.experimental.pallas import tpu as pltpu
from jax.sharding import PartitionSpec as P

HEAD_SIZE = 128
QUERY_HEADS = 64
KEY_VALUE_HEADS = 8
BLOCK_TOKENS = 1024
QUERY_GROUP_ROWS = 128


def attend_kernel(sel_ref, home_ref, q_ref, kv_ref, own_ref, out_ref,
                  s_buf, own_buf, p_buf, mpart, lpart, m_scr, acc_scr,
                  *, groups, heads, first, all_heads, blocks, chunks, factor):
    rows = QUERY_GROUP_ROWS
    slots = blocks * heads
    lanes = HEAD_SIZE
    q = q_ref[...].reshape(slots * rows, HEAD_SIZE)
    home = home_ref[0]
    mpart[...] = jnp.full(mpart.shape, -jnp.inf, jnp.float32)
    lpart[...] = jnp.zeros(lpart.shape, jnp.float32)
    acc_scr[...] = jnp.zeros(acc_scr.shape, jnp.float32)

    def on(slot, g):
        b, h = divmod(slot, heads)
        return sel_ref[(b * all_heads + first + h) * groups + g] != 0

    def fold(x, op):
        out = x[:, :lanes]
        for c in range(1, x.shape[1] // lanes):
            out = op(out, x[:, c * lanes:(c + 1) * lanes])
        return out

    def score(g, carry):
        if chunks == 1:
            s = jnp.dot(q, kv_ref[g, 0, 0], preferred_element_type=jnp.float32)
        else:
            s = jnp.concatenate(
                [jnp.dot(q, kv_ref[g, 0, c], preferred_element_type=jnp.float32)
                 for c in range(chunks)], axis=1)
        s_buf[g] = s
        for slot in range(slots):
            @pl.when(on(slot, g))
            def _():
                mpart[slot] = jnp.maximum(mpart[slot], fold(s[slot * rows:(slot + 1) * rows],
                                                            jnp.maximum))
        return carry

    lax.fori_loop(0, groups, score, 0)

    causal = lax.broadcasted_iota(jnp.int32, (rows, rows), 0) >= lax.broadcasted_iota(
        jnp.int32, (rows, rows), 1)
    s_own = jnp.dot(q_ref[home].reshape(heads * rows, HEAD_SIZE), own_ref[0],
                    preferred_element_type=jnp.float32)
    for h in range(heads):
        s_h = jnp.where(causal, s_own[h * rows:(h + 1) * rows], -jnp.inf)
        own_buf[h] = s_h
        slot = home * heads + h
        mpart[slot] = jnp.maximum(mpart[slot], fold(s_h, jnp.maximum))

    for slot in range(slots):
        m = jnp.max(mpart[slot], axis=1, keepdims=True) * factor
        m_scr[slot] = m
        mpart[slot] = jnp.broadcast_to(jnp.where(m == -jnp.inf, 0.0, m), (rows, lanes))

    def mix(g, carry):
        width = s_buf.shape[2]
        ons = [on(slot, g) for slot in range(slots)]
        for slot in range(slots):
            @pl.when(ons[slot])
            def _():
                p = jnp.exp2(s_buf[g, slot * rows:(slot + 1) * rows] * factor - mpart[slot][:, :1])
                lpart[slot] += fold(p, jnp.add)
                p_buf[slot * rows:(slot + 1) * rows] = p.astype(jnp.bfloat16)

            @pl.when(jnp.logical_not(ons[slot]))
            def _():
                p_buf[slot * rows:(slot + 1) * rows] = jnp.zeros((rows, width), jnp.bfloat16)

        value = kv_ref[g, 1].reshape(chunks * HEAD_SIZE, HEAD_SIZE)
        pv = jnp.dot(p_buf[...], value, preferred_element_type=jnp.float32)
        for slot in range(slots):
            @pl.when(ons[slot])
            def _():
                acc_scr[slot] += pv[slot * rows:(slot + 1) * rows]
        return carry

    lax.fori_loop(0, groups, mix, 0)

    for h in range(heads):
        slot = home * heads + h
        p = jnp.exp2(own_buf[h] * factor - mpart[slot][:, :1])
        lpart[slot] += p
        acc_scr[slot] += jnp.dot(p.astype(jnp.bfloat16), own_ref[1],
                                 preferred_element_type=jnp.float32)

    stats = heads * HEAD_SIZE
    for b in range(blocks):
        out_ref[b, :, stats:] = jnp.zeros((rows, HEAD_SIZE), jnp.float32)
        for h in range(heads):
            slot = b * heads + h
            out_ref[b, :, h * HEAD_SIZE:(h + 1) * HEAD_SIZE] = acc_scr[slot]
            out_ref[b, :, stats + h:stats + h + 1] = m_scr[slot]
            out_ref[b, :, stats + heads + h:stats + heads + h + 1] = jnp.sum(
                lpart[slot], axis=1, keepdims=True)


def join_kernel(got_ref, out_ref, *, sources, heads):
    stats = heads * HEAD_SIZE
    for h in range(heads):
        ms = [got_ref[s, :, stats + h:stats + h + 1] for s in range(sources)]
        top = ms[0]
        for m in ms[1:]:
            top = jnp.maximum(top, m)
        top = jnp.where(top == -jnp.inf, 0.0, top)
        total = None
        acc = None
        for s in range(sources):
            fade = jnp.exp2(ms[s] - top)
            part_total = fade * got_ref[s, :, stats + heads + h:stats + heads + h + 1]
            part_acc = fade * got_ref[s, :, h * HEAD_SIZE:(h + 1) * HEAD_SIZE]
            total = part_total if total is None else total + part_total
            acc = part_acc if acc is None else acc + part_acc
        out_ref[:, h * HEAD_SIZE:(h + 1) * HEAD_SIZE] = acc / total


def join(a, b):
    acc_a, m_a, l_a = a
    acc_b, m_b, l_b = b
    m = jnp.maximum(m_a, m_b)
    m_safe = jnp.where(m == -jnp.inf, 0.0, m)
    f_a = jnp.exp2(m_a - m_safe)
    f_b = jnp.exp2(m_b - m_safe)
    acc = acc_a * f_a[..., None] + acc_b * f_b[..., None]
    return acc, m, l_a * f_a + l_b * f_b


def local(queries, query_key_value, cached_key_value, selected):
    rows = queries.shape[0]
    heads = queries.shape[1] // HEAD_SIZE
    head_group = QUERY_HEADS // KEY_VALUE_HEADS
    scale = 1.0 / math.sqrt(HEAD_SIZE)
    groups = lax.axis_size("blk")
    helpers = lax.axis_size("help")
    worker = lax.axis_index("blk")
    helper = lax.axis_index("help")
    piece = cached_key_value.shape[0]
    picks = selected.shape[1] * selected.shape[2]
    assert rows == QUERY_GROUP_ROWS and head_group % heads == 0 and selected.shape[0] == 1
    assert BLOCK_TOKENS % piece == 0 and piece % HEAD_SIZE == 0 and picks % HEAD_SIZE == 0 and picks // HEAD_SIZE <= rows
    per_group = piece * helpers // BLOCK_TOKENS
    query_blocks = helpers

    kv = cached_key_value.reshape(piece, 2, KEY_VALUE_HEADS, HEAD_SIZE)
    wanted = np.array([(t * heads) // head_group for t in range(groups)], np.int32)
    if not np.array_equal(wanted, np.arange(KEY_VALUE_HEADS)):
        kv = jnp.take(kv, wanted, axis=2)
    chunks = piece // HEAD_SIZE
    kv = kv.reshape(chunks, HEAD_SIZE, 2, groups, HEAD_SIZE)
    keys = jnp.transpose(kv[:, :, 0], (2, 0, 3, 1))
    values = jnp.transpose(kv[:, :, 1], (2, 0, 1, 3))
    held = lax.all_to_all(jnp.stack([keys, values], axis=1), "blk", 0, 0, tiled=True)

    q = jnp.transpose(queries.reshape(rows, heads, HEAD_SIZE), (1, 0, 2))
    sel_rows = selected.reshape(picks // HEAD_SIZE, HEAD_SIZE).astype(jnp.bfloat16)
    sel_rows = jnp.pad(sel_rows, ((0, rows - picks // HEAD_SIZE), (0, 0)))
    q = jnp.concatenate([q, sel_rows[None]], axis=0)
    q_all = lax.all_gather(q[None], "help", axis=0, tiled=True)
    sel_all = q_all[:, heads, :picks // HEAD_SIZE].astype(jnp.int32).reshape(
        query_blocks, selected.shape[1], selected.shape[2])

    kv_head = (worker * heads) // head_group
    own = query_key_value.reshape(rows, 2, KEY_VALUE_HEADS, HEAD_SIZE)
    own = lax.dynamic_index_in_dim(own, kv_head, axis=2, keepdims=False)
    own = jnp.stack([own[:, 0].T, own[:, 1]])

    my_heads = lax.dynamic_slice_in_dim(sel_all, worker * heads, heads, axis=1)
    piece_block = per_group * jnp.arange(groups, dtype=jnp.int32) + (helper * piece) // BLOCK_TOKENS
    hit = jnp.any(my_heads[:, :, None, :] == piece_block[None, None, :, None], axis=3)
    sel_flat = hit.astype(jnp.int32).reshape(-1)
    home = helper.reshape(1).astype(jnp.int32)

    slices = min(4, heads)
    part = heads // slices
    assert part * slices == heads and 2 * part <= HEAD_SIZE
    width = (part + 1) * HEAD_SIZE
    outs = []
    for c in range(slices):
        kernel = functools.partial(attend_kernel, groups=groups, heads=part, first=c * part,
                                   all_heads=heads, blocks=query_blocks, chunks=chunks,
                                   factor=scale * math.log2(math.e))
        slots = query_blocks * part
        partial = pl.pallas_call(
            kernel,
            grid_spec=pltpu.PrefetchScalarGridSpec(
                num_scalar_prefetch=2,
                grid=(1,),
                in_specs=[
                    pl.BlockSpec((query_blocks, part, rows, HEAD_SIZE),
                                 lambda i, s, h, c=c: (0, c, 0, 0)),
                    pl.BlockSpec((groups, 2, chunks, HEAD_SIZE, HEAD_SIZE),
                                 lambda i, s, h: (0, 0, 0, 0, 0)),
                    pl.BlockSpec((2, rows, HEAD_SIZE), lambda i, s, h: (0, 0, 0)),
                ],
                out_specs=pl.BlockSpec((query_blocks, rows, width), lambda i, s, h: (0, 0, 0)),
                scratch_shapes=[
                    pltpu.VMEM((groups, slots * rows, piece), jnp.float32),
                    pltpu.VMEM((part, rows, rows), jnp.float32),
                    pltpu.VMEM((slots * rows, piece), jnp.bfloat16),
                    pltpu.VMEM((slots, rows, HEAD_SIZE), jnp.float32),
                    pltpu.VMEM((slots, rows, HEAD_SIZE), jnp.float32),
                    pltpu.VMEM((slots, rows, 1), jnp.float32),
                    pltpu.VMEM((slots, rows, HEAD_SIZE), jnp.float32),
                ],
            ),
            compiler_params=pltpu.CompilerParams(vmem_limit_bytes=48 * 1024 * 1024),
            out_shape=jax.ShapeDtypeStruct((query_blocks, rows, width), jnp.float32),
            cost_estimate=pl.CostEstimate(
                flops=4 * query_blocks * part * rows * groups * piece * HEAD_SIZE,
                transcendentals=query_blocks * part * rows * groups * piece,
                bytes_accessed=2 * groups * 2 * piece * HEAD_SIZE + 4 * query_blocks * rows * width),
        )(sel_flat, home, q_all, held, own)
        got = lax.all_to_all(partial, "help", 0, 0, tiled=True)
        outs.append(pl.pallas_call(
            functools.partial(join_kernel, sources=helpers, heads=part),
            in_specs=[pl.BlockSpec(memory_space=pltpu.VMEM)],
            out_specs=pl.BlockSpec(memory_space=pltpu.VMEM),
            out_shape=jax.ShapeDtypeStruct((rows, part * HEAD_SIZE), jnp.float32),
        )(got))
    return jnp.concatenate(outs, axis=1)


def solution(mesh):
    in_specs = (P("help", "blk"), P("help", None), P(("blk", "help"), None), P("help", None, None))
    out_specs = P("help", "blk")
    return jax.shard_map(local, mesh=mesh, in_specs=in_specs, out_specs=out_specs, check_vma=False)
```

```python
import functools
import math

import jax
import jax.numpy as jnp
import numpy as np
from jax import lax
from jax.experimental import pallas as pl
from jax.experimental.pallas import tpu as pltpu
from jax.sharding import PartitionSpec as P

HEAD_SIZE = 128
QUERY_HEADS = 64
KEY_VALUE_HEADS = 8
BLOCK_TOKENS = 1024
QUERY_GROUP_ROWS = 128
STAT_ROWS = 8


def attend_kernel(sel_ref, home_ref, q_ref, kv_ref, own_ref, out_ref,
                  s_buf, own_buf, p_buf, mpart, lpart, m_scr, acc_scr, st_scr,
                  *, groups, heads, first, all_heads, blocks, chunks, factor):
    rows = QUERY_GROUP_ROWS
    slots = blocks * heads
    lanes = HEAD_SIZE
    q = q_ref[...].reshape(slots * rows, HEAD_SIZE)
    home = home_ref[0]
    mpart[...] = jnp.full(mpart.shape, -jnp.inf, jnp.float32)
    lpart[...] = jnp.zeros(lpart.shape, jnp.float32)
    acc_scr[...] = jnp.zeros(acc_scr.shape, jnp.float32)

    def on(slot, g):
        b, h = divmod(slot, heads)
        return sel_ref[(b * all_heads + first + h) * groups + g] != 0

    def fold(x, op):
        out = x[:, :lanes]
        for c in range(1, x.shape[1] // lanes):
            out = op(out, x[:, c * lanes:(c + 1) * lanes])
        return out

    def score(g, carry):
        if chunks == 1:
            s = jnp.dot(q, kv_ref[g, 0, 0], preferred_element_type=jnp.float32)
        else:
            s = jnp.concatenate(
                [jnp.dot(q, kv_ref[g, 0, c], preferred_element_type=jnp.float32)
                 for c in range(chunks)], axis=1)
        s_buf[g] = s
        for slot in range(slots):
            @pl.when(on(slot, g))
            def _():
                mpart[slot] = jnp.maximum(mpart[slot], fold(s[slot * rows:(slot + 1) * rows],
                                                            jnp.maximum))
        return carry

    lax.fori_loop(0, groups, score, 0)

    causal = lax.broadcasted_iota(jnp.int32, (rows, rows), 0) >= lax.broadcasted_iota(
        jnp.int32, (rows, rows), 1)
    s_own = jnp.dot(q_ref[home].reshape(heads * rows, HEAD_SIZE), own_ref[0],
                    preferred_element_type=jnp.float32)
    for h in range(heads):
        s_h = jnp.where(causal, s_own[h * rows:(h + 1) * rows], -jnp.inf)
        own_buf[h] = s_h
        slot = home * heads + h
        mpart[slot] = jnp.maximum(mpart[slot], fold(s_h, jnp.maximum))

    for slot in range(slots):
        m = jnp.max(mpart[slot], axis=1, keepdims=True) * factor
        m_scr[slot] = m
        mpart[slot] = jnp.broadcast_to(jnp.where(m == -jnp.inf, 0.0, m), (rows, lanes))

    def mix(g, carry):
        width = s_buf.shape[2]
        ons = [on(slot, g) for slot in range(slots)]
        for slot in range(slots):
            @pl.when(ons[slot])
            def _():
                p = jnp.exp2(s_buf[g, slot * rows:(slot + 1) * rows] * factor - mpart[slot][:, :1])
                lpart[slot] += fold(p, jnp.add)
                p_buf[slot * rows:(slot + 1) * rows] = p.astype(jnp.bfloat16)

            @pl.when(jnp.logical_not(ons[slot]))
            def _():
                p_buf[slot * rows:(slot + 1) * rows] = jnp.zeros((rows, width), jnp.bfloat16)

        value = kv_ref[g, 1].reshape(chunks * HEAD_SIZE, HEAD_SIZE)
        pv = jnp.dot(p_buf[...], value, preferred_element_type=jnp.float32)
        for slot in range(slots):
            @pl.when(ons[slot])
            def _():
                acc_scr[slot] += pv[slot * rows:(slot + 1) * rows]
        return carry

    lax.fori_loop(0, groups, mix, 0)

    for h in range(heads):
        slot = home * heads + h
        p = jnp.exp2(own_buf[h] * factor - mpart[slot][:, :1])
        lpart[slot] += p
        acc_scr[slot] += jnp.dot(p.astype(jnp.bfloat16), own_ref[1],
                                 preferred_element_type=jnp.float32)

    for b in range(blocks):
        st_scr[...] = jnp.zeros(st_scr.shape, jnp.float32)
        for h in range(heads):
            slot = b * heads + h
            out_ref[b, :rows, h * HEAD_SIZE:(h + 1) * HEAD_SIZE] = acc_scr[slot]
            st_scr[:, h:h + 1] = m_scr[slot]
            st_scr[:, heads + h:heads + h + 1] = jnp.sum(lpart[slot], axis=1, keepdims=True)
        out_ref[b, rows:, :HEAD_SIZE] = st_scr[...].T[:STAT_ROWS]
        if heads > 1:
            out_ref[b, rows:, HEAD_SIZE:] = jnp.zeros((STAT_ROWS, (heads - 1) * HEAD_SIZE), jnp.float32)


def join_kernel(got_ref, prev_ref, out_ref, *, sources, heads):
    rows = QUERY_GROUP_ROWS
    del prev_ref
    cols = [got_ref[s, rows:, :HEAD_SIZE].T for s in range(sources)]
    for h in range(heads):
        ms = [c[:, h:h + 1] for c in cols]
        top = ms[0]
        for m in ms[1:]:
            top = jnp.maximum(top, m)
        top = jnp.where(top == -jnp.inf, 0.0, top)
        total = None
        acc = None
        for s in range(sources):
            fade = jnp.exp2(ms[s] - top)
            part_total = fade * cols[s][:, heads + h:heads + h + 1]
            part_acc = fade * got_ref[s, :rows, h * HEAD_SIZE:(h + 1) * HEAD_SIZE]
            total = part_total if total is None else total + part_total
            acc = part_acc if acc is None else acc + part_acc
        out_ref[:, h * HEAD_SIZE:(h + 1) * HEAD_SIZE] = acc / total


def join(a, b):
    acc_a, m_a, l_a = a
    acc_b, m_b, l_b = b
    m = jnp.maximum(m_a, m_b)
    m_safe = jnp.where(m == -jnp.inf, 0.0, m)
    f_a = jnp.exp2(m_a - m_safe)
    f_b = jnp.exp2(m_b - m_safe)
    acc = acc_a * f_a[..., None] + acc_b * f_b[..., None]
    return acc, m, l_a * f_a + l_b * f_b


def local(queries, query_key_value, cached_key_value, selected):
    rows = queries.shape[0]
    heads = queries.shape[1] // HEAD_SIZE
    head_group = QUERY_HEADS // KEY_VALUE_HEADS
    scale = 1.0 / math.sqrt(HEAD_SIZE)
    groups = lax.axis_size("blk")
    helpers = lax.axis_size("help")
    worker = lax.axis_index("blk")
    helper = lax.axis_index("help")
    piece = cached_key_value.shape[0]
    picks = selected.shape[1] * selected.shape[2]
    assert rows == QUERY_GROUP_ROWS and head_group % heads == 0 and selected.shape[0] == 1
    assert BLOCK_TOKENS % piece == 0 and piece % HEAD_SIZE == 0 and picks % HEAD_SIZE == 0 and picks // HEAD_SIZE <= rows
    per_group = piece * helpers // BLOCK_TOKENS
    query_blocks = helpers

    kv = cached_key_value.reshape(piece, 2, KEY_VALUE_HEADS, HEAD_SIZE)
    wanted = np.array([(t * heads) // head_group for t in range(groups)], np.int32)
    if not np.array_equal(wanted, np.arange(KEY_VALUE_HEADS)):
        kv = jnp.take(kv, wanted, axis=2)
    chunks = piece // HEAD_SIZE
    kv = kv.reshape(chunks, HEAD_SIZE, 2, groups, HEAD_SIZE)
    keys = jnp.transpose(kv[:, :, 0], (2, 0, 3, 1))
    values = jnp.transpose(kv[:, :, 1], (2, 0, 1, 3))
    held = lax.all_to_all(jnp.stack([keys, values], axis=1), "blk", 0, 0, tiled=True)

    q = jnp.transpose(queries.reshape(rows, heads, HEAD_SIZE), (1, 0, 2))
    sel_rows = selected.reshape(picks // HEAD_SIZE, HEAD_SIZE).astype(jnp.bfloat16)
    sel_rows = jnp.pad(sel_rows, ((0, rows - picks // HEAD_SIZE), (0, 0)))
    q = jnp.concatenate([q, sel_rows[None]], axis=0)
    q_all = lax.all_gather(q[None], "help", axis=0, tiled=True)
    sel_all = q_all[:, heads, :picks // HEAD_SIZE].astype(jnp.int32).reshape(
        query_blocks, selected.shape[1], selected.shape[2])

    kv_head = (worker * heads) // head_group
    own = query_key_value.reshape(rows, 2, KEY_VALUE_HEADS, HEAD_SIZE)
    own = lax.dynamic_index_in_dim(own, kv_head, axis=2, keepdims=False)
    own = jnp.stack([own[:, 0].T, own[:, 1]])

    my_heads = lax.dynamic_slice_in_dim(sel_all, worker * heads, heads, axis=1)
    piece_block = per_group * jnp.arange(groups, dtype=jnp.int32) + (helper * piece) // BLOCK_TOKENS
    hit = jnp.any(my_heads[:, :, None, :] == piece_block[None, None, :, None], axis=3)
    sel_flat = hit.astype(jnp.int32).reshape(-1)
    home = helper.reshape(1).astype(jnp.int32)

    slices = min(4, heads)
    part = heads // slices
    assert part * slices == heads and 2 * part <= STAT_ROWS
    width = part * HEAD_SIZE
    result = jnp.zeros((rows, heads * HEAD_SIZE), jnp.float32)
    for c in range(slices):
        kernel = functools.partial(attend_kernel, groups=groups, heads=part, first=c * part,
                                   all_heads=heads, blocks=query_blocks, chunks=chunks,
                                   factor=scale * math.log2(math.e))
        slots = query_blocks * part
        partial = pl.pallas_call(
            kernel,
            grid_spec=pltpu.PrefetchScalarGridSpec(
                num_scalar_prefetch=2,
                grid=(1,),
                in_specs=[
                    pl.BlockSpec((query_blocks, part, rows, HEAD_SIZE),
                                 lambda i, s, h, c=c: (0, c, 0, 0)),
                    pl.BlockSpec((groups, 2, chunks, HEAD_SIZE, HEAD_SIZE),
                                 lambda i, s, h: (0, 0, 0, 0, 0)),
                    pl.BlockSpec((2, rows, HEAD_SIZE), lambda i, s, h: (0, 0, 0)),
                ],
                out_specs=pl.BlockSpec((query_blocks, rows + STAT_ROWS, width),
                                       lambda i, s, h: (0, 0, 0)),
                scratch_shapes=[
                    pltpu.VMEM((groups, slots * rows, piece), jnp.float32),
                    pltpu.VMEM((part, rows, rows), jnp.float32),
                    pltpu.VMEM((slots * rows, piece), jnp.bfloat16),
                    pltpu.VMEM((slots, rows, HEAD_SIZE), jnp.float32),
                    pltpu.VMEM((slots, rows, HEAD_SIZE), jnp.float32),
                    pltpu.VMEM((slots, rows, 1), jnp.float32),
                    pltpu.VMEM((slots, rows, HEAD_SIZE), jnp.float32),
                    pltpu.VMEM((rows, HEAD_SIZE), jnp.float32),
                ],
            ),
            compiler_params=pltpu.CompilerParams(vmem_limit_bytes=48 * 1024 * 1024),
            out_shape=jax.ShapeDtypeStruct((query_blocks, rows + STAT_ROWS, width), jnp.float32),
            cost_estimate=pl.CostEstimate(
                flops=4 * query_blocks * part * rows * groups * piece * HEAD_SIZE,
                transcendentals=query_blocks * part * rows * groups * piece,
                bytes_accessed=2 * groups * 2 * piece * HEAD_SIZE + 4 * query_blocks * rows * width),
        )(sel_flat, home, q_all, held, own)
        got = lax.all_to_all(partial, "help", 0, 0, tiled=True)
        result = pl.pallas_call(
            functools.partial(join_kernel, sources=helpers, heads=part),
            grid=(1,),
            in_specs=[pl.BlockSpec((helpers, rows + STAT_ROWS, width), lambda i: (0, 0, 0)),
                      pl.BlockSpec(memory_space=pl.ANY)],
            out_specs=pl.BlockSpec((rows, width), lambda i, c=c: (0, c)),
            out_shape=jax.ShapeDtypeStruct((rows, heads * HEAD_SIZE), jnp.float32),
            input_output_aliases={1: 0},
        )(got, result)
    return result


def solution(mesh):
    in_specs = (P("help", "blk"), P("help", None), P(("blk", "help"), None), P("help", None, None))
    out_specs = P("help", "blk")
    return jax.shard_map(local, mesh=mesh, in_specs=in_specs, out_specs=out_specs, check_vma=False)
```

```python
import functools
import math

import jax
import jax.numpy as jnp
import numpy as np
from jax import lax
from jax.experimental import pallas as pl
from jax.experimental.pallas import tpu as pltpu
from jax.sharding import PartitionSpec as P

HEAD_SIZE = 128
QUERY_HEADS = 64
KEY_VALUE_HEADS = 8
BLOCK_TOKENS = 1024
QUERY_GROUP_ROWS = 128
STAT_ROWS = 8


def attend_kernel(sel_ref, home_ref, q_ref, kv_ref, own_ref, out_ref,
                  s_buf, own_buf, p_buf, mpart, lpart, m_scr, acc_scr, st_scr,
                  *, groups, heads, first, all_heads, blocks, chunks, factor):
    rows = QUERY_GROUP_ROWS
    slots = blocks * heads
    lanes = HEAD_SIZE
    q = q_ref[...].reshape(slots * rows, HEAD_SIZE)
    home = home_ref[0]
    mpart[...] = jnp.full(mpart.shape, -jnp.inf, jnp.float32)
    lpart[...] = jnp.zeros(lpart.shape, jnp.float32)
    acc_scr[...] = jnp.zeros(acc_scr.shape, jnp.float32)

    def on(slot, g):
        b, h = divmod(slot, heads)
        return sel_ref[(b * all_heads + first + h) * groups + g] != 0

    def fold(x, op):
        out = x[:, :lanes]
        for c in range(1, x.shape[1] // lanes):
            out = op(out, x[:, c * lanes:(c + 1) * lanes])
        return out

    def score(g, carry):
        if chunks == 1:
            s = jnp.dot(q, kv_ref[g, 0, 0], preferred_element_type=jnp.float32)
        else:
            s = jnp.concatenate(
                [jnp.dot(q, kv_ref[g, 0, c], preferred_element_type=jnp.float32)
                 for c in range(chunks)], axis=1)
        s_buf[g] = s
        for slot in range(slots):
            @pl.when(on(slot, g))
            def _():
                mpart[slot] = jnp.maximum(mpart[slot], fold(s[slot * rows:(slot + 1) * rows],
                                                            jnp.maximum))
        return carry

    lax.fori_loop(0, groups, score, 0)

    causal = lax.broadcasted_iota(jnp.int32, (rows, rows), 0) >= lax.broadcasted_iota(
        jnp.int32, (rows, rows), 1)
    s_own = jnp.dot(q_ref[home], own_ref[0],
                    preferred_element_type=jnp.float32)
    for h in range(heads):
        s_h = jnp.where(causal, s_own[h * rows:(h + 1) * rows], -jnp.inf)
        own_buf[h] = s_h
        slot = home * heads + h
        mpart[slot] = jnp.maximum(mpart[slot], fold(s_h, jnp.maximum))

    for slot in range(slots):
        m = jnp.max(mpart[slot], axis=1, keepdims=True) * factor
        m_scr[slot] = m
        mpart[slot] = jnp.broadcast_to(jnp.where(m == -jnp.inf, 0.0, m), (rows, lanes))

    def mix(g, carry):
        width = s_buf.shape[2]
        ons = [on(slot, g) for slot in range(slots)]
        for slot in range(slots):
            @pl.when(ons[slot])
            def _():
                p = jnp.exp2(s_buf[g, slot * rows:(slot + 1) * rows] * factor - mpart[slot][:, :1])
                lpart[slot] += fold(p, jnp.add)
                p_buf[slot * rows:(slot + 1) * rows] = p.astype(jnp.bfloat16)

            @pl.when(jnp.logical_not(ons[slot]))
            def _():
                p_buf[slot * rows:(slot + 1) * rows] = jnp.zeros((rows, width), jnp.bfloat16)

        value = kv_ref[g, 1].reshape(chunks * HEAD_SIZE, HEAD_SIZE)
        pv = jnp.dot(p_buf[...], value, preferred_element_type=jnp.float32)
        for slot in range(slots):
            @pl.when(ons[slot])
            def _():
                acc_scr[slot] += pv[slot * rows:(slot + 1) * rows]
        return carry

    lax.fori_loop(0, groups, mix, 0)

    for h in range(heads):
        slot = home * heads + h
        p = jnp.exp2(own_buf[h] * factor - mpart[slot][:, :1])
        lpart[slot] += p
        acc_scr[slot] += jnp.dot(p.astype(jnp.bfloat16), own_ref[1],
                                 preferred_element_type=jnp.float32)

    for b in range(blocks):
        st_scr[...] = jnp.zeros(st_scr.shape, jnp.float32)
        for h in range(heads):
            slot = b * heads + h
            out_ref[b, :rows, h * HEAD_SIZE:(h + 1) * HEAD_SIZE] = acc_scr[slot]
            st_scr[:, h:h + 1] = m_scr[slot]
            st_scr[:, heads + h:heads + h + 1] = jnp.sum(lpart[slot], axis=1, keepdims=True)
        out_ref[b, rows:, :HEAD_SIZE] = st_scr[...].T[:STAT_ROWS]
        if heads > 1:
            out_ref[b, rows:, HEAD_SIZE:] = jnp.zeros((STAT_ROWS, (heads - 1) * HEAD_SIZE), jnp.float32)


def join_kernel(got_ref, *refs, sources, heads):
    rows = QUERY_GROUP_ROWS
    out_ref = refs[-1]
    cols = [got_ref[s, rows:, :HEAD_SIZE].T for s in range(sources)]
    for h in range(heads):
        ms = [c[:, h:h + 1] for c in cols]
        top = ms[0]
        for m in ms[1:]:
            top = jnp.maximum(top, m)
        top = jnp.where(top == -jnp.inf, 0.0, top)
        total = None
        acc = None
        for s in range(sources):
            fade = jnp.exp2(ms[s] - top)
            part_total = fade * cols[s][:, heads + h:heads + h + 1]
            part_acc = fade * got_ref[s, :rows, h * HEAD_SIZE:(h + 1) * HEAD_SIZE]
            total = part_total if total is None else total + part_total
            acc = part_acc if acc is None else acc + part_acc
        out_ref[:, h * HEAD_SIZE:(h + 1) * HEAD_SIZE] = acc / total


def join(a, b):
    acc_a, m_a, l_a = a
    acc_b, m_b, l_b = b
    m = jnp.maximum(m_a, m_b)
    m_safe = jnp.where(m == -jnp.inf, 0.0, m)
    f_a = jnp.exp2(m_a - m_safe)
    f_b = jnp.exp2(m_b - m_safe)
    acc = acc_a * f_a[..., None] + acc_b * f_b[..., None]
    return acc, m, l_a * f_a + l_b * f_b


def local(queries, query_key_value, cached_key_value, selected):
    rows = queries.shape[0]
    heads = queries.shape[1] // HEAD_SIZE
    head_group = QUERY_HEADS // KEY_VALUE_HEADS
    scale = 1.0 / math.sqrt(HEAD_SIZE)
    groups = lax.axis_size("blk")
    helpers = lax.axis_size("help")
    worker = lax.axis_index("blk")
    helper = lax.axis_index("help")
    piece = cached_key_value.shape[0]
    picks = selected.shape[1] * selected.shape[2]
    assert rows == QUERY_GROUP_ROWS and head_group % heads == 0 and selected.shape[0] == 1
    assert BLOCK_TOKENS % piece == 0 and piece % HEAD_SIZE == 0 and picks % HEAD_SIZE == 0
    per_group = piece * helpers // BLOCK_TOKENS
    query_blocks = helpers

    kv = cached_key_value.reshape(piece, 2, KEY_VALUE_HEADS, HEAD_SIZE)
    wanted = np.array([(t * heads) // head_group for t in range(groups)], np.int32)
    if not np.array_equal(wanted, np.arange(KEY_VALUE_HEADS)):
        kv = jnp.take(kv, wanted, axis=2)
    chunks = piece // HEAD_SIZE
    kv = kv.reshape(chunks, HEAD_SIZE, 2, groups, HEAD_SIZE)
    keys = jnp.transpose(kv[:, :, 0], (2, 0, 3, 1))
    values = jnp.transpose(kv[:, :, 1], (2, 0, 1, 3))
    held = lax.all_to_all(jnp.stack([keys, values], axis=1), "blk", 0, 0, tiled=True)

    q = jnp.transpose(queries.reshape(rows, heads, HEAD_SIZE), (1, 0, 2)).reshape(heads * rows, HEAD_SIZE)
    sel_rows = selected.reshape(picks // HEAD_SIZE, HEAD_SIZE).astype(jnp.bfloat16)
    sel_pad = -(-(picks // HEAD_SIZE) // 16) * 16
    sel_rows = jnp.pad(sel_rows, ((0, sel_pad - picks // HEAD_SIZE), (0, 0)))
    q = jnp.concatenate([q, sel_rows], axis=0)
    q_all = lax.all_gather(q[None], "help", axis=0, tiled=True)
    sel_all = q_all[:, heads * rows:heads * rows + picks // HEAD_SIZE].astype(jnp.int32).reshape(
        query_blocks, selected.shape[1], selected.shape[2])

    kv_head = (worker * heads) // head_group
    own = query_key_value.reshape(rows, 2, KEY_VALUE_HEADS, HEAD_SIZE)
    own = lax.dynamic_index_in_dim(own, kv_head, axis=2, keepdims=False)
    own = jnp.stack([own[:, 0].T, own[:, 1]])

    my_heads = lax.dynamic_slice_in_dim(sel_all, worker * heads, heads, axis=1)
    piece_block = per_group * jnp.arange(groups, dtype=jnp.int32) + (helper * piece) // BLOCK_TOKENS
    hit = jnp.any(my_heads[:, :, None, :] == piece_block[None, None, :, None], axis=3)
    sel_flat = hit.astype(jnp.int32).reshape(-1)
    home = helper.reshape(1).astype(jnp.int32)

    slices = min(4, heads)
    part = heads // slices
    assert part * slices == heads and 2 * part <= STAT_ROWS
    width = part * HEAD_SIZE
    result = None
    for c in range(slices):
        kernel = functools.partial(attend_kernel, groups=groups, heads=part, first=c * part,
                                   all_heads=heads, blocks=query_blocks, chunks=chunks,
                                   factor=scale * math.log2(math.e))
        slots = query_blocks * part
        partial = pl.pallas_call(
            kernel,
            grid_spec=pltpu.PrefetchScalarGridSpec(
                num_scalar_prefetch=2,
                grid=(1,),
                in_specs=[
                    pl.BlockSpec((query_blocks, part * rows, HEAD_SIZE),
                                 lambda i, s, h, c=c: (0, c, 0)),
                    pl.BlockSpec((groups, 2, chunks, HEAD_SIZE, HEAD_SIZE),
                                 lambda i, s, h: (0, 0, 0, 0, 0)),
                    pl.BlockSpec((2, rows, HEAD_SIZE), lambda i, s, h: (0, 0, 0)),
                ],
                out_specs=pl.BlockSpec((query_blocks, rows + STAT_ROWS, width),
                                       lambda i, s, h: (0, 0, 0)),
                scratch_shapes=[
                    pltpu.VMEM((groups, slots * rows, piece), jnp.float32),
                    pltpu.VMEM((part, rows, rows), jnp.float32),
                    pltpu.VMEM((slots * rows, piece), jnp.bfloat16),
                    pltpu.VMEM((slots, rows, HEAD_SIZE), jnp.float32),
                    pltpu.VMEM((slots, rows, HEAD_SIZE), jnp.float32),
                    pltpu.VMEM((slots, rows, 1), jnp.float32),
                    pltpu.VMEM((slots, rows, HEAD_SIZE), jnp.float32),
                    pltpu.VMEM((rows, HEAD_SIZE), jnp.float32),
                ],
            ),
            compiler_params=pltpu.CompilerParams(vmem_limit_bytes=48 * 1024 * 1024),
            out_shape=jax.ShapeDtypeStruct((query_blocks, rows + STAT_ROWS, width), jnp.float32),
            cost_estimate=pl.CostEstimate(
                flops=4 * query_blocks * part * rows * groups * piece * HEAD_SIZE,
                transcendentals=query_blocks * part * rows * groups * piece,
                bytes_accessed=2 * groups * 2 * piece * HEAD_SIZE + 4 * query_blocks * rows * width),
        )(sel_flat, home, q_all, held, own)
        got = lax.all_to_all(partial, "help", 0, 0, tiled=True)
        first_join = c == 0
        result = pl.pallas_call(
            functools.partial(join_kernel, sources=helpers, heads=part),
            grid=(1,),
            in_specs=[pl.BlockSpec((helpers, rows + STAT_ROWS, width), lambda i: (0, 0, 0))]
            + ([] if first_join else [pl.BlockSpec(memory_space=pl.ANY)]),
            out_specs=pl.BlockSpec((rows, width), lambda i, c=c: (0, c)),
            out_shape=jax.ShapeDtypeStruct((rows, heads * HEAD_SIZE), jnp.float32),
            input_output_aliases={} if first_join else {1: 0},
        )(*((got,) if first_join else (got, result)))
    return result


def solution(mesh):
    in_specs = (P("help", "blk"), P("help", None), P(("blk", "help"), None), P("help", None, None))
    out_specs = P("help", "blk")
    return jax.shard_map(local, mesh=mesh, in_specs=in_specs, out_specs=out_specs, check_vma=False)
```

```python
import functools
import math

import jax
import jax.numpy as jnp
import numpy as np
from jax import lax
from jax.experimental import pallas as pl
from jax.experimental.pallas import tpu as pltpu
from jax.sharding import PartitionSpec as P

HEAD_SIZE = 128
QUERY_HEADS = 64
KEY_VALUE_HEADS = 8
BLOCK_TOKENS = 1024
QUERY_GROUP_ROWS = 128
STAT_ROWS = 8


def relayout_kernel(x_ref, out_ref, *, wanted, chunks):
    for t, kv_head in enumerate(wanted):
        for c in range(chunks):
            tokens = slice(c * HEAD_SIZE, (c + 1) * HEAD_SIZE)
            keys = x_ref[tokens, kv_head * HEAD_SIZE:(kv_head + 1) * HEAD_SIZE]
            out_ref[t, 0, c] = keys.astype(jnp.float32).T.astype(jnp.bfloat16)
            column = (KEY_VALUE_HEADS + kv_head) * HEAD_SIZE
            out_ref[t, 1, c] = x_ref[tokens, column:column + HEAD_SIZE]


def attend_kernel(sel_ref, home_ref, q_ref, kv_ref, own_ref, out_ref,
                  s_buf, own_buf, p_buf, mpart, lpart, m_scr, acc_scr, st_scr,
                  *, groups, heads, first, all_heads, blocks, chunks, factor):
    rows = QUERY_GROUP_ROWS
    slots = blocks * heads
    lanes = HEAD_SIZE
    q = q_ref[...].reshape(slots * rows, HEAD_SIZE)
    home = home_ref[0]
    mpart[...] = jnp.full(mpart.shape, -jnp.inf, jnp.float32)
    lpart[...] = jnp.zeros(lpart.shape, jnp.float32)
    acc_scr[...] = jnp.zeros(acc_scr.shape, jnp.float32)

    def on(slot, g):
        b, h = divmod(slot, heads)
        return sel_ref[(b * all_heads + first + h) * groups + g] != 0

    def fold(x, op):
        out = x[:, :lanes]
        for c in range(1, x.shape[1] // lanes):
            out = op(out, x[:, c * lanes:(c + 1) * lanes])
        return out

    def score(g, carry):
        if chunks == 1:
            s = jnp.dot(q, kv_ref[g, 0, 0], preferred_element_type=jnp.float32)
        else:
            s = jnp.concatenate(
                [jnp.dot(q, kv_ref[g, 0, c], preferred_element_type=jnp.float32)
                 for c in range(chunks)], axis=1)
        s_buf[g] = s
        for slot in range(slots):
            @pl.when(on(slot, g))
            def _():
                mpart[slot] = jnp.maximum(mpart[slot], fold(s[slot * rows:(slot + 1) * rows],
                                                            jnp.maximum))
        return carry

    lax.fori_loop(0, groups, score, 0)

    causal = lax.broadcasted_iota(jnp.int32, (rows, rows), 0) >= lax.broadcasted_iota(
        jnp.int32, (rows, rows), 1)
    s_own = jnp.dot(q_ref[home], own_ref[0],
                    preferred_element_type=jnp.float32)
    for h in range(heads):
        s_h = jnp.where(causal, s_own[h * rows:(h + 1) * rows], -jnp.inf)
        own_buf[h] = s_h
        slot = home * heads + h
        mpart[slot] = jnp.maximum(mpart[slot], fold(s_h, jnp.maximum))

    for slot in range(slots):
        m = jnp.max(mpart[slot], axis=1, keepdims=True) * factor
        m_scr[slot] = m
        mpart[slot] = jnp.broadcast_to(jnp.where(m == -jnp.inf, 0.0, m), (rows, lanes))

    def mix(g, carry):
        width = s_buf.shape[2]
        ons = [on(slot, g) for slot in range(slots)]
        for slot in range(slots):
            @pl.when(ons[slot])
            def _():
                p = jnp.exp2(s_buf[g, slot * rows:(slot + 1) * rows] * factor - mpart[slot][:, :1])
                lpart[slot] += fold(p, jnp.add)
                p_buf[slot * rows:(slot + 1) * rows] = p.astype(jnp.bfloat16)

            @pl.when(jnp.logical_not(ons[slot]))
            def _():
                p_buf[slot * rows:(slot + 1) * rows] = jnp.zeros((rows, width), jnp.bfloat16)

        value = kv_ref[g, 1].reshape(chunks * HEAD_SIZE, HEAD_SIZE)
        pv = jnp.dot(p_buf[...], value, preferred_element_type=jnp.float32)
        for slot in range(slots):
            @pl.when(ons[slot])
            def _():
                acc_scr[slot] += pv[slot * rows:(slot + 1) * rows]
        return carry

    lax.fori_loop(0, groups, mix, 0)

    for h in range(heads):
        slot = home * heads + h
        p = jnp.exp2(own_buf[h] * factor - mpart[slot][:, :1])
        lpart[slot] += p
        acc_scr[slot] += jnp.dot(p.astype(jnp.bfloat16), own_ref[1],
                                 preferred_element_type=jnp.float32)

    for b in range(blocks):
        st_scr[...] = jnp.zeros(st_scr.shape, jnp.float32)
        for h in range(heads):
            slot = b * heads + h
            out_ref[b, :rows, h * HEAD_SIZE:(h + 1) * HEAD_SIZE] = acc_scr[slot]
            st_scr[:, h:h + 1] = m_scr[slot]
            st_scr[:, heads + h:heads + h + 1] = jnp.sum(lpart[slot], axis=1, keepdims=True)
        out_ref[b, rows:, :HEAD_SIZE] = st_scr[...].T[:STAT_ROWS]
        if heads > 1:
            out_ref[b, rows:, HEAD_SIZE:] = jnp.zeros((STAT_ROWS, (heads - 1) * HEAD_SIZE), jnp.float32)


def join_kernel(got_ref, *refs, sources, heads):
    rows = QUERY_GROUP_ROWS
    out_ref = refs[-1]
    cols = [got_ref[s, rows:, :HEAD_SIZE].T for s in range(sources)]
    for h in range(heads):
        ms = [c[:, h:h + 1] for c in cols]
        top = ms[0]
        for m in ms[1:]:
            top = jnp.maximum(top, m)
        top = jnp.where(top == -jnp.inf, 0.0, top)
        total = None
        acc = None
        for s in range(sources):
            fade = jnp.exp2(ms[s] - top)
            part_total = fade * cols[s][:, heads + h:heads + h + 1]
            part_acc = fade * got_ref[s, :rows, h * HEAD_SIZE:(h + 1) * HEAD_SIZE]
            total = part_total if total is None else total + part_total
            acc = part_acc if acc is None else acc + part_acc
        out_ref[:, h * HEAD_SIZE:(h + 1) * HEAD_SIZE] = acc / total


def join(a, b):
    acc_a, m_a, l_a = a
    acc_b, m_b, l_b = b
    m = jnp.maximum(m_a, m_b)
    m_safe = jnp.where(m == -jnp.inf, 0.0, m)
    f_a = jnp.exp2(m_a - m_safe)
    f_b = jnp.exp2(m_b - m_safe)
    acc = acc_a * f_a[..., None] + acc_b * f_b[..., None]
    return acc, m, l_a * f_a + l_b * f_b


def local(queries, query_key_value, cached_key_value, selected):
    rows = queries.shape[0]
    heads = queries.shape[1] // HEAD_SIZE
    head_group = QUERY_HEADS // KEY_VALUE_HEADS
    scale = 1.0 / math.sqrt(HEAD_SIZE)
    groups = lax.axis_size("blk")
    helpers = lax.axis_size("help")
    worker = lax.axis_index("blk")
    helper = lax.axis_index("help")
    piece = cached_key_value.shape[0]
    picks = selected.shape[1] * selected.shape[2]
    assert rows == QUERY_GROUP_ROWS and head_group % heads == 0 and selected.shape[0] == 1
    assert BLOCK_TOKENS % piece == 0 and piece % HEAD_SIZE == 0 and picks % HEAD_SIZE == 0
    per_group = piece * helpers // BLOCK_TOKENS
    query_blocks = helpers

    wanted = tuple((t * heads) // head_group for t in range(groups))
    chunks = piece // HEAD_SIZE
    send = pl.pallas_call(
        functools.partial(relayout_kernel, wanted=wanted, chunks=chunks),
        in_specs=[pl.BlockSpec(memory_space=pltpu.VMEM)],
        out_specs=pl.BlockSpec(memory_space=pltpu.VMEM),
        out_shape=jax.ShapeDtypeStruct((groups, 2, chunks, HEAD_SIZE, HEAD_SIZE), jnp.bfloat16),
    )(cached_key_value)
    held = lax.all_to_all(send, "blk", 0, 0, tiled=True)

    q = jnp.transpose(queries.reshape(rows, heads, HEAD_SIZE), (1, 0, 2)).reshape(heads * rows, HEAD_SIZE)
    sel_rows = selected.reshape(picks // HEAD_SIZE, HEAD_SIZE).astype(jnp.bfloat16)
    sel_pad = -(-(picks // HEAD_SIZE) // 16) * 16
    sel_rows = jnp.pad(sel_rows, ((0, sel_pad - picks // HEAD_SIZE), (0, 0)))
    q = jnp.concatenate([q, sel_rows], axis=0)
    q_all = lax.all_gather(q[None], "help", axis=0, tiled=True)
    sel_all = q_all[:, heads * rows:heads * rows + picks // HEAD_SIZE].astype(jnp.int32).reshape(
        query_blocks, selected.shape[1], selected.shape[2])

    kv_head = (worker * heads) // head_group
    own = query_key_value.reshape(rows, 2, KEY_VALUE_HEADS, HEAD_SIZE)
    own = lax.dynamic_index_in_dim(own, kv_head, axis=2, keepdims=False)
    own = jnp.stack([own[:, 0].T, own[:, 1]])

    my_heads = lax.dynamic_slice_in_dim(sel_all, worker * heads, heads, axis=1)
    piece_block = per_group * jnp.arange(groups, dtype=jnp.int32) + (helper * piece) // BLOCK_TOKENS
    hit = jnp.any(my_heads[:, :, None, :] == piece_block[None, None, :, None], axis=3)
    sel_flat = hit.astype(jnp.int32).reshape(-1)
    home = helper.reshape(1).astype(jnp.int32)

    slices = min(4, heads)
    part = heads // slices
    assert part * slices == heads and 2 * part <= STAT_ROWS
    width = part * HEAD_SIZE
    result = None
    for c in range(slices):
        kernel = functools.partial(attend_kernel, groups=groups, heads=part, first=c * part,
                                   all_heads=heads, blocks=query_blocks, chunks=chunks,
                                   factor=scale * math.log2(math.e))
        slots = query_blocks * part
        partial = pl.pallas_call(
            kernel,
            grid_spec=pltpu.PrefetchScalarGridSpec(
                num_scalar_prefetch=2,
                grid=(1,),
                in_specs=[
                    pl.BlockSpec((query_blocks, part * rows, HEAD_SIZE),
                                 lambda i, s, h, c=c: (0, c, 0)),
                    pl.BlockSpec((groups, 2, chunks, HEAD_SIZE, HEAD_SIZE),
                                 lambda i, s, h: (0, 0, 0, 0, 0)),
                    pl.BlockSpec((2, rows, HEAD_SIZE), lambda i, s, h: (0, 0, 0)),
                ],
                out_specs=pl.BlockSpec((query_blocks, rows + STAT_ROWS, width),
                                       lambda i, s, h: (0, 0, 0)),
                scratch_shapes=[
                    pltpu.VMEM((groups, slots * rows, piece), jnp.float32),
                    pltpu.VMEM((part, rows, rows), jnp.float32),
                    pltpu.VMEM((slots * rows, piece), jnp.bfloat16),
                    pltpu.VMEM((slots, rows, HEAD_SIZE), jnp.float32),
                    pltpu.VMEM((slots, rows, HEAD_SIZE), jnp.float32),
                    pltpu.VMEM((slots, rows, 1), jnp.float32),
                    pltpu.VMEM((slots, rows, HEAD_SIZE), jnp.float32),
                    pltpu.VMEM((rows, HEAD_SIZE), jnp.float32),
                ],
            ),
            compiler_params=pltpu.CompilerParams(vmem_limit_bytes=48 * 1024 * 1024),
            out_shape=jax.ShapeDtypeStruct((query_blocks, rows + STAT_ROWS, width), jnp.float32),
            cost_estimate=pl.CostEstimate(
                flops=4 * query_blocks * part * rows * groups * piece * HEAD_SIZE,
                transcendentals=query_blocks * part * rows * groups * piece,
                bytes_accessed=2 * groups * 2 * piece * HEAD_SIZE + 4 * query_blocks * rows * width),
        )(sel_flat, home, q_all, held, own)
        got = lax.all_to_all(partial, "help", 0, 0, tiled=True)
        first_join = c == 0
        result = pl.pallas_call(
            functools.partial(join_kernel, sources=helpers, heads=part),
            grid=(1,),
            in_specs=[pl.BlockSpec((helpers, rows + STAT_ROWS, width), lambda i: (0, 0, 0))]
            + ([] if first_join else [pl.BlockSpec(memory_space=pl.ANY)]),
            out_specs=pl.BlockSpec((rows, width), lambda i, c=c: (0, c)),
            out_shape=jax.ShapeDtypeStruct((rows, heads * HEAD_SIZE), jnp.float32),
            input_output_aliases={} if first_join else {1: 0},
        )(*((got,) if first_join else (got, result)))
    return result


def solution(mesh):
    in_specs = (P("help", "blk"), P("help", None), P(("blk", "help"), None), P("help", None, None))
    out_specs = P("help", "blk")
    return jax.shard_map(local, mesh=mesh, in_specs=in_specs, out_specs=out_specs, check_vma=False)
```

```python
import functools
import math

import jax
import jax.numpy as jnp
import numpy as np
from jax import lax
from jax.experimental import pallas as pl
from jax.experimental.pallas import tpu as pltpu
from jax.sharding import PartitionSpec as P

HEAD_SIZE = 128
QUERY_HEADS = 64
KEY_VALUE_HEADS = 8
BLOCK_TOKENS = 1024
QUERY_GROUP_ROWS = 128
STAT_ROWS = 8


def relayout_kernel(x_ref, out_ref, *, wanted, chunks):
    for t, kv_head in enumerate(wanted):
        for c in range(chunks):
            tokens = slice(c * HEAD_SIZE, (c + 1) * HEAD_SIZE)
            keys = x_ref[tokens, kv_head * HEAD_SIZE:(kv_head + 1) * HEAD_SIZE]
            out_ref[t, 0, c] = keys.astype(jnp.float32).T.astype(jnp.bfloat16)
            column = (KEY_VALUE_HEADS + kv_head) * HEAD_SIZE
            out_ref[t, 1, c] = x_ref[tokens, column:column + HEAD_SIZE]


def attend_kernel(sel_ref, home_ref, q_ref, kv_ref, own_ref, out_ref,
                  s_buf, own_buf, p_buf, mpart, lpart, m_scr, acc_scr, st_scr,
                  *, groups, heads, first, all_heads, blocks, chunks, factor):
    rows = QUERY_GROUP_ROWS
    slots = blocks * heads
    lanes = HEAD_SIZE
    q = q_ref[...].reshape(slots * rows, HEAD_SIZE)
    home = home_ref[0]
    mpart[...] = jnp.full(mpart.shape, -jnp.inf, jnp.float32)
    lpart[...] = jnp.zeros(lpart.shape, jnp.float32)
    acc_scr[...] = jnp.zeros(acc_scr.shape, jnp.float32)

    def on(slot, g):
        b, h = divmod(slot, heads)
        return sel_ref[(b * all_heads + first + h) * groups + g] != 0

    def fold(x, op):
        out = x[:, :lanes]
        for c in range(1, x.shape[1] // lanes):
            out = op(out, x[:, c * lanes:(c + 1) * lanes])
        return out

    def score(g, carry):
        if chunks == 1:
            s = jnp.dot(q, kv_ref[g, 0, 0], preferred_element_type=jnp.float32)
        else:
            s = jnp.concatenate(
                [jnp.dot(q, kv_ref[g, 0, c], preferred_element_type=jnp.float32)
                 for c in range(chunks)], axis=1)
        for slot in range(slots):
            @pl.when(on(slot, g))
            def _():
                s_slot = s[slot * rows:(slot + 1) * rows]
                s_buf[g, slot * rows:(slot + 1) * rows] = s_slot
                mpart[slot] = jnp.maximum(mpart[slot], fold(s_slot, jnp.maximum))
        return carry

    lax.fori_loop(0, groups, score, 0)

    causal = lax.broadcasted_iota(jnp.int32, (rows, rows), 0) >= lax.broadcasted_iota(
        jnp.int32, (rows, rows), 1)
    s_own = jnp.dot(q_ref[home], own_ref[0],
                    preferred_element_type=jnp.float32)
    for h in range(heads):
        s_h = jnp.where(causal, s_own[h * rows:(h + 1) * rows], -jnp.inf)
        own_buf[h] = s_h
        slot = home * heads + h
        mpart[slot] = jnp.maximum(mpart[slot], fold(s_h, jnp.maximum))

    for slot in range(slots):
        m = jnp.max(mpart[slot], axis=1, keepdims=True) * factor
        m_scr[slot] = m
        mpart[slot] = jnp.broadcast_to(jnp.where(m == -jnp.inf, 0.0, m), (rows, lanes))

    def mix(g, carry):
        ons = [on(slot, g) for slot in range(slots)]
        for slot in range(slots):
            @pl.when(ons[slot])
            def _():
                p = jnp.exp2(s_buf[g, slot * rows:(slot + 1) * rows] * factor - mpart[slot][:, :1])
                lpart[slot] += fold(p, jnp.add)
                p_buf[slot * rows:(slot + 1) * rows] = p.astype(jnp.bfloat16)

        value = kv_ref[g, 1].reshape(chunks * HEAD_SIZE, HEAD_SIZE)
        pv = jnp.dot(p_buf[...], value, preferred_element_type=jnp.float32)
        for slot in range(slots):
            @pl.when(ons[slot])
            def _():
                acc_scr[slot] += pv[slot * rows:(slot + 1) * rows]
        return carry

    lax.fori_loop(0, groups, mix, 0)

    for h in range(heads):
        slot = home * heads + h
        p = jnp.exp2(own_buf[h] * factor - mpart[slot][:, :1])
        lpart[slot] += p
        acc_scr[slot] += jnp.dot(p.astype(jnp.bfloat16), own_ref[1],
                                 preferred_element_type=jnp.float32)

    for b in range(blocks):
        st_scr[...] = jnp.zeros(st_scr.shape, jnp.float32)
        for h in range(heads):
            slot = b * heads + h
            out_ref[b, :rows, h * HEAD_SIZE:(h + 1) * HEAD_SIZE] = acc_scr[slot]
            st_scr[:, h:h + 1] = m_scr[slot]
            st_scr[:, heads + h:heads + h + 1] = jnp.sum(lpart[slot], axis=1, keepdims=True)
        out_ref[b, rows:, :HEAD_SIZE] = st_scr[...].T[:STAT_ROWS]
        if heads > 1:
            out_ref[b, rows:, HEAD_SIZE:] = jnp.zeros((STAT_ROWS, (heads - 1) * HEAD_SIZE), jnp.float32)


def join_kernel(got_ref, *refs, sources, heads):
    rows = QUERY_GROUP_ROWS
    out_ref = refs[-1]
    cols = [got_ref[s, rows:, :HEAD_SIZE].T for s in range(sources)]
    for h in range(heads):
        ms = [c[:, h:h + 1] for c in cols]
        top = ms[0]
        for m in ms[1:]:
            top = jnp.maximum(top, m)
        top = jnp.where(top == -jnp.inf, 0.0, top)
        total = None
        acc = None
        for s in range(sources):
            fade = jnp.exp2(ms[s] - top)
            part_total = fade * cols[s][:, heads + h:heads + h + 1]
            part_acc = fade * got_ref[s, :rows, h * HEAD_SIZE:(h + 1) * HEAD_SIZE]
            total = part_total if total is None else total + part_total
            acc = part_acc if acc is None else acc + part_acc
        out_ref[:, h * HEAD_SIZE:(h + 1) * HEAD_SIZE] = acc / total


def join(a, b):
    acc_a, m_a, l_a = a
    acc_b, m_b, l_b = b
    m = jnp.maximum(m_a, m_b)
    m_safe = jnp.where(m == -jnp.inf, 0.0, m)
    f_a = jnp.exp2(m_a - m_safe)
    f_b = jnp.exp2(m_b - m_safe)
    acc = acc_a * f_a[..., None] + acc_b * f_b[..., None]
    return acc, m, l_a * f_a + l_b * f_b


def local(queries, query_key_value, cached_key_value, selected):
    rows = queries.shape[0]
    heads = queries.shape[1] // HEAD_SIZE
    head_group = QUERY_HEADS // KEY_VALUE_HEADS
    scale = 1.0 / math.sqrt(HEAD_SIZE)
    groups = lax.axis_size("blk")
    helpers = lax.axis_size("help")
    worker = lax.axis_index("blk")
    helper = lax.axis_index("help")
    piece = cached_key_value.shape[0]
    picks = selected.shape[1] * selected.shape[2]
    assert rows == QUERY_GROUP_ROWS and head_group % heads == 0 and selected.shape[0] == 1
    assert BLOCK_TOKENS % piece == 0 and piece % HEAD_SIZE == 0 and picks % HEAD_SIZE == 0
    per_group = piece * helpers // BLOCK_TOKENS
    query_blocks = helpers

    wanted = tuple((t * heads) // head_group for t in range(groups))
    chunks = piece // HEAD_SIZE
    send = pl.pallas_call(
        functools.partial(relayout_kernel, wanted=wanted, chunks=chunks),
        in_specs=[pl.BlockSpec(memory_space=pltpu.VMEM)],
        out_specs=pl.BlockSpec(memory_space=pltpu.VMEM),
        out_shape=jax.ShapeDtypeStruct((groups, 2, chunks, HEAD_SIZE, HEAD_SIZE), jnp.bfloat16),
    )(cached_key_value)
    held = lax.all_to_all(send, "blk", 0, 0, tiled=True)

    q = jnp.transpose(queries.reshape(rows, heads, HEAD_SIZE), (1, 0, 2)).reshape(heads * rows, HEAD_SIZE)
    sel_rows = selected.reshape(picks // HEAD_SIZE, HEAD_SIZE).astype(jnp.bfloat16)
    sel_pad = -(-(picks // HEAD_SIZE) // 16) * 16
    sel_rows = jnp.pad(sel_rows, ((0, sel_pad - picks // HEAD_SIZE), (0, 0)))
    q = jnp.concatenate([q, sel_rows], axis=0)
    q_all = lax.all_gather(q[None], "help", axis=0, tiled=True)
    sel_all = q_all[:, heads * rows:heads * rows + picks // HEAD_SIZE].astype(jnp.int32).reshape(
        query_blocks, selected.shape[1], selected.shape[2])

    kv_head = (worker * heads) // head_group
    own = query_key_value.reshape(rows, 2, KEY_VALUE_HEADS, HEAD_SIZE)
    own = lax.dynamic_index_in_dim(own, kv_head, axis=2, keepdims=False)
    own = jnp.stack([own[:, 0].T, own[:, 1]])

    my_heads = lax.dynamic_slice_in_dim(sel_all, worker * heads, heads, axis=1)
    piece_block = per_group * jnp.arange(groups, dtype=jnp.int32) + (helper * piece) // BLOCK_TOKENS
    hit = jnp.any(my_heads[:, :, None, :] == piece_block[None, None, :, None], axis=3)
    sel_flat = hit.astype(jnp.int32).reshape(-1)
    home = helper.reshape(1).astype(jnp.int32)

    slices = min(4, heads)
    part = heads // slices
    assert part * slices == heads and 2 * part <= STAT_ROWS
    width = part * HEAD_SIZE
    result = None
    for c in range(slices):
        kernel = functools.partial(attend_kernel, groups=groups, heads=part, first=c * part,
                                   all_heads=heads, blocks=query_blocks, chunks=chunks,
                                   factor=scale * math.log2(math.e))
        slots = query_blocks * part
        partial = pl.pallas_call(
            kernel,
            grid_spec=pltpu.PrefetchScalarGridSpec(
                num_scalar_prefetch=2,
                grid=(1,),
                in_specs=[
                    pl.BlockSpec((query_blocks, part * rows, HEAD_SIZE),
                                 lambda i, s, h, c=c: (0, c, 0)),
                    pl.BlockSpec((groups, 2, chunks, HEAD_SIZE, HEAD_SIZE),
                                 lambda i, s, h: (0, 0, 0, 0, 0)),
                    pl.BlockSpec((2, rows, HEAD_SIZE), lambda i, s, h: (0, 0, 0)),
                ],
                out_specs=pl.BlockSpec((query_blocks, rows + STAT_ROWS, width),
                                       lambda i, s, h: (0, 0, 0)),
                scratch_shapes=[
                    pltpu.VMEM((groups, slots * rows, piece), jnp.float32),
                    pltpu.VMEM((part, rows, rows), jnp.float32),
                    pltpu.VMEM((slots * rows, piece), jnp.bfloat16),
                    pltpu.VMEM((slots, rows, HEAD_SIZE), jnp.float32),
                    pltpu.VMEM((slots, rows, HEAD_SIZE), jnp.float32),
                    pltpu.VMEM((slots, rows, 1), jnp.float32),
                    pltpu.VMEM((slots, rows, HEAD_SIZE), jnp.float32),
                    pltpu.VMEM((rows, HEAD_SIZE), jnp.float32),
                ],
            ),
            compiler_params=pltpu.CompilerParams(vmem_limit_bytes=48 * 1024 * 1024),
            out_shape=jax.ShapeDtypeStruct((query_blocks, rows + STAT_ROWS, width), jnp.float32),
            cost_estimate=pl.CostEstimate(
                flops=4 * query_blocks * part * rows * groups * piece * HEAD_SIZE,
                transcendentals=query_blocks * part * rows * groups * piece,
                bytes_accessed=2 * groups * 2 * piece * HEAD_SIZE + 4 * query_blocks * rows * width),
        )(sel_flat, home, q_all, held, own)
        got = lax.all_to_all(partial, "help", 0, 0, tiled=True)
        first_join = c == 0
        result = pl.pallas_call(
            functools.partial(join_kernel, sources=helpers, heads=part),
            grid=(1,),
            in_specs=[pl.BlockSpec((helpers, rows + STAT_ROWS, width), lambda i: (0, 0, 0))]
            + ([] if first_join else [pl.BlockSpec(memory_space=pl.ANY)]),
            out_specs=pl.BlockSpec((rows, width), lambda i, c=c: (0, c)),
            out_shape=jax.ShapeDtypeStruct((rows, heads * HEAD_SIZE), jnp.float32),
            input_output_aliases={} if first_join else {1: 0},
        )(*((got,) if first_join else (got, result)))
    return result


def solution(mesh):
    in_specs = (P("help", "blk"), P("help", None), P(("blk", "help"), None), P("help", None, None))
    out_specs = P("help", "blk")
    return jax.shard_map(local, mesh=mesh, in_specs=in_specs, out_specs=out_specs, check_vma=False)
```

```python
import functools
import math

import jax
import jax.numpy as jnp
import numpy as np
from jax import lax
from jax.experimental import pallas as pl
from jax.experimental.pallas import tpu as pltpu
from jax.sharding import PartitionSpec as P

HEAD_SIZE = 128
QUERY_HEADS = 64
KEY_VALUE_HEADS = 8
BLOCK_TOKENS = 1024
QUERY_GROUP_ROWS = 128
STAT_ROWS = 8


def relayout_kernel(x_ref, out_ref, *, wanted, chunks):
    for t, kv_head in enumerate(wanted):
        for c in range(chunks):
            tokens = slice(c * HEAD_SIZE, (c + 1) * HEAD_SIZE)
            keys = x_ref[tokens, kv_head * HEAD_SIZE:(kv_head + 1) * HEAD_SIZE]
            out_ref[t, 0, c] = keys.astype(jnp.float32).T.astype(jnp.bfloat16)
            column = (KEY_VALUE_HEADS + kv_head) * HEAD_SIZE
            out_ref[t, 1, c] = x_ref[tokens, column:column + HEAD_SIZE]


def attend_kernel(sel_ref, home_ref, q_ref, kv_ref, own_ref, out_ref,
                  s_buf, own_buf, p_buf, mpart, lpart, m_scr, acc_scr, st_scr,
                  *, groups, heads, first, all_heads, blocks, chunks, factor):
    rows = QUERY_GROUP_ROWS
    slots = blocks * heads
    lanes = HEAD_SIZE
    q = q_ref[...].reshape(slots * rows, HEAD_SIZE)
    home = home_ref[0]
    mpart[...] = jnp.full(mpart.shape, -jnp.inf, jnp.float32)
    lpart[...] = jnp.zeros(lpart.shape, jnp.float32)
    acc_scr[...] = jnp.zeros(acc_scr.shape, jnp.float32)

    def on(slot, g):
        b, h = divmod(slot, heads)
        return sel_ref[(b * all_heads + first + h) * groups + g] != 0

    def fold(x, op):
        out = x[:, :lanes]
        for c in range(1, x.shape[1] // lanes):
            out = op(out, x[:, c * lanes:(c + 1) * lanes])
        return out

    def score(g, carry):
        for c in range(chunks):
            s_buf[g, :, c * HEAD_SIZE:(c + 1) * HEAD_SIZE] = jnp.dot(
                q, kv_ref[g, 0, c], preferred_element_type=jnp.float32)
        for slot in range(slots):
            @pl.when(on(slot, g))
            def _():
                mpart[slot] = jnp.maximum(
                    mpart[slot], fold(s_buf[g, slot * rows:(slot + 1) * rows], jnp.maximum))
        return carry

    lax.fori_loop(0, groups, score, 0)

    causal = lax.broadcasted_iota(jnp.int32, (rows, rows), 0) >= lax.broadcasted_iota(
        jnp.int32, (rows, rows), 1)
    s_own = jnp.dot(q_ref[home], own_ref[0],
                    preferred_element_type=jnp.float32)
    for h in range(heads):
        s_h = jnp.where(causal, s_own[h * rows:(h + 1) * rows], -jnp.inf)
        own_buf[h] = s_h
        slot = home * heads + h
        mpart[slot] = jnp.maximum(mpart[slot], fold(s_h, jnp.maximum))

    for slot in range(slots):
        m = jnp.max(mpart[slot], axis=1, keepdims=True) * factor
        m_scr[slot] = m
        mpart[slot] = jnp.broadcast_to(jnp.where(m == -jnp.inf, 0.0, m), (rows, lanes))

    def mix(g, carry):
        ons = [on(slot, g) for slot in range(slots)]
        for slot in range(slots):
            @pl.when(ons[slot])
            def _():
                p = jnp.exp2(s_buf[g, slot * rows:(slot + 1) * rows] * factor - mpart[slot][:, :1])
                lpart[slot] += fold(p, jnp.add)
                p_buf[slot * rows:(slot + 1) * rows] = p.astype(jnp.bfloat16)

        value = kv_ref[g, 1].reshape(chunks * HEAD_SIZE, HEAD_SIZE)
        pv = jnp.dot(p_buf[...], value, preferred_element_type=jnp.float32)
        for slot in range(slots):
            @pl.when(ons[slot])
            def _():
                acc_scr[slot] += pv[slot * rows:(slot + 1) * rows]
        return carry

    lax.fori_loop(0, groups, mix, 0)

    for h in range(heads):
        slot = home * heads + h
        p = jnp.exp2(own_buf[h] * factor - mpart[slot][:, :1])
        lpart[slot] += p
        acc_scr[slot] += jnp.dot(p.astype(jnp.bfloat16), own_ref[1],
                                 preferred_element_type=jnp.float32)

    for b in range(blocks):
        st_scr[...] = jnp.zeros(st_scr.shape, jnp.float32)
        for h in range(heads):
            slot = b * heads + h
            out_ref[b, :rows, h * HEAD_SIZE:(h + 1) * HEAD_SIZE] = acc_scr[slot]
            st_scr[:, h:h + 1] = m_scr[slot]
            st_scr[:, heads + h:heads + h + 1] = jnp.sum(lpart[slot], axis=1, keepdims=True)
        out_ref[b, rows:, :HEAD_SIZE] = st_scr[...].T[:STAT_ROWS]
        if heads > 1:
            out_ref[b, rows:, HEAD_SIZE:] = jnp.zeros((STAT_ROWS, (heads - 1) * HEAD_SIZE), jnp.float32)


def join_kernel(got_ref, *refs, sources, heads):
    rows = QUERY_GROUP_ROWS
    out_ref = refs[-1]
    cols = [got_ref[s, rows:, :HEAD_SIZE].T for s in range(sources)]
    for h in range(heads):
        ms = [c[:, h:h + 1] for c in cols]
        top = ms[0]
        for m in ms[1:]:
            top = jnp.maximum(top, m)
        top = jnp.where(top == -jnp.inf, 0.0, top)
        total = None
        acc = None
        for s in range(sources):
            fade = jnp.exp2(ms[s] - top)
            part_total = fade * cols[s][:, heads + h:heads + h + 1]
            part_acc = fade * got_ref[s, :rows, h * HEAD_SIZE:(h + 1) * HEAD_SIZE]
            total = part_total if total is None else total + part_total
            acc = part_acc if acc is None else acc + part_acc
        out_ref[:, h * HEAD_SIZE:(h + 1) * HEAD_SIZE] = acc / total


def join(a, b):
    acc_a, m_a, l_a = a
    acc_b, m_b, l_b = b
    m = jnp.maximum(m_a, m_b)
    m_safe = jnp.where(m == -jnp.inf, 0.0, m)
    f_a = jnp.exp2(m_a - m_safe)
    f_b = jnp.exp2(m_b - m_safe)
    acc = acc_a * f_a[..., None] + acc_b * f_b[..., None]
    return acc, m, l_a * f_a + l_b * f_b


def local(queries, query_key_value, cached_key_value, selected):
    rows = queries.shape[0]
    heads = queries.shape[1] // HEAD_SIZE
    head_group = QUERY_HEADS // KEY_VALUE_HEADS
    scale = 1.0 / math.sqrt(HEAD_SIZE)
    groups = lax.axis_size("blk")
    helpers = lax.axis_size("help")
    worker = lax.axis_index("blk")
    helper = lax.axis_index("help")
    piece = cached_key_value.shape[0]
    picks = selected.shape[1] * selected.shape[2]
    assert rows == QUERY_GROUP_ROWS and head_group % heads == 0 and selected.shape[0] == 1
    assert BLOCK_TOKENS % piece == 0 and piece % HEAD_SIZE == 0 and picks % HEAD_SIZE == 0
    per_group = piece * helpers // BLOCK_TOKENS
    query_blocks = helpers

    wanted = tuple((t * heads) // head_group for t in range(groups))
    chunks = piece // HEAD_SIZE
    send = pl.pallas_call(
        functools.partial(relayout_kernel, wanted=wanted, chunks=chunks),
        in_specs=[pl.BlockSpec(memory_space=pltpu.VMEM)],
        out_specs=pl.BlockSpec(memory_space=pltpu.VMEM),
        out_shape=jax.ShapeDtypeStruct((groups, 2, chunks, HEAD_SIZE, HEAD_SIZE), jnp.bfloat16),
    )(cached_key_value)
    held = lax.all_to_all(send, "blk", 0, 0, tiled=True)

    q = jnp.transpose(queries.reshape(rows, heads, HEAD_SIZE), (1, 0, 2)).reshape(heads * rows, HEAD_SIZE)
    sel_rows = selected.reshape(picks // HEAD_SIZE, HEAD_SIZE).astype(jnp.bfloat16)
    sel_pad = -(-(picks // HEAD_SIZE) // 16) * 16
    sel_rows = jnp.pad(sel_rows, ((0, sel_pad - picks // HEAD_SIZE), (0, 0)))
    q = jnp.concatenate([q, sel_rows], axis=0)
    q_all = lax.all_gather(q[None], "help", axis=0, tiled=True)
    sel_all = q_all[:, heads * rows:heads * rows + picks // HEAD_SIZE].astype(jnp.int32).reshape(
        query_blocks, selected.shape[1], selected.shape[2])

    kv_head = (worker * heads) // head_group
    own = query_key_value.reshape(rows, 2, KEY_VALUE_HEADS, HEAD_SIZE)
    own = lax.dynamic_index_in_dim(own, kv_head, axis=2, keepdims=False)
    own = jnp.stack([own[:, 0].T, own[:, 1]])

    my_heads = lax.dynamic_slice_in_dim(sel_all, worker * heads, heads, axis=1)
    piece_block = per_group * jnp.arange(groups, dtype=jnp.int32) + (helper * piece) // BLOCK_TOKENS
    hit = jnp.any(my_heads[:, :, None, :] == piece_block[None, None, :, None], axis=3)
    sel_flat = hit.astype(jnp.int32).reshape(-1)
    home = helper.reshape(1).astype(jnp.int32)

    slices = min(4, heads)
    part = heads // slices
    assert part * slices == heads and 2 * part <= STAT_ROWS
    width = part * HEAD_SIZE
    result = None
    for c in range(slices):
        kernel = functools.partial(attend_kernel, groups=groups, heads=part, first=c * part,
                                   all_heads=heads, blocks=query_blocks, chunks=chunks,
                                   factor=scale * math.log2(math.e))
        slots = query_blocks * part
        partial = pl.pallas_call(
            kernel,
            grid_spec=pltpu.PrefetchScalarGridSpec(
                num_scalar_prefetch=2,
                grid=(1,),
                in_specs=[
                    pl.BlockSpec((query_blocks, part * rows, HEAD_SIZE),
                                 lambda i, s, h, c=c: (0, c, 0)),
                    pl.BlockSpec((groups, 2, chunks, HEAD_SIZE, HEAD_SIZE),
                                 lambda i, s, h: (0, 0, 0, 0, 0)),
                    pl.BlockSpec((2, rows, HEAD_SIZE), lambda i, s, h: (0, 0, 0)),
                ],
                out_specs=pl.BlockSpec((query_blocks, rows + STAT_ROWS, width),
                                       lambda i, s, h: (0, 0, 0)),
                scratch_shapes=[
                    pltpu.VMEM((groups, slots * rows, piece), jnp.float32),
                    pltpu.VMEM((part, rows, rows), jnp.float32),
                    pltpu.VMEM((slots * rows, piece), jnp.bfloat16),
                    pltpu.VMEM((slots, rows, HEAD_SIZE), jnp.float32),
                    pltpu.VMEM((slots, rows, HEAD_SIZE), jnp.float32),
                    pltpu.VMEM((slots, rows, 1), jnp.float32),
                    pltpu.VMEM((slots, rows, HEAD_SIZE), jnp.float32),
                    pltpu.VMEM((rows, HEAD_SIZE), jnp.float32),
                ],
            ),
            compiler_params=pltpu.CompilerParams(vmem_limit_bytes=48 * 1024 * 1024),
            out_shape=jax.ShapeDtypeStruct((query_blocks, rows + STAT_ROWS, width), jnp.float32),
            cost_estimate=pl.CostEstimate(
                flops=4 * query_blocks * part * rows * groups * piece * HEAD_SIZE,
                transcendentals=query_blocks * part * rows * groups * piece,
                bytes_accessed=2 * groups * 2 * piece * HEAD_SIZE + 4 * query_blocks * rows * width),
        )(sel_flat, home, q_all, held, own)
        got = lax.all_to_all(partial, "help", 0, 0, tiled=True)
        first_join = c == 0
        result = pl.pallas_call(
            functools.partial(join_kernel, sources=helpers, heads=part),
            grid=(1,),
            in_specs=[pl.BlockSpec((helpers, rows + STAT_ROWS, width), lambda i: (0, 0, 0))]
            + ([] if first_join else [pl.BlockSpec(memory_space=pl.ANY)]),
            out_specs=pl.BlockSpec((rows, width), lambda i, c=c: (0, c)),
            out_shape=jax.ShapeDtypeStruct((rows, heads * HEAD_SIZE), jnp.float32),
            input_output_aliases={} if first_join else {1: 0},
        )(*((got,) if first_join else (got, result)))
    return result


def solution(mesh):
    in_specs = (P("help", "blk"), P("help", None), P(("blk", "help"), None), P("help", None, None))
    out_specs = P("help", "blk")
    return jax.shard_map(local, mesh=mesh, in_specs=in_specs, out_specs=out_specs, check_vma=False)
```

```python
import functools
import math

import jax
import jax.numpy as jnp
import numpy as np
from jax import lax
from jax.experimental import pallas as pl
from jax.experimental.pallas import tpu as pltpu
from jax.sharding import PartitionSpec as P

HEAD_SIZE = 128
QUERY_HEADS = 64
KEY_VALUE_HEADS = 8
BLOCK_TOKENS = 1024
QUERY_GROUP_ROWS = 128
STAT_ROWS = 8


def relayout_kernel(x_ref, out_ref, *, wanted, chunks):
    for t, kv_head in enumerate(wanted):
        for c in range(chunks):
            tokens = slice(c * HEAD_SIZE, (c + 1) * HEAD_SIZE)
            keys = x_ref[tokens, kv_head * HEAD_SIZE:(kv_head + 1) * HEAD_SIZE]
            out_ref[t, 0, c] = keys.astype(jnp.float32).T.astype(jnp.bfloat16)
            column = (KEY_VALUE_HEADS + kv_head) * HEAD_SIZE
            out_ref[t, 1, c] = x_ref[tokens, column:column + HEAD_SIZE]


def attend_kernel(sel_ref, home_ref, q_ref, kv_ref, own_ref, out_ref,
                  s_buf, own_buf, p_buf, mpart, lpart, m_scr, acc_scr, st_scr,
                  *, groups, heads, first, all_heads, blocks, chunks, factor):
    rows = QUERY_GROUP_ROWS
    slots = blocks * heads
    lanes = HEAD_SIZE
    q = q_ref[...].reshape(slots * rows, HEAD_SIZE)
    home = home_ref[0]
    mpart[...] = jnp.full(mpart.shape, -jnp.inf, jnp.float32)
    lpart[...] = jnp.zeros(lpart.shape, jnp.float32)
    acc_scr[...] = jnp.zeros(acc_scr.shape, jnp.float32)

    def on(slot, g):
        b, h = divmod(slot, heads)
        return sel_ref[(b * all_heads + first + h) * groups + g] != 0

    def fold(x, op):
        out = x[:, :lanes]
        for c in range(1, x.shape[1] // lanes):
            out = op(out, x[:, c * lanes:(c + 1) * lanes])
        return out

    def score(g, carry):
        for c in range(chunks):
            s_buf[g, :, c * HEAD_SIZE:(c + 1) * HEAD_SIZE] = jnp.dot(
                q, kv_ref[g, 0, c], preferred_element_type=jnp.float32)
        for slot in range(slots):
            @pl.when(on(slot, g))
            def _():
                mpart[slot] = jnp.maximum(
                    mpart[slot], fold(s_buf[g, slot * rows:(slot + 1) * rows], jnp.maximum))
        return carry

    lax.fori_loop(0, groups, score, 0, unroll=2)

    causal = lax.broadcasted_iota(jnp.int32, (rows, rows), 0) >= lax.broadcasted_iota(
        jnp.int32, (rows, rows), 1)
    s_own = jnp.dot(q_ref[home], own_ref[0],
                    preferred_element_type=jnp.float32)
    for h in range(heads):
        s_h = jnp.where(causal, s_own[h * rows:(h + 1) * rows], -jnp.inf)
        own_buf[h] = s_h
        slot = home * heads + h
        mpart[slot] = jnp.maximum(mpart[slot], fold(s_h, jnp.maximum))

    for slot in range(slots):
        m = jnp.max(mpart[slot], axis=1, keepdims=True) * factor
        m_scr[slot] = m
        mpart[slot] = jnp.broadcast_to(jnp.where(m == -jnp.inf, 0.0, m), (rows, lanes))

    def mix(g, carry):
        ons = [on(slot, g) for slot in range(slots)]
        for slot in range(slots):
            @pl.when(ons[slot])
            def _():
                p = jnp.exp2(s_buf[g, slot * rows:(slot + 1) * rows] * factor - mpart[slot][:, :1])
                lpart[slot] += fold(p, jnp.add)
                p_buf[slot * rows:(slot + 1) * rows] = p.astype(jnp.bfloat16)

        value = kv_ref[g, 1].reshape(chunks * HEAD_SIZE, HEAD_SIZE)
        pv = jnp.dot(p_buf[...], value, preferred_element_type=jnp.float32)
        for slot in range(slots):
            @pl.when(ons[slot])
            def _():
                acc_scr[slot] += pv[slot * rows:(slot + 1) * rows]
        return carry

    lax.fori_loop(0, groups, mix, 0, unroll=2)

    for h in range(heads):
        slot = home * heads + h
        p = jnp.exp2(own_buf[h] * factor - mpart[slot][:, :1])
        lpart[slot] += p
        acc_scr[slot] += jnp.dot(p.astype(jnp.bfloat16), own_ref[1],
                                 preferred_element_type=jnp.float32)

    for b in range(blocks):
        st_scr[...] = jnp.zeros(st_scr.shape, jnp.float32)
        for h in range(heads):
            slot = b * heads + h
            out_ref[b, :rows, h * HEAD_SIZE:(h + 1) * HEAD_SIZE] = acc_scr[slot]
            st_scr[:, h:h + 1] = m_scr[slot]
            st_scr[:, heads + h:heads + h + 1] = jnp.sum(lpart[slot], axis=1, keepdims=True)
        out_ref[b, rows:, :HEAD_SIZE] = st_scr[...].T[:STAT_ROWS]
        if heads > 1:
            out_ref[b, rows:, HEAD_SIZE:] = jnp.zeros((STAT_ROWS, (heads - 1) * HEAD_SIZE), jnp.float32)


def join_kernel(got_ref, *refs, sources, heads):
    rows = QUERY_GROUP_ROWS
    out_ref = refs[-1]
    cols = [got_ref[s, rows:, :HEAD_SIZE].T for s in range(sources)]
    for h in range(heads):
        ms = [c[:, h:h + 1] for c in cols]
        top = ms[0]
        for m in ms[1:]:
            top = jnp.maximum(top, m)
        top = jnp.where(top == -jnp.inf, 0.0, top)
        total = None
        acc = None
        for s in range(sources):
            fade = jnp.exp2(ms[s] - top)
            part_total = fade * cols[s][:, heads + h:heads + h + 1]
            part_acc = fade * got_ref[s, :rows, h * HEAD_SIZE:(h + 1) * HEAD_SIZE]
            total = part_total if total is None else total + part_total
            acc = part_acc if acc is None else acc + part_acc
        out_ref[:, h * HEAD_SIZE:(h + 1) * HEAD_SIZE] = acc / total


def join(a, b):
    acc_a, m_a, l_a = a
    acc_b, m_b, l_b = b
    m = jnp.maximum(m_a, m_b)
    m_safe = jnp.where(m == -jnp.inf, 0.0, m)
    f_a = jnp.exp2(m_a - m_safe)
    f_b = jnp.exp2(m_b - m_safe)
    acc = acc_a * f_a[..., None] + acc_b * f_b[..., None]
    return acc, m, l_a * f_a + l_b * f_b


def local(queries, query_key_value, cached_key_value, selected):
    rows = queries.shape[0]
    heads = queries.shape[1] // HEAD_SIZE
    head_group = QUERY_HEADS // KEY_VALUE_HEADS
    scale = 1.0 / math.sqrt(HEAD_SIZE)
    groups = lax.axis_size("blk")
    helpers = lax.axis_size("help")
    worker = lax.axis_index("blk")
    helper = lax.axis_index("help")
    piece = cached_key_value.shape[0]
    picks = selected.shape[1] * selected.shape[2]
    assert rows == QUERY_GROUP_ROWS and head_group % heads == 0 and selected.shape[0] == 1
    assert BLOCK_TOKENS % piece == 0 and piece % HEAD_SIZE == 0 and picks % HEAD_SIZE == 0
    per_group = piece * helpers // BLOCK_TOKENS
    query_blocks = helpers

    wanted = tuple((t * heads) // head_group for t in range(groups))
    chunks = piece // HEAD_SIZE
    send = pl.pallas_call(
        functools.partial(relayout_kernel, wanted=wanted, chunks=chunks),
        in_specs=[pl.BlockSpec(memory_space=pltpu.VMEM)],
        out_specs=pl.BlockSpec(memory_space=pltpu.VMEM),
        out_shape=jax.ShapeDtypeStruct((groups, 2, chunks, HEAD_SIZE, HEAD_SIZE), jnp.bfloat16),
    )(cached_key_value)
    held = lax.all_to_all(send, "blk", 0, 0, tiled=True)

    q = jnp.transpose(queries.reshape(rows, heads, HEAD_SIZE), (1, 0, 2)).reshape(heads * rows, HEAD_SIZE)
    sel_rows = selected.reshape(picks // HEAD_SIZE, HEAD_SIZE).astype(jnp.bfloat16)
    sel_pad = -(-(picks // HEAD_SIZE) // 16) * 16
    sel_rows = jnp.pad(sel_rows, ((0, sel_pad - picks // HEAD_SIZE), (0, 0)))
    q = jnp.concatenate([q, sel_rows], axis=0)
    q_all = lax.all_gather(q[None], "help", axis=0, tiled=True)
    sel_all = q_all[:, heads * rows:heads * rows + picks // HEAD_SIZE].astype(jnp.int32).reshape(
        query_blocks, selected.shape[1], selected.shape[2])

    kv_head = (worker * heads) // head_group
    own = query_key_value.reshape(rows, 2, KEY_VALUE_HEADS, HEAD_SIZE)
    own = lax.dynamic_index_in_dim(own, kv_head, axis=2, keepdims=False)
    own = jnp.stack([own[:, 0].T, own[:, 1]])

    my_heads = lax.dynamic_slice_in_dim(sel_all, worker * heads, heads, axis=1)
    piece_block = per_group * jnp.arange(groups, dtype=jnp.int32) + (helper * piece) // BLOCK_TOKENS
    hit = jnp.any(my_heads[:, :, None, :] == piece_block[None, None, :, None], axis=3)
    sel_flat = hit.astype(jnp.int32).reshape(-1)
    home = helper.reshape(1).astype(jnp.int32)

    slices = min(4, heads)
    part = heads // slices
    assert part * slices == heads and 2 * part <= STAT_ROWS
    width = part * HEAD_SIZE
    result = None
    for c in range(slices):
        kernel = functools.partial(attend_kernel, groups=groups, heads=part, first=c * part,
                                   all_heads=heads, blocks=query_blocks, chunks=chunks,
                                   factor=scale * math.log2(math.e))
        slots = query_blocks * part
        partial = pl.pallas_call(
            kernel,
            grid_spec=pltpu.PrefetchScalarGridSpec(
                num_scalar_prefetch=2,
                grid=(1,),
                in_specs=[
                    pl.BlockSpec((query_blocks, part * rows, HEAD_SIZE),
                                 lambda i, s, h, c=c: (0, c, 0)),
                    pl.BlockSpec((groups, 2, chunks, HEAD_SIZE, HEAD_SIZE),
                                 lambda i, s, h: (0, 0, 0, 0, 0)),
                    pl.BlockSpec((2, rows, HEAD_SIZE), lambda i, s, h: (0, 0, 0)),
                ],
                out_specs=pl.BlockSpec((query_blocks, rows + STAT_ROWS, width),
                                       lambda i, s, h: (0, 0, 0)),
                scratch_shapes=[
                    pltpu.VMEM((groups, slots * rows, piece), jnp.float32),
                    pltpu.VMEM((part, rows, rows), jnp.float32),
                    pltpu.VMEM((slots * rows, piece), jnp.bfloat16),
                    pltpu.VMEM((slots, rows, HEAD_SIZE), jnp.float32),
                    pltpu.VMEM((slots, rows, HEAD_SIZE), jnp.float32),
                    pltpu.VMEM((slots, rows, 1), jnp.float32),
                    pltpu.VMEM((slots, rows, HEAD_SIZE), jnp.float32),
                    pltpu.VMEM((rows, HEAD_SIZE), jnp.float32),
                ],
            ),
            compiler_params=pltpu.CompilerParams(vmem_limit_bytes=48 * 1024 * 1024),
            out_shape=jax.ShapeDtypeStruct((query_blocks, rows + STAT_ROWS, width), jnp.float32),
            cost_estimate=pl.CostEstimate(
                flops=4 * query_blocks * part * rows * groups * piece * HEAD_SIZE,
                transcendentals=query_blocks * part * rows * groups * piece,
                bytes_accessed=2 * groups * 2 * piece * HEAD_SIZE + 4 * query_blocks * rows * width),
        )(sel_flat, home, q_all, held, own)
        got = lax.all_to_all(partial, "help", 0, 0, tiled=True)
        first_join = c == 0
        result = pl.pallas_call(
            functools.partial(join_kernel, sources=helpers, heads=part),
            grid=(1,),
            in_specs=[pl.BlockSpec((helpers, rows + STAT_ROWS, width), lambda i: (0, 0, 0))]
            + ([] if first_join else [pl.BlockSpec(memory_space=pl.ANY)]),
            out_specs=pl.BlockSpec((rows, width), lambda i, c=c: (0, c)),
            out_shape=jax.ShapeDtypeStruct((rows, heads * HEAD_SIZE), jnp.float32),
            input_output_aliases={} if first_join else {1: 0},
        )(*((got,) if first_join else (got, result)))
    return result


def solution(mesh):
    in_specs = (P("help", "blk"), P("help", None), P(("blk", "help"), None), P("help", None, None))
    out_specs = P("help", "blk")
    return jax.shard_map(local, mesh=mesh, in_specs=in_specs, out_specs=out_specs, check_vma=False)
```

```python
import functools
import math

import jax
import jax.numpy as jnp
import numpy as np
from jax import lax
from jax.experimental import pallas as pl
from jax.experimental.pallas import tpu as pltpu
from jax.sharding import PartitionSpec as P

HEAD_SIZE = 128
QUERY_HEADS = 64
KEY_VALUE_HEADS = 8
BLOCK_TOKENS = 1024
QUERY_GROUP_ROWS = 128
STAT_ROWS = 8


def relayout_kernel(x_ref, out_ref, *, wanted, chunks):
    for t, kv_head in enumerate(wanted):
        for c in range(chunks):
            tokens = slice(c * HEAD_SIZE, (c + 1) * HEAD_SIZE)
            keys = x_ref[tokens, kv_head * HEAD_SIZE:(kv_head + 1) * HEAD_SIZE]
            out_ref[t, 0, c] = keys.astype(jnp.float32).T.astype(jnp.bfloat16)
            column = (KEY_VALUE_HEADS + kv_head) * HEAD_SIZE
            out_ref[t, 1, c] = x_ref[tokens, column:column + HEAD_SIZE]


def attend_kernel(sel_ref, home_ref, q_ref, kv_ref, own_ref, out_ref,
                  s_buf, own_buf, p_buf, mpart, lpart, m_scr, acc_scr, st_scr,
                  *, groups, heads, first, all_heads, blocks, chunks, factor):
    rows = QUERY_GROUP_ROWS
    slots = blocks * heads
    lanes = HEAD_SIZE
    q = q_ref[...].reshape(slots * rows, HEAD_SIZE)
    home = home_ref[0]
    mpart[...] = jnp.full(mpart.shape, -jnp.inf, jnp.float32)
    lpart[...] = jnp.zeros(lpart.shape, jnp.float32)
    acc_scr[...] = jnp.zeros(acc_scr.shape, jnp.float32)

    def on(slot, g):
        b, h = divmod(slot, heads)
        return sel_ref[(b * all_heads + first + h) * groups + g] != 0

    def fold(x, op):
        out = x[:, :lanes]
        for c in range(1, x.shape[1] // lanes):
            out = op(out, x[:, c * lanes:(c + 1) * lanes])
        return out

    def score(g, carry):
        for c in range(chunks):
            s_buf[g, :, c * HEAD_SIZE:(c + 1) * HEAD_SIZE] = jnp.dot(
                q, kv_ref[g, 0, c], preferred_element_type=jnp.float32)
        for slot in range(slots):
            @pl.when(on(slot, g))
            def _():
                mpart[slot] = jnp.maximum(
                    mpart[slot], fold(s_buf[g, slot * rows:(slot + 1) * rows], jnp.maximum))
        return carry

    lax.fori_loop(0, groups, score, 0)

    causal = lax.broadcasted_iota(jnp.int32, (rows, rows), 0) >= lax.broadcasted_iota(
        jnp.int32, (rows, rows), 1)
    s_own = jnp.dot(q_ref[home], own_ref[0],
                    preferred_element_type=jnp.float32)
    for h in range(heads):
        s_h = jnp.where(causal, s_own[h * rows:(h + 1) * rows], -jnp.inf)
        own_buf[h] = s_h
        slot = home * heads + h
        mpart[slot] = jnp.maximum(mpart[slot], fold(s_h, jnp.maximum))

    for slot in range(slots):
        m = jnp.max(mpart[slot], axis=1, keepdims=True) * factor
        m_scr[slot] = m
        mpart[slot] = jnp.broadcast_to(jnp.where(m == -jnp.inf, 0.0, m), (rows, lanes))

    def mix(g, carry):
        ons = [on(slot, g) for slot in range(slots)]
        for slot in range(slots):
            @pl.when(ons[slot])
            def _():
                p = jnp.exp2(s_buf[g, slot * rows:(slot + 1) * rows] * factor - mpart[slot][:, :1])
                lpart[slot] += fold(p, jnp.add)
                p_buf[slot * rows:(slot + 1) * rows] = p.astype(jnp.bfloat16)

        value = kv_ref[g, 1].reshape(chunks * HEAD_SIZE, HEAD_SIZE)
        pv = jnp.dot(p_buf[...], value, preferred_element_type=jnp.float32)
        for slot in range(slots):
            @pl.when(ons[slot])
            def _():
                acc_scr[slot] += pv[slot * rows:(slot + 1) * rows]
        return carry

    lax.fori_loop(0, groups, mix, 0)

    for h in range(heads):
        slot = home * heads + h
        p = jnp.exp2(own_buf[h] * factor - mpart[slot][:, :1])
        lpart[slot] += p
        acc_scr[slot] += jnp.dot(p.astype(jnp.bfloat16), own_ref[1],
                                 preferred_element_type=jnp.float32)

    for b in range(blocks):
        st_scr[...] = jnp.zeros(st_scr.shape, jnp.float32)
        for h in range(heads):
            slot = b * heads + h
            out_ref[b, :rows, h * HEAD_SIZE:(h + 1) * HEAD_SIZE] = acc_scr[slot]
            st_scr[:, h:h + 1] = m_scr[slot]
            st_scr[:, heads + h:heads + h + 1] = jnp.sum(lpart[slot], axis=1, keepdims=True)
        out_ref[b, rows:, :HEAD_SIZE] = st_scr[...].T[:STAT_ROWS]
        if heads > 1:
            out_ref[b, rows:, HEAD_SIZE:] = jnp.zeros((STAT_ROWS, (heads - 1) * HEAD_SIZE), jnp.float32)


def join_kernel(got_ref, *refs, sources, heads):
    rows = QUERY_GROUP_ROWS
    out_ref = refs[-1]
    cols = [got_ref[s, rows:, :HEAD_SIZE].T for s in range(sources)]
    for h in range(heads):
        ms = [c[:, h:h + 1] for c in cols]
        top = ms[0]
        for m in ms[1:]:
            top = jnp.maximum(top, m)
        top = jnp.where(top == -jnp.inf, 0.0, top)
        total = None
        acc = None
        for s in range(sources):
            fade = jnp.exp2(ms[s] - top)
            part_total = fade * cols[s][:, heads + h:heads + h + 1]
            part_acc = fade * got_ref[s, :rows, h * HEAD_SIZE:(h + 1) * HEAD_SIZE]
            total = part_total if total is None else total + part_total
            acc = part_acc if acc is None else acc + part_acc
        out_ref[:, h * HEAD_SIZE:(h + 1) * HEAD_SIZE] = acc / total


def join(a, b):
    acc_a, m_a, l_a = a
    acc_b, m_b, l_b = b
    m = jnp.maximum(m_a, m_b)
    m_safe = jnp.where(m == -jnp.inf, 0.0, m)
    f_a = jnp.exp2(m_a - m_safe)
    f_b = jnp.exp2(m_b - m_safe)
    acc = acc_a * f_a[..., None] + acc_b * f_b[..., None]
    return acc, m, l_a * f_a + l_b * f_b


def local(queries, query_key_value, cached_key_value, selected):
    rows = queries.shape[0]
    heads = queries.shape[1] // HEAD_SIZE
    head_group = QUERY_HEADS // KEY_VALUE_HEADS
    scale = 1.0 / math.sqrt(HEAD_SIZE)
    groups = lax.axis_size("blk")
    helpers = lax.axis_size("help")
    worker = lax.axis_index("blk")
    helper = lax.axis_index("help")
    piece = cached_key_value.shape[0]
    picks = selected.shape[1] * selected.shape[2]
    assert rows == QUERY_GROUP_ROWS and head_group % heads == 0 and selected.shape[0] == 1
    assert BLOCK_TOKENS % piece == 0 and piece % HEAD_SIZE == 0 and picks % HEAD_SIZE == 0
    per_group = piece * helpers // BLOCK_TOKENS
    query_blocks = helpers

    wanted = tuple((t * heads) // head_group for t in range(groups))
    chunks = piece // HEAD_SIZE
    send = pl.pallas_call(
        functools.partial(relayout_kernel, wanted=wanted, chunks=chunks),
        in_specs=[pl.BlockSpec(memory_space=pltpu.VMEM)],
        out_specs=pl.BlockSpec(memory_space=pltpu.VMEM),
        out_shape=jax.ShapeDtypeStruct((groups, 2, chunks, HEAD_SIZE, HEAD_SIZE), jnp.bfloat16),
    )(cached_key_value)
    held = lax.all_to_all(send, "blk", 0, 0, tiled=True)

    q = jnp.transpose(queries.reshape(rows, heads, HEAD_SIZE), (1, 0, 2)).reshape(heads * rows, HEAD_SIZE)
    sel_rows = selected.reshape(picks // HEAD_SIZE, HEAD_SIZE).astype(jnp.bfloat16)
    sel_pad = -(-(picks // HEAD_SIZE) // 16) * 16
    sel_rows = jnp.pad(sel_rows, ((0, sel_pad - picks // HEAD_SIZE), (0, 0)))
    q = jnp.concatenate([q, sel_rows], axis=0)
    q_all = lax.all_gather(q[None], "help", axis=0, tiled=True)
    sel_all = q_all[:, heads * rows:heads * rows + picks // HEAD_SIZE].astype(jnp.int32).reshape(
        query_blocks, selected.shape[1], selected.shape[2])

    kv_head = (worker * heads) // head_group
    own = query_key_value.reshape(rows, 2, KEY_VALUE_HEADS, HEAD_SIZE)
    own = lax.dynamic_index_in_dim(own, kv_head, axis=2, keepdims=False)
    own = jnp.stack([own[:, 0].T, own[:, 1]])

    my_heads = lax.dynamic_slice_in_dim(sel_all, worker * heads, heads, axis=1)
    piece_block = per_group * jnp.arange(groups, dtype=jnp.int32) + (helper * piece) // BLOCK_TOKENS
    hit = jnp.any(my_heads[:, :, None, :] == piece_block[None, None, :, None], axis=3)
    sel_flat = hit.astype(jnp.int32).reshape(-1)
    home = helper.reshape(1).astype(jnp.int32)

    slices = min(2, heads)
    part = heads // slices
    assert part * slices == heads and 2 * part <= STAT_ROWS
    width = part * HEAD_SIZE
    result = None
    for c in range(slices):
        kernel = functools.partial(attend_kernel, groups=groups, heads=part, first=c * part,
                                   all_heads=heads, blocks=query_blocks, chunks=chunks,
                                   factor=scale * math.log2(math.e))
        slots = query_blocks * part
        partial = pl.pallas_call(
            kernel,
            grid_spec=pltpu.PrefetchScalarGridSpec(
                num_scalar_prefetch=2,
                grid=(1,),
                in_specs=[
                    pl.BlockSpec((query_blocks, part * rows, HEAD_SIZE),
                                 lambda i, s, h, c=c: (0, c, 0)),
                    pl.BlockSpec((groups, 2, chunks, HEAD_SIZE, HEAD_SIZE),
                                 lambda i, s, h: (0, 0, 0, 0, 0)),
                    pl.BlockSpec((2, rows, HEAD_SIZE), lambda i, s, h: (0, 0, 0)),
                ],
                out_specs=pl.BlockSpec((query_blocks, rows + STAT_ROWS, width),
                                       lambda i, s, h: (0, 0, 0)),
                scratch_shapes=[
                    pltpu.VMEM((groups, slots * rows, piece), jnp.float32),
                    pltpu.VMEM((part, rows, rows), jnp.float32),
                    pltpu.VMEM((slots * rows, piece), jnp.bfloat16),
                    pltpu.VMEM((slots, rows, HEAD_SIZE), jnp.float32),
                    pltpu.VMEM((slots, rows, HEAD_SIZE), jnp.float32),
                    pltpu.VMEM((slots, rows, 1), jnp.float32),
                    pltpu.VMEM((slots, rows, HEAD_SIZE), jnp.float32),
                    pltpu.VMEM((rows, HEAD_SIZE), jnp.float32),
                ],
            ),
            compiler_params=pltpu.CompilerParams(vmem_limit_bytes=48 * 1024 * 1024),
            out_shape=jax.ShapeDtypeStruct((query_blocks, rows + STAT_ROWS, width), jnp.float32),
            cost_estimate=pl.CostEstimate(
                flops=4 * query_blocks * part * rows * groups * piece * HEAD_SIZE,
                transcendentals=query_blocks * part * rows * groups * piece,
                bytes_accessed=2 * groups * 2 * piece * HEAD_SIZE + 4 * query_blocks * rows * width),
        )(sel_flat, home, q_all, held, own)
        got = lax.all_to_all(partial, "help", 0, 0, tiled=True)
        first_join = c == 0
        result = pl.pallas_call(
            functools.partial(join_kernel, sources=helpers, heads=part),
            grid=(1,),
            in_specs=[pl.BlockSpec((helpers, rows + STAT_ROWS, width), lambda i: (0, 0, 0))]
            + ([] if first_join else [pl.BlockSpec(memory_space=pl.ANY)]),
            out_specs=pl.BlockSpec((rows, width), lambda i, c=c: (0, c)),
            out_shape=jax.ShapeDtypeStruct((rows, heads * HEAD_SIZE), jnp.float32),
            input_output_aliases={} if first_join else {1: 0},
        )(*((got,) if first_join else (got, result)))
    return result


def solution(mesh):
    in_specs = (P("help", "blk"), P("help", None), P(("blk", "help"), None), P("help", None, None))
    out_specs = P("help", "blk")
    return jax.shard_map(local, mesh=mesh, in_specs=in_specs, out_specs=out_specs, check_vma=False)
```

```python
import functools
import math

import jax
import jax.numpy as jnp
import numpy as np
from jax import lax
from jax.experimental import pallas as pl
from jax.experimental.pallas import tpu as pltpu
from jax.sharding import PartitionSpec as P

HEAD_SIZE = 128
QUERY_HEADS = 64
KEY_VALUE_HEADS = 8
BLOCK_TOKENS = 1024
QUERY_GROUP_ROWS = 128
STAT_ROWS = 8


def relayout_kernel(x_ref, out_ref, *, wanted, chunks):
    for t, kv_head in enumerate(wanted):
        for c in range(chunks):
            tokens = slice(c * HEAD_SIZE, (c + 1) * HEAD_SIZE)
            keys = x_ref[tokens, kv_head * HEAD_SIZE:(kv_head + 1) * HEAD_SIZE]
            out_ref[t, 0, c] = keys.astype(jnp.float32).T.astype(jnp.bfloat16)
            column = (KEY_VALUE_HEADS + kv_head) * HEAD_SIZE
            out_ref[t, 1, c] = x_ref[tokens, column:column + HEAD_SIZE]


def attend_kernel(sel_ref, home_ref, q_ref, kv_ref, own_ref, out_ref,
                  s_buf, own_buf, p_buf, mpart, lpart, m_scr, acc_scr, st_scr,
                  *, groups, heads, first, all_heads, blocks, chunks, factor, mode):
    rows = QUERY_GROUP_ROWS
    slots = blocks * heads
    lanes = HEAD_SIZE
    q = q_ref[...].reshape(slots * rows, HEAD_SIZE)
    home = home_ref[0]
    mpart[...] = jnp.full(mpart.shape, -jnp.inf, jnp.float32)
    lpart[...] = jnp.zeros(lpart.shape, jnp.float32)
    acc_scr[...] = jnp.zeros(acc_scr.shape, jnp.float32)

    def on(slot, g):
        b, h = divmod(slot, heads)
        if mode == "home":
            b = home
        hit = sel_ref[(b * all_heads + first + h) * groups + g] != 0
        if mode == "remote":
            hit = jnp.logical_and(hit, b != home)
        return hit

    def fold(x, op):
        out = x[:, :lanes]
        for c in range(1, x.shape[1] // lanes):
            out = op(out, x[:, c * lanes:(c + 1) * lanes])
        return out

    def score(g, carry):
        for c in range(chunks):
            s_buf[g, :, c * HEAD_SIZE:(c + 1) * HEAD_SIZE] = jnp.dot(
                q, kv_ref[g, 0, c], preferred_element_type=jnp.float32)
        for slot in range(slots):
            @pl.when(on(slot, g))
            def _():
                mpart[slot] = jnp.maximum(
                    mpart[slot], fold(s_buf[g, slot * rows:(slot + 1) * rows], jnp.maximum))
        return carry

    lax.fori_loop(0, groups, score, 0)

    home_block = 0 if mode == "home" else home
    causal = lax.broadcasted_iota(jnp.int32, (rows, rows), 0) >= lax.broadcasted_iota(
        jnp.int32, (rows, rows), 1)
    if mode != "remote":
        s_own = jnp.dot(q_ref[home_block], own_ref[0], preferred_element_type=jnp.float32)
        for h in range(heads):
            s_h = jnp.where(causal, s_own[h * rows:(h + 1) * rows], -jnp.inf)
            own_buf[h] = s_h
            slot = home_block * heads + h
            mpart[slot] = jnp.maximum(mpart[slot], fold(s_h, jnp.maximum))

    for slot in range(slots):
        m = jnp.max(mpart[slot], axis=1, keepdims=True) * factor
        m_scr[slot] = m
        mpart[slot] = jnp.broadcast_to(jnp.where(m == -jnp.inf, 0.0, m), (rows, lanes))

    def mix(g, carry):
        ons = [on(slot, g) for slot in range(slots)]
        for slot in range(slots):
            @pl.when(ons[slot])
            def _():
                p = jnp.exp2(s_buf[g, slot * rows:(slot + 1) * rows] * factor - mpart[slot][:, :1])
                lpart[slot] += fold(p, jnp.add)
                p_buf[slot * rows:(slot + 1) * rows] = p.astype(jnp.bfloat16)

        value = kv_ref[g, 1].reshape(chunks * HEAD_SIZE, HEAD_SIZE)
        pv = jnp.dot(p_buf[...], value, preferred_element_type=jnp.float32)
        for slot in range(slots):
            @pl.when(ons[slot])
            def _():
                acc_scr[slot] += pv[slot * rows:(slot + 1) * rows]
        return carry

    lax.fori_loop(0, groups, mix, 0)

    for h in range(heads if mode != "remote" else 0):
        slot = home_block * heads + h
        p = jnp.exp2(own_buf[h] * factor - mpart[slot][:, :1])
        lpart[slot] += p
        acc_scr[slot] += jnp.dot(p.astype(jnp.bfloat16), own_ref[1],
                                 preferred_element_type=jnp.float32)

    for b in range(blocks):
        st_scr[...] = jnp.zeros(st_scr.shape, jnp.float32)
        for h in range(heads):
            slot = b * heads + h
            out_ref[b, :rows, h * HEAD_SIZE:(h + 1) * HEAD_SIZE] = acc_scr[slot]
            st_scr[:, h:h + 1] = m_scr[slot]
            st_scr[:, heads + h:heads + h + 1] = jnp.sum(lpart[slot], axis=1, keepdims=True)
        out_ref[b, rows:, :HEAD_SIZE] = st_scr[...].T[:STAT_ROWS]
        if heads > 1:
            out_ref[b, rows:, HEAD_SIZE:] = jnp.zeros((STAT_ROWS, (heads - 1) * HEAD_SIZE), jnp.float32)


def join_kernel(got_ref, *refs, sources, heads, extra):
    rows = QUERY_GROUP_ROWS
    out_ref = refs[-1]
    blocks = [(got_ref, s) for s in range(sources)] + ([(refs[0], 0)] if extra else [])
    cols = [ref[s, rows:, :HEAD_SIZE].T for ref, s in blocks]
    for h in range(heads):
        ms = [c[:, h:h + 1] for c in cols]
        top = ms[0]
        for m in ms[1:]:
            top = jnp.maximum(top, m)
        top = jnp.where(top == -jnp.inf, 0.0, top)
        total = None
        acc = None
        for (ref, s), col, m in zip(blocks, cols, ms):
            fade = jnp.exp2(m - top)
            part_total = fade * col[:, heads + h:heads + h + 1]
            part_acc = fade * ref[s, :rows, h * HEAD_SIZE:(h + 1) * HEAD_SIZE]
            total = part_total if total is None else total + part_total
            acc = part_acc if acc is None else acc + part_acc
        out_ref[:, h * HEAD_SIZE:(h + 1) * HEAD_SIZE] = acc / total


def join(a, b):
    acc_a, m_a, l_a = a
    acc_b, m_b, l_b = b
    m = jnp.maximum(m_a, m_b)
    m_safe = jnp.where(m == -jnp.inf, 0.0, m)
    f_a = jnp.exp2(m_a - m_safe)
    f_b = jnp.exp2(m_b - m_safe)
    acc = acc_a * f_a[..., None] + acc_b * f_b[..., None]
    return acc, m, l_a * f_a + l_b * f_b


def local(queries, query_key_value, cached_key_value, selected):
    rows = queries.shape[0]
    heads = queries.shape[1] // HEAD_SIZE
    head_group = QUERY_HEADS // KEY_VALUE_HEADS
    scale = 1.0 / math.sqrt(HEAD_SIZE)
    groups = lax.axis_size("blk")
    helpers = lax.axis_size("help")
    worker = lax.axis_index("blk")
    helper = lax.axis_index("help")
    piece = cached_key_value.shape[0]
    picks = selected.shape[1] * selected.shape[2]
    assert rows == QUERY_GROUP_ROWS and head_group % heads == 0 and selected.shape[0] == 1
    assert BLOCK_TOKENS % piece == 0 and piece % HEAD_SIZE == 0 and picks % HEAD_SIZE == 0
    per_group = piece * helpers // BLOCK_TOKENS
    query_blocks = helpers

    wanted = tuple((t * heads) // head_group for t in range(groups))
    chunks = piece // HEAD_SIZE
    send = pl.pallas_call(
        functools.partial(relayout_kernel, wanted=wanted, chunks=chunks),
        in_specs=[pl.BlockSpec(memory_space=pltpu.VMEM)],
        out_specs=pl.BlockSpec(memory_space=pltpu.VMEM),
        out_shape=jax.ShapeDtypeStruct((groups, 2, chunks, HEAD_SIZE, HEAD_SIZE), jnp.bfloat16),
    )(cached_key_value)
    held = lax.all_to_all(send, "blk", 0, 0, tiled=True)

    q = jnp.transpose(queries.reshape(rows, heads, HEAD_SIZE), (1, 0, 2)).reshape(heads * rows, HEAD_SIZE)
    sel_rows = selected.reshape(picks // HEAD_SIZE, HEAD_SIZE).astype(jnp.bfloat16)
    sel_pad = -(-(picks // HEAD_SIZE) // 16) * 16
    sel_rows = jnp.pad(sel_rows, ((0, sel_pad - picks // HEAD_SIZE), (0, 0)))
    q = jnp.concatenate([q, sel_rows], axis=0)
    q_all = lax.all_gather(q[None], "help", axis=0, tiled=True)
    sel_all = q_all[:, heads * rows:heads * rows + picks // HEAD_SIZE].astype(jnp.int32).reshape(
        query_blocks, selected.shape[1], selected.shape[2])

    kv_head = (worker * heads) // head_group
    own = query_key_value.reshape(rows, 2, KEY_VALUE_HEADS, HEAD_SIZE)
    own = lax.dynamic_index_in_dim(own, kv_head, axis=2, keepdims=False)
    own = jnp.stack([own[:, 0].T, own[:, 1]])

    my_heads = lax.dynamic_slice_in_dim(sel_all, worker * heads, heads, axis=1)
    piece_block = per_group * jnp.arange(groups, dtype=jnp.int32) + (helper * piece) // BLOCK_TOKENS
    hit = jnp.any(my_heads[:, :, None, :] == piece_block[None, None, :, None], axis=3)
    sel_flat = hit.astype(jnp.int32).reshape(-1)
    home = helper.reshape(1).astype(jnp.int32)

    slices = min(2, heads)
    part = heads // slices
    assert part * slices == heads and 2 * part <= STAT_ROWS
    width = part * HEAD_SIZE
    result = None

    def attend_call(c, mode):
        blocks = 1 if mode == "home" else query_blocks
        slots = blocks * part
        kernel = functools.partial(attend_kernel, groups=groups, heads=part, first=c * part,
                                   all_heads=heads, blocks=blocks, chunks=chunks,
                                   factor=scale * math.log2(math.e), mode=mode)
        if mode == "home":
            q_spec = pl.BlockSpec((1, part * rows, HEAD_SIZE), lambda i, s, h, c=c: (h[0], c, 0))
        else:
            q_spec = pl.BlockSpec((query_blocks, part * rows, HEAD_SIZE), lambda i, s, h, c=c: (0, c, 0))
        return pl.pallas_call(
            kernel,
            grid_spec=pltpu.PrefetchScalarGridSpec(
                num_scalar_prefetch=2,
                grid=(1,),
                in_specs=[
                    q_spec,
                    pl.BlockSpec((groups, 2, chunks, HEAD_SIZE, HEAD_SIZE),
                                 lambda i, s, h: (0, 0, 0, 0, 0)),
                    pl.BlockSpec((2, rows, HEAD_SIZE), lambda i, s, h: (0, 0, 0)),
                ],
                out_specs=pl.BlockSpec((blocks, rows + STAT_ROWS, width), lambda i, s, h: (0, 0, 0)),
                scratch_shapes=[
                    pltpu.VMEM((groups, slots * rows, piece), jnp.float32),
                    pltpu.VMEM((part, rows, rows), jnp.float32),
                    pltpu.VMEM((slots * rows, piece), jnp.bfloat16),
                    pltpu.VMEM((slots, rows, HEAD_SIZE), jnp.float32),
                    pltpu.VMEM((slots, rows, HEAD_SIZE), jnp.float32),
                    pltpu.VMEM((slots, rows, 1), jnp.float32),
                    pltpu.VMEM((slots, rows, HEAD_SIZE), jnp.float32),
                    pltpu.VMEM((rows, HEAD_SIZE), jnp.float32),
                ],
            ),
            compiler_params=pltpu.CompilerParams(vmem_limit_bytes=48 * 1024 * 1024),
            out_shape=jax.ShapeDtypeStruct((blocks, rows + STAT_ROWS, width), jnp.float32),
            cost_estimate=pl.CostEstimate(
                flops=4 * blocks * part * rows * groups * piece * HEAD_SIZE,
                transcendentals=blocks * part * rows * groups * piece,
                bytes_accessed=2 * groups * 2 * piece * HEAD_SIZE + 4 * blocks * rows * width),
        )(sel_flat, home, q_all, held, own)

    for c in range(slices):
        last = c == slices - 1
        partial = attend_call(c, "remote" if last else "all")
        got = lax.all_to_all(partial, "help", 0, 0, tiled=True)
        extra = [attend_call(c, "home")] if last else []
        first_join = c == 0
        result = pl.pallas_call(
            functools.partial(join_kernel, sources=helpers, heads=part, extra=last),
            grid=(1,),
            in_specs=[pl.BlockSpec((helpers, rows + STAT_ROWS, width), lambda i: (0, 0, 0))]
            + [pl.BlockSpec((1, rows + STAT_ROWS, width), lambda i: (0, 0, 0))] * len(extra)
            + ([] if first_join else [pl.BlockSpec(memory_space=pl.ANY)]),
            out_specs=pl.BlockSpec((rows, width), lambda i, c=c: (0, c)),
            out_shape=jax.ShapeDtypeStruct((rows, heads * HEAD_SIZE), jnp.float32),
            input_output_aliases={} if first_join else {1 + len(extra): 0},
        )(got, *extra, *(() if first_join else (result,)))
    return result


def solution(mesh):
    in_specs = (P("help", "blk"), P("help", None), P(("blk", "help"), None), P("help", None, None))
    out_specs = P("help", "blk")
    return jax.shard_map(local, mesh=mesh, in_specs=in_specs, out_specs=out_specs, check_vma=False)
```

```python
import functools
import math

import jax
import jax.numpy as jnp
import numpy as np
from jax import lax
from jax.experimental import pallas as pl
from jax.experimental.pallas import tpu as pltpu
from jax.sharding import PartitionSpec as P

HEAD_SIZE = 128
QUERY_HEADS = 64
KEY_VALUE_HEADS = 8
BLOCK_TOKENS = 1024
QUERY_GROUP_ROWS = 128
STAT_ROWS = 8


def relayout_kernel(x_ref, out_ref, *, wanted, chunks):
    for t, kv_head in enumerate(wanted):
        for c in range(chunks):
            tokens = slice(c * HEAD_SIZE, (c + 1) * HEAD_SIZE)
            keys = x_ref[tokens, kv_head * HEAD_SIZE:(kv_head + 1) * HEAD_SIZE]
            out_ref[t, 0, c] = keys.astype(jnp.float32).T.astype(jnp.bfloat16)
            column = (KEY_VALUE_HEADS + kv_head) * HEAD_SIZE
            out_ref[t, 1, c] = x_ref[tokens, column:column + HEAD_SIZE]


def attend_kernel(sel_ref, home_ref, q_ref, kv_ref, own_ref, out_ref,
                  s_buf, own_buf, p_buf, mpart, lpart, m_scr, acc_scr, st_scr,
                  *, groups, heads, first, all_heads, blocks, chunks, factor):
    rows = QUERY_GROUP_ROWS
    slots = blocks * heads
    lanes = HEAD_SIZE
    q = jnp.concatenate([q_ref[b, :, h * HEAD_SIZE:(h + 1) * HEAD_SIZE]
                         for b in range(blocks) for h in range(heads)], axis=0)
    home = home_ref[0]
    mpart[...] = jnp.full(mpart.shape, -jnp.inf, jnp.float32)
    lpart[...] = jnp.zeros(lpart.shape, jnp.float32)
    acc_scr[...] = jnp.zeros(acc_scr.shape, jnp.float32)

    def on(slot, g):
        b, h = divmod(slot, heads)
        return sel_ref[(b * all_heads + first + h) * groups + g] != 0

    def fold(x, op):
        out = x[:, :lanes]
        for c in range(1, x.shape[1] // lanes):
            out = op(out, x[:, c * lanes:(c + 1) * lanes])
        return out

    def score(g, carry):
        for c in range(chunks):
            s_buf[g, :, c * HEAD_SIZE:(c + 1) * HEAD_SIZE] = jnp.dot(
                q, kv_ref[g, 0, c], preferred_element_type=jnp.float32)
        for slot in range(slots):
            @pl.when(on(slot, g))
            def _():
                mpart[slot] = jnp.maximum(
                    mpart[slot], fold(s_buf[g, slot * rows:(slot + 1) * rows], jnp.maximum))
        return carry

    lax.fori_loop(0, groups, score, 0)

    causal = lax.broadcasted_iota(jnp.int32, (rows, rows), 0) >= lax.broadcasted_iota(
        jnp.int32, (rows, rows), 1)
    q_home = q_ref[home]
    s_own = jnp.dot(jnp.concatenate([q_home[:, h * HEAD_SIZE:(h + 1) * HEAD_SIZE]
                                     for h in range(heads)], axis=0),
                    own_ref[0], preferred_element_type=jnp.float32)
    for h in range(heads):
        s_h = jnp.where(causal, s_own[h * rows:(h + 1) * rows], -jnp.inf)
        own_buf[h] = s_h
        slot = home * heads + h
        mpart[slot] = jnp.maximum(mpart[slot], fold(s_h, jnp.maximum))

    for slot in range(slots):
        m = jnp.max(mpart[slot], axis=1, keepdims=True) * factor
        m_scr[slot] = m
        mpart[slot] = jnp.broadcast_to(jnp.where(m == -jnp.inf, 0.0, m), (rows, lanes))

    def mix(g, carry):
        ons = [on(slot, g) for slot in range(slots)]
        for slot in range(slots):
            @pl.when(ons[slot])
            def _():
                p = jnp.exp2(s_buf[g, slot * rows:(slot + 1) * rows] * factor - mpart[slot][:, :1])
                lpart[slot] += fold(p, jnp.add)
                p_buf[slot * rows:(slot + 1) * rows] = p.astype(jnp.bfloat16)

        value = kv_ref[g, 1].reshape(chunks * HEAD_SIZE, HEAD_SIZE)
        pv = jnp.dot(p_buf[...], value, preferred_element_type=jnp.float32)
        for slot in range(slots):
            @pl.when(ons[slot])
            def _():
                acc_scr[slot] += pv[slot * rows:(slot + 1) * rows]
        return carry

    lax.fori_loop(0, groups, mix, 0)

    for h in range(heads):
        slot = home * heads + h
        p = jnp.exp2(own_buf[h] * factor - mpart[slot][:, :1])
        lpart[slot] += p
        acc_scr[slot] += jnp.dot(p.astype(jnp.bfloat16), own_ref[1],
                                 preferred_element_type=jnp.float32)

    for b in range(blocks):
        st_scr[...] = jnp.zeros(st_scr.shape, jnp.float32)
        for h in range(heads):
            slot = b * heads + h
            out_ref[b, :rows, h * HEAD_SIZE:(h + 1) * HEAD_SIZE] = acc_scr[slot]
            st_scr[:, h:h + 1] = m_scr[slot]
            st_scr[:, heads + h:heads + h + 1] = jnp.sum(lpart[slot], axis=1, keepdims=True)
        out_ref[b, rows:, :HEAD_SIZE] = st_scr[...].T[:STAT_ROWS]
        if heads > 1:
            out_ref[b, rows:, HEAD_SIZE:] = jnp.zeros((STAT_ROWS, (heads - 1) * HEAD_SIZE), jnp.float32)


def join_kernel(got_ref, *refs, sources, heads):
    rows = QUERY_GROUP_ROWS
    out_ref = refs[-1]
    cols = [got_ref[s, rows:, :HEAD_SIZE].T for s in range(sources)]
    for h in range(heads):
        ms = [c[:, h:h + 1] for c in cols]
        top = ms[0]
        for m in ms[1:]:
            top = jnp.maximum(top, m)
        top = jnp.where(top == -jnp.inf, 0.0, top)
        total = None
        acc = None
        for s in range(sources):
            fade = jnp.exp2(ms[s] - top)
            part_total = fade * cols[s][:, heads + h:heads + h + 1]
            part_acc = fade * got_ref[s, :rows, h * HEAD_SIZE:(h + 1) * HEAD_SIZE]
            total = part_total if total is None else total + part_total
            acc = part_acc if acc is None else acc + part_acc
        out_ref[:, h * HEAD_SIZE:(h + 1) * HEAD_SIZE] = acc / total


def join(a, b):
    acc_a, m_a, l_a = a
    acc_b, m_b, l_b = b
    m = jnp.maximum(m_a, m_b)
    m_safe = jnp.where(m == -jnp.inf, 0.0, m)
    f_a = jnp.exp2(m_a - m_safe)
    f_b = jnp.exp2(m_b - m_safe)
    acc = acc_a * f_a[..., None] + acc_b * f_b[..., None]
    return acc, m, l_a * f_a + l_b * f_b


def local(queries, query_key_value, cached_key_value, selected):
    rows = queries.shape[0]
    heads = queries.shape[1] // HEAD_SIZE
    head_group = QUERY_HEADS // KEY_VALUE_HEADS
    scale = 1.0 / math.sqrt(HEAD_SIZE)
    groups = lax.axis_size("blk")
    helpers = lax.axis_size("help")
    worker = lax.axis_index("blk")
    helper = lax.axis_index("help")
    piece = cached_key_value.shape[0]
    picks = selected.shape[1] * selected.shape[2]
    assert rows == QUERY_GROUP_ROWS and head_group % heads == 0 and selected.shape[0] == 1
    assert BLOCK_TOKENS % piece == 0 and piece % HEAD_SIZE == 0 and picks % HEAD_SIZE == 0
    per_group = piece * helpers // BLOCK_TOKENS
    query_blocks = helpers

    wanted = tuple((t * heads) // head_group for t in range(groups))
    chunks = piece // HEAD_SIZE
    send = pl.pallas_call(
        functools.partial(relayout_kernel, wanted=wanted, chunks=chunks),
        in_specs=[pl.BlockSpec(memory_space=pltpu.VMEM)],
        out_specs=pl.BlockSpec(memory_space=pltpu.VMEM),
        out_shape=jax.ShapeDtypeStruct((groups, 2, chunks, HEAD_SIZE, HEAD_SIZE), jnp.bfloat16),
    )(cached_key_value)
    held = lax.all_to_all(send, "blk", 0, 0, tiled=True)

    full_width = heads * HEAD_SIZE
    assert picks <= full_width
    sel_rows = jnp.pad(selected.reshape(1, picks).astype(jnp.bfloat16),
                       ((0, 15), (0, full_width - picks)))
    q = jnp.concatenate([queries, sel_rows], axis=0)
    q_all = lax.all_gather(q[None], "help", axis=0, tiled=True)
    sel_all = q_all[:, rows, :picks].astype(jnp.int32).reshape(
        query_blocks, selected.shape[1], selected.shape[2])

    kv_head = (worker * heads) // head_group
    own = query_key_value.reshape(rows, 2, KEY_VALUE_HEADS, HEAD_SIZE)
    own = lax.dynamic_index_in_dim(own, kv_head, axis=2, keepdims=False)
    own = jnp.stack([own[:, 0].T, own[:, 1]])

    my_heads = lax.dynamic_slice_in_dim(sel_all, worker * heads, heads, axis=1)
    piece_block = per_group * jnp.arange(groups, dtype=jnp.int32) + (helper * piece) // BLOCK_TOKENS
    hit = jnp.any(my_heads[:, :, None, :] == piece_block[None, None, :, None], axis=3)
    sel_flat = hit.astype(jnp.int32).reshape(-1)
    home = helper.reshape(1).astype(jnp.int32)

    slices = min(2, heads)
    part = heads // slices
    assert part * slices == heads and 2 * part <= STAT_ROWS
    width = part * HEAD_SIZE
    result = None
    for c in range(slices):
        kernel = functools.partial(attend_kernel, groups=groups, heads=part, first=c * part,
                                   all_heads=heads, blocks=query_blocks, chunks=chunks,
                                   factor=scale * math.log2(math.e))
        slots = query_blocks * part
        partial = pl.pallas_call(
            kernel,
            grid_spec=pltpu.PrefetchScalarGridSpec(
                num_scalar_prefetch=2,
                grid=(1,),
                in_specs=[
                    pl.BlockSpec((query_blocks, rows, part * HEAD_SIZE),
                                 lambda i, s, h, c=c: (0, 0, c)),
                    pl.BlockSpec((groups, 2, chunks, HEAD_SIZE, HEAD_SIZE),
                                 lambda i, s, h: (0, 0, 0, 0, 0)),
                    pl.BlockSpec((2, rows, HEAD_SIZE), lambda i, s, h: (0, 0, 0)),
                ],
                out_specs=pl.BlockSpec((query_blocks, rows + STAT_ROWS, width),
                                       lambda i, s, h: (0, 0, 0)),
                scratch_shapes=[
                    pltpu.VMEM((groups, slots * rows, piece), jnp.float32),
                    pltpu.VMEM((part, rows, rows), jnp.float32),
                    pltpu.VMEM((slots * rows, piece), jnp.bfloat16),
                    pltpu.VMEM((slots, rows, HEAD_SIZE), jnp.float32),
                    pltpu.VMEM((slots, rows, HEAD_SIZE), jnp.float32),
                    pltpu.VMEM((slots, rows, 1), jnp.float32),
                    pltpu.VMEM((slots, rows, HEAD_SIZE), jnp.float32),
                    pltpu.VMEM((rows, HEAD_SIZE), jnp.float32),
                ],
            ),
            compiler_params=pltpu.CompilerParams(vmem_limit_bytes=48 * 1024 * 1024),
            out_shape=jax.ShapeDtypeStruct((query_blocks, rows + STAT_ROWS, width), jnp.float32),
            cost_estimate=pl.CostEstimate(
                flops=4 * query_blocks * part * rows * groups * piece * HEAD_SIZE,
                transcendentals=query_blocks * part * rows * groups * piece,
                bytes_accessed=2 * groups * 2 * piece * HEAD_SIZE + 4 * query_blocks * rows * width),
        )(sel_flat, home, q_all, held, own)
        got = lax.all_to_all(partial, "help", 0, 0, tiled=True)
        first_join = c == 0
        result = pl.pallas_call(
            functools.partial(join_kernel, sources=helpers, heads=part),
            grid=(1,),
            in_specs=[pl.BlockSpec((helpers, rows + STAT_ROWS, width), lambda i: (0, 0, 0))]
            + ([] if first_join else [pl.BlockSpec(memory_space=pl.ANY)]),
            out_specs=pl.BlockSpec((rows, width), lambda i, c=c: (0, c)),
            out_shape=jax.ShapeDtypeStruct((rows, heads * HEAD_SIZE), jnp.float32),
            input_output_aliases={} if first_join else {1: 0},
        )(*((got,) if first_join else (got, result)))
    return result


def solution(mesh):
    in_specs = (P("help", "blk"), P("help", None), P(("blk", "help"), None), P("help", None, None))
    out_specs = P("help", "blk")
    return jax.shard_map(local, mesh=mesh, in_specs=in_specs, out_specs=out_specs, check_vma=False)
```

```python
import functools
import math

import jax
import jax.numpy as jnp
import numpy as np
from jax import lax
from jax.experimental import pallas as pl
from jax.experimental.pallas import tpu as pltpu
from jax.sharding import PartitionSpec as P

HEAD_SIZE = 128
QUERY_HEADS = 64
KEY_VALUE_HEADS = 8
BLOCK_TOKENS = 1024
QUERY_GROUP_ROWS = 128
STAT_ROWS = 8


def relayout_kernel(x_ref, out_ref, *, wanted, chunks):
    for t, kv_head in enumerate(wanted):
        for c in range(chunks):
            tokens = slice(c * HEAD_SIZE, (c + 1) * HEAD_SIZE)
            keys = x_ref[tokens, kv_head * HEAD_SIZE:(kv_head + 1) * HEAD_SIZE]
            out_ref[t, 0, c] = keys.astype(jnp.float32).T.astype(jnp.bfloat16)
            column = (KEY_VALUE_HEADS + kv_head) * HEAD_SIZE
            out_ref[t, 1, c] = x_ref[tokens, column:column + HEAD_SIZE]


def attend_kernel(sel_ref, home_ref, q_ref, kv_ref, own_ref, out_ref,
                  s_buf, own_buf, p_buf, mpart, lpart, m_scr, acc_scr, st_scr,
                  *, groups, heads, first, all_heads, blocks, chunks, factor):
    rows = QUERY_GROUP_ROWS
    slots = blocks * heads
    lanes = HEAD_SIZE
    q = q_ref[...].reshape(slots * rows, HEAD_SIZE)
    home = home_ref[0]
    mpart[...] = jnp.full(mpart.shape, -jnp.inf, jnp.float32)
    lpart[...] = jnp.zeros(lpart.shape, jnp.float32)
    acc_scr[...] = jnp.zeros(acc_scr.shape, jnp.float32)

    def on(slot, g):
        b, h = divmod(slot, heads)
        return sel_ref[(b * all_heads + first + h) * groups + g] != 0

    def fold(x, op):
        out = x[:, :lanes]
        for c in range(1, x.shape[1] // lanes):
            out = op(out, x[:, c * lanes:(c + 1) * lanes])
        return out

    def score(g, carry):
        for c in range(chunks):
            s_buf[g, :, c * HEAD_SIZE:(c + 1) * HEAD_SIZE] = jnp.dot(
                q, kv_ref[g, 0, c], preferred_element_type=jnp.float32)
        for slot in range(slots):
            @pl.when(on(slot, g))
            def _():
                mpart[slot] = jnp.maximum(
                    mpart[slot], fold(s_buf[g, slot * rows:(slot + 1) * rows], jnp.maximum))
        return carry

    lax.fori_loop(0, groups, score, 0)

    causal = lax.broadcasted_iota(jnp.int32, (rows, rows), 0) >= lax.broadcasted_iota(
        jnp.int32, (rows, rows), 1)
    s_own = jnp.dot(q_ref[home], own_ref[0],
                    preferred_element_type=jnp.float32)
    for h in range(heads):
        s_h = jnp.where(causal, s_own[h * rows:(h + 1) * rows], -jnp.inf)
        own_buf[h] = s_h
        slot = home * heads + h
        mpart[slot] = jnp.maximum(mpart[slot], fold(s_h, jnp.maximum))

    for slot in range(slots):
        m = jnp.max(mpart[slot], axis=1, keepdims=True) * factor
        m_scr[slot] = m
        mpart[slot] = jnp.broadcast_to(jnp.where(m == -jnp.inf, 0.0, m), (rows, lanes))

    def mix(g, carry):
        ons = [on(slot, g) for slot in range(slots)]
        for slot in range(slots):
            @pl.when(ons[slot])
            def _():
                p = jnp.exp2(s_buf[g, slot * rows:(slot + 1) * rows] * factor - mpart[slot][:, :1])
                lpart[slot] += fold(p, jnp.add)
                p_buf[slot * rows:(slot + 1) * rows] = p.astype(jnp.bfloat16)

        value = kv_ref[g, 1].reshape(chunks * HEAD_SIZE, HEAD_SIZE)
        pv = jnp.dot(p_buf[...], value, preferred_element_type=jnp.float32)
        for slot in range(slots):
            @pl.when(ons[slot])
            def _():
                acc_scr[slot] += pv[slot * rows:(slot + 1) * rows]
        return carry

    lax.fori_loop(0, groups, mix, 0)

    for h in range(heads):
        slot = home * heads + h
        p = jnp.exp2(own_buf[h] * factor - mpart[slot][:, :1])
        lpart[slot] += p
        acc_scr[slot] += jnp.dot(p.astype(jnp.bfloat16), own_ref[1],
                                 preferred_element_type=jnp.float32)

    for b in range(blocks):
        st_scr[...] = jnp.zeros(st_scr.shape, jnp.float32)
        for h in range(heads):
            slot = b * heads + h
            out_ref[b, :rows, h * HEAD_SIZE:(h + 1) * HEAD_SIZE] = acc_scr[slot]
            st_scr[:, h:h + 1] = m_scr[slot]
            st_scr[:, heads + h:heads + h + 1] = jnp.sum(lpart[slot], axis=1, keepdims=True)
        out_ref[b, rows:, :HEAD_SIZE] = st_scr[...].T[:STAT_ROWS]
        if heads > 1:
            out_ref[b, rows:, HEAD_SIZE:] = jnp.zeros((STAT_ROWS, (heads - 1) * HEAD_SIZE), jnp.float32)


def join_kernel(got_ref, *refs, sources, heads):
    rows = QUERY_GROUP_ROWS
    out_ref = refs[-1]
    cols = [got_ref[s, rows:, :HEAD_SIZE].T for s in range(sources)]
    for h in range(heads):
        ms = [c[:, h:h + 1] for c in cols]
        top = ms[0]
        for m in ms[1:]:
            top = jnp.maximum(top, m)
        top = jnp.where(top == -jnp.inf, 0.0, top)
        total = None
        acc = None
        for s in range(sources):
            fade = jnp.exp2(ms[s] - top)
            part_total = fade * cols[s][:, heads + h:heads + h + 1]
            part_acc = fade * got_ref[s, :rows, h * HEAD_SIZE:(h + 1) * HEAD_SIZE]
            total = part_total if total is None else total + part_total
            acc = part_acc if acc is None else acc + part_acc
        out_ref[:, h * HEAD_SIZE:(h + 1) * HEAD_SIZE] = acc / total


def join(a, b):
    acc_a, m_a, l_a = a
    acc_b, m_b, l_b = b
    m = jnp.maximum(m_a, m_b)
    m_safe = jnp.where(m == -jnp.inf, 0.0, m)
    f_a = jnp.exp2(m_a - m_safe)
    f_b = jnp.exp2(m_b - m_safe)
    acc = acc_a * f_a[..., None] + acc_b * f_b[..., None]
    return acc, m, l_a * f_a + l_b * f_b


def local(queries, query_key_value, cached_key_value, selected):
    rows = queries.shape[0]
    heads = queries.shape[1] // HEAD_SIZE
    head_group = QUERY_HEADS // KEY_VALUE_HEADS
    scale = 1.0 / math.sqrt(HEAD_SIZE)
    groups = lax.axis_size("blk")
    helpers = lax.axis_size("help")
    worker = lax.axis_index("blk")
    helper = lax.axis_index("help")
    piece = cached_key_value.shape[0]
    picks = selected.shape[1] * selected.shape[2]
    assert rows == QUERY_GROUP_ROWS and head_group % heads == 0 and selected.shape[0] == 1
    assert BLOCK_TOKENS % piece == 0 and piece % HEAD_SIZE == 0 and picks % HEAD_SIZE == 0
    per_group = piece * helpers // BLOCK_TOKENS
    query_blocks = helpers

    wanted = tuple((t * heads) // head_group for t in range(groups))
    chunks = piece // HEAD_SIZE
    send = pl.pallas_call(
        functools.partial(relayout_kernel, wanted=wanted, chunks=chunks),
        in_specs=[pl.BlockSpec(memory_space=pltpu.VMEM)],
        out_specs=pl.BlockSpec(memory_space=pltpu.VMEM),
        out_shape=jax.ShapeDtypeStruct((groups, 2, chunks, HEAD_SIZE, HEAD_SIZE), jnp.bfloat16),
    )(cached_key_value)
    held = lax.all_to_all(send, "blk", 0, 0, tiled=True)

    q = jnp.transpose(queries.reshape(rows, heads, HEAD_SIZE), (1, 0, 2)).reshape(heads * rows, HEAD_SIZE)
    sel_rows = selected.reshape(picks // HEAD_SIZE, HEAD_SIZE).astype(jnp.bfloat16)
    sel_pad = -(-(picks // HEAD_SIZE) // 16) * 16
    sel_rows = jnp.pad(sel_rows, ((0, sel_pad - picks // HEAD_SIZE), (0, 0)))
    q = jnp.concatenate([q, sel_rows], axis=0)
    q_all = lax.all_gather(q[None], "help", axis=0, tiled=True)
    sel_all = q_all[:, heads * rows:heads * rows + picks // HEAD_SIZE].astype(jnp.int32).reshape(
        query_blocks, selected.shape[1], selected.shape[2])

    kv_head = (worker * heads) // head_group
    own = query_key_value.reshape(rows, 2, KEY_VALUE_HEADS, HEAD_SIZE)
    own = lax.dynamic_index_in_dim(own, kv_head, axis=2, keepdims=False)
    own = jnp.stack([own[:, 0].T, own[:, 1]])

    my_heads = lax.dynamic_slice_in_dim(sel_all, worker * heads, heads, axis=1)
    piece_block = per_group * jnp.arange(groups, dtype=jnp.int32) + (helper * piece) // BLOCK_TOKENS
    hit = jnp.any(my_heads[:, :, None, :] == piece_block[None, None, :, None], axis=3)
    sel_flat = hit.astype(jnp.int32).reshape(-1)
    home = helper.reshape(1).astype(jnp.int32)

    slices = min(2, heads)
    part = heads // slices
    assert part * slices == heads and 2 * part <= STAT_ROWS
    width = part * HEAD_SIZE
    result = None
    for c in range(slices):
        kernel = functools.partial(attend_kernel, groups=groups, heads=part, first=c * part,
                                   all_heads=heads, blocks=query_blocks, chunks=chunks,
                                   factor=scale * math.log2(math.e))
        slots = query_blocks * part
        partial = pl.pallas_call(
            kernel,
            grid_spec=pltpu.PrefetchScalarGridSpec(
                num_scalar_prefetch=2,
                grid=(1,),
                in_specs=[
                    pl.BlockSpec((query_blocks, part * rows, HEAD_SIZE),
                                 lambda i, s, h, c=c: (0, c, 0)),
                    pl.BlockSpec(memory_space=pltpu.VMEM),
                    pl.BlockSpec((2, rows, HEAD_SIZE), lambda i, s, h: (0, 0, 0)),
                ],
                out_specs=pl.BlockSpec((query_blocks, rows + STAT_ROWS, width),
                                       lambda i, s, h: (0, 0, 0)),
                scratch_shapes=[
                    pltpu.VMEM((groups, slots * rows, piece), jnp.float32),
                    pltpu.VMEM((part, rows, rows), jnp.float32),
                    pltpu.VMEM((slots * rows, piece), jnp.bfloat16),
                    pltpu.VMEM((slots, rows, HEAD_SIZE), jnp.float32),
                    pltpu.VMEM((slots, rows, HEAD_SIZE), jnp.float32),
                    pltpu.VMEM((slots, rows, 1), jnp.float32),
                    pltpu.VMEM((slots, rows, HEAD_SIZE), jnp.float32),
                    pltpu.VMEM((rows, HEAD_SIZE), jnp.float32),
                ],
            ),
            compiler_params=pltpu.CompilerParams(vmem_limit_bytes=48 * 1024 * 1024),
            out_shape=jax.ShapeDtypeStruct((query_blocks, rows + STAT_ROWS, width), jnp.float32),
            cost_estimate=pl.CostEstimate(
                flops=4 * query_blocks * part * rows * groups * piece * HEAD_SIZE,
                transcendentals=query_blocks * part * rows * groups * piece,
                bytes_accessed=2 * groups * 2 * piece * HEAD_SIZE + 4 * query_blocks * rows * width),
        )(sel_flat, home, q_all, held, own)
        got = lax.all_to_all(partial, "help", 0, 0, tiled=True)
        first_join = c == 0
        result = pl.pallas_call(
            functools.partial(join_kernel, sources=helpers, heads=part),
            grid=(1,),
            in_specs=[pl.BlockSpec((helpers, rows + STAT_ROWS, width), lambda i: (0, 0, 0))]
            + ([] if first_join else [pl.BlockSpec(memory_space=pl.ANY)]),
            out_specs=pl.BlockSpec((rows, width), lambda i, c=c: (0, c)),
            out_shape=jax.ShapeDtypeStruct((rows, heads * HEAD_SIZE), jnp.float32),
            input_output_aliases={} if first_join else {1: 0},
        )(*((got,) if first_join else (got, result)))
    return result


def solution(mesh):
    in_specs = (P("help", "blk"), P("help", None), P(("blk", "help"), None), P("help", None, None))
    out_specs = P("help", "blk")
    return jax.shard_map(local, mesh=mesh, in_specs=in_specs, out_specs=out_specs, check_vma=False)
```

```python
import functools
import math

import jax
import jax.numpy as jnp
import numpy as np
from jax import lax
from jax.experimental import pallas as pl
from jax.experimental.pallas import tpu as pltpu
from jax.sharding import PartitionSpec as P

HEAD_SIZE = 128
QUERY_HEADS = 64
KEY_VALUE_HEADS = 8
BLOCK_TOKENS = 1024
QUERY_GROUP_ROWS = 128
STAT_ROWS = 8


def relayout_kernel(x_ref, out_ref, *, wanted, chunks):
    for t, kv_head in enumerate(wanted):
        for c in range(chunks):
            tokens = slice(c * HEAD_SIZE, (c + 1) * HEAD_SIZE)
            keys = x_ref[tokens, kv_head * HEAD_SIZE:(kv_head + 1) * HEAD_SIZE]
            out_ref[t, 0, c] = keys.astype(jnp.float32).T.astype(jnp.bfloat16)
            column = (KEY_VALUE_HEADS + kv_head) * HEAD_SIZE
            out_ref[t, 1, c] = x_ref[tokens, column:column + HEAD_SIZE]


def attend_kernel(sel_ref, home_ref, q_ref, kv_ref, own_ref, out_ref,
                  s_buf, own_buf, p_buf, mpart, lpart, m_scr, acc_scr, st_scr,
                  *, groups, heads, first, all_heads, blocks, chunks, factor):
    rows = QUERY_GROUP_ROWS
    slots = blocks * heads
    lanes = HEAD_SIZE
    q = q_ref[...].reshape(slots * rows, HEAD_SIZE)
    home = home_ref[0]
    mpart[...] = jnp.full(mpart.shape, -jnp.inf, jnp.float32)
    lpart[...] = jnp.zeros(lpart.shape, jnp.float32)
    acc_scr[...] = jnp.zeros(acc_scr.shape, jnp.float32)

    def on(slot, g):
        b, h = divmod(slot, heads)
        return sel_ref[(b * all_heads + first + h) * groups + g] != 0

    def fold(x, op):
        out = x[:, :lanes]
        for c in range(1, x.shape[1] // lanes):
            out = op(out, x[:, c * lanes:(c + 1) * lanes])
        return out

    def score(g, carry):
        for c in range(chunks):
            s_buf[g, :, c * HEAD_SIZE:(c + 1) * HEAD_SIZE] = jnp.dot(
                q, kv_ref[g, 0, c], preferred_element_type=jnp.float32)
        for slot in range(slots):
            @pl.when(on(slot, g))
            def _():
                mpart[slot] = jnp.maximum(
                    mpart[slot], fold(s_buf[g, slot * rows:(slot + 1) * rows], jnp.maximum))
        return carry

    lax.fori_loop(0, groups, score, 0)

    for slot in range(slots):
        m = jnp.max(mpart[slot], axis=1, keepdims=True) * factor
        m_scr[slot] = m
        mpart[slot] = jnp.broadcast_to(jnp.where(m == -jnp.inf, 0.0, m), (rows, lanes))

    def mix(g, carry):
        ons = [on(slot, g) for slot in range(slots)]
        for slot in range(slots):
            @pl.when(ons[slot])
            def _():
                p = jnp.exp2(s_buf[g, slot * rows:(slot + 1) * rows] * factor - mpart[slot][:, :1])
                lpart[slot] += fold(p, jnp.add)
                p_buf[slot * rows:(slot + 1) * rows] = p.astype(jnp.bfloat16)

        value = kv_ref[g, 1].reshape(chunks * HEAD_SIZE, HEAD_SIZE)
        pv = jnp.dot(p_buf[...], value, preferred_element_type=jnp.float32)
        for slot in range(slots):
            @pl.when(ons[slot])
            def _():
                acc_scr[slot] += pv[slot * rows:(slot + 1) * rows]
        return carry

    lax.fori_loop(0, groups, mix, 0)

    for b in range(blocks):
        st_scr[...] = jnp.zeros(st_scr.shape, jnp.float32)
        for h in range(heads):
            slot = b * heads + h
            out_ref[b, :rows, h * HEAD_SIZE:(h + 1) * HEAD_SIZE] = acc_scr[slot]
            st_scr[:, h:h + 1] = m_scr[slot]
            st_scr[:, heads + h:heads + h + 1] = jnp.sum(lpart[slot], axis=1, keepdims=True)
        out_ref[b, rows:, :HEAD_SIZE] = st_scr[...].T[:STAT_ROWS]
        if heads > 1:
            out_ref[b, rows:, HEAD_SIZE:] = jnp.zeros((STAT_ROWS, (heads - 1) * HEAD_SIZE), jnp.float32)


def own_kernel(q_ref, own_ref, out_ref, st_scr, *, heads, factor):
    rows = QUERY_GROUP_ROWS
    causal = lax.broadcasted_iota(jnp.int32, (rows, rows), 0) >= lax.broadcasted_iota(
        jnp.int32, (rows, rows), 1)
    for c in range(out_ref.shape[0]):
        st_scr[...] = jnp.zeros(st_scr.shape, jnp.float32)
        for h in range(heads):
            column = (c * heads + h) * HEAD_SIZE
            s = jnp.dot(q_ref[:, column:column + HEAD_SIZE], own_ref[0],
                        preferred_element_type=jnp.float32)
            s = jnp.where(causal, s, -jnp.inf)
            m = jnp.max(s, axis=1, keepdims=True) * factor
            p = jnp.exp2(s * factor - m)
            out_ref[c, :rows, h * HEAD_SIZE:(h + 1) * HEAD_SIZE] = jnp.dot(
                p.astype(jnp.bfloat16), own_ref[1], preferred_element_type=jnp.float32)
            st_scr[:, h:h + 1] = m
            st_scr[:, heads + h:heads + h + 1] = jnp.sum(p, axis=1, keepdims=True)
        out_ref[c, rows:, :HEAD_SIZE] = st_scr[...].T[:STAT_ROWS]
        if heads > 1:
            out_ref[c, rows:, HEAD_SIZE:] = jnp.zeros((STAT_ROWS, (heads - 1) * HEAD_SIZE), jnp.float32)


def join_kernel(got_ref, own_ref, *refs, sources, heads):
    rows = QUERY_GROUP_ROWS
    out_ref = refs[-1]
    blocks = [(got_ref, s) for s in range(sources)] + [(own_ref, 0)]
    cols = [ref[s, rows:, :HEAD_SIZE].T for ref, s in blocks]
    for h in range(heads):
        ms = [c[:, h:h + 1] for c in cols]
        top = ms[0]
        for m in ms[1:]:
            top = jnp.maximum(top, m)
        top = jnp.where(top == -jnp.inf, 0.0, top)
        total = None
        acc = None
        for (ref, s), col, m in zip(blocks, cols, ms):
            fade = jnp.exp2(m - top)
            part_total = fade * col[:, heads + h:heads + h + 1]
            part_acc = fade * ref[s, :rows, h * HEAD_SIZE:(h + 1) * HEAD_SIZE]
            total = part_total if total is None else total + part_total
            acc = part_acc if acc is None else acc + part_acc
        out_ref[:, h * HEAD_SIZE:(h + 1) * HEAD_SIZE] = acc / total


def join(a, b):
    acc_a, m_a, l_a = a
    acc_b, m_b, l_b = b
    m = jnp.maximum(m_a, m_b)
    m_safe = jnp.where(m == -jnp.inf, 0.0, m)
    f_a = jnp.exp2(m_a - m_safe)
    f_b = jnp.exp2(m_b - m_safe)
    acc = acc_a * f_a[..., None] + acc_b * f_b[..., None]
    return acc, m, l_a * f_a + l_b * f_b


def local(queries, query_key_value, cached_key_value, selected):
    rows = queries.shape[0]
    heads = queries.shape[1] // HEAD_SIZE
    head_group = QUERY_HEADS // KEY_VALUE_HEADS
    scale = 1.0 / math.sqrt(HEAD_SIZE)
    groups = lax.axis_size("blk")
    helpers = lax.axis_size("help")
    worker = lax.axis_index("blk")
    helper = lax.axis_index("help")
    piece = cached_key_value.shape[0]
    picks = selected.shape[1] * selected.shape[2]
    assert rows == QUERY_GROUP_ROWS and head_group % heads == 0 and selected.shape[0] == 1
    assert BLOCK_TOKENS % piece == 0 and piece % HEAD_SIZE == 0 and picks % HEAD_SIZE == 0
    per_group = piece * helpers // BLOCK_TOKENS
    query_blocks = helpers

    wanted = tuple((t * heads) // head_group for t in range(groups))
    chunks = piece // HEAD_SIZE
    send = pl.pallas_call(
        functools.partial(relayout_kernel, wanted=wanted, chunks=chunks),
        in_specs=[pl.BlockSpec(memory_space=pltpu.VMEM)],
        out_specs=pl.BlockSpec(memory_space=pltpu.VMEM),
        out_shape=jax.ShapeDtypeStruct((groups, 2, chunks, HEAD_SIZE, HEAD_SIZE), jnp.bfloat16),
    )(cached_key_value)
    held = lax.all_to_all(send, "blk", 0, 0, tiled=True)

    q = jnp.transpose(queries.reshape(rows, heads, HEAD_SIZE), (1, 0, 2)).reshape(heads * rows, HEAD_SIZE)
    sel_rows = selected.reshape(picks // HEAD_SIZE, HEAD_SIZE).astype(jnp.bfloat16)
    sel_pad = -(-(picks // HEAD_SIZE) // 16) * 16
    sel_rows = jnp.pad(sel_rows, ((0, sel_pad - picks // HEAD_SIZE), (0, 0)))
    q = jnp.concatenate([q, sel_rows], axis=0)
    q_all = lax.all_gather(q[None], "help", axis=0, tiled=True)
    sel_all = q_all[:, heads * rows:heads * rows + picks // HEAD_SIZE].astype(jnp.int32).reshape(
        query_blocks, selected.shape[1], selected.shape[2])

    kv_head = (worker * heads) // head_group
    own = query_key_value.reshape(rows, 2, KEY_VALUE_HEADS, HEAD_SIZE)
    own = lax.dynamic_index_in_dim(own, kv_head, axis=2, keepdims=False)
    own = jnp.stack([own[:, 0].T, own[:, 1]])

    my_heads = lax.dynamic_slice_in_dim(sel_all, worker * heads, heads, axis=1)
    piece_block = per_group * jnp.arange(groups, dtype=jnp.int32) + (helper * piece) // BLOCK_TOKENS
    hit = jnp.any(my_heads[:, :, None, :] == piece_block[None, None, :, None], axis=3)
    sel_flat = hit.astype(jnp.int32).reshape(-1)
    home = helper.reshape(1).astype(jnp.int32)

    slices = min(2, heads)
    part = heads // slices
    assert part * slices == heads and 2 * part <= STAT_ROWS
    width = part * HEAD_SIZE
    own_part = pl.pallas_call(
        functools.partial(own_kernel, heads=part, factor=scale * math.log2(math.e)),
        in_specs=[pl.BlockSpec(memory_space=pltpu.VMEM)] * 2,
        out_specs=pl.BlockSpec(memory_space=pltpu.VMEM),
        out_shape=jax.ShapeDtypeStruct((slices, rows + STAT_ROWS, width), jnp.float32),
        scratch_shapes=[pltpu.VMEM((rows, HEAD_SIZE), jnp.float32)],
    )(queries, own)
    result = None
    for c in range(slices):
        kernel = functools.partial(attend_kernel, groups=groups, heads=part, first=c * part,
                                   all_heads=heads, blocks=query_blocks, chunks=chunks,
                                   factor=scale * math.log2(math.e))
        slots = query_blocks * part
        partial = pl.pallas_call(
            kernel,
            grid_spec=pltpu.PrefetchScalarGridSpec(
                num_scalar_prefetch=2,
                grid=(1,),
                in_specs=[
                    pl.BlockSpec((query_blocks, part * rows, HEAD_SIZE),
                                 lambda i, s, h, c=c: (0, c, 0)),
                    pl.BlockSpec((groups, 2, chunks, HEAD_SIZE, HEAD_SIZE),
                                 lambda i, s, h: (0, 0, 0, 0, 0)),
                    pl.BlockSpec((2, rows, HEAD_SIZE), lambda i, s, h: (0, 0, 0)),
                ],
                out_specs=pl.BlockSpec((query_blocks, rows + STAT_ROWS, width),
                                       lambda i, s, h: (0, 0, 0)),
                scratch_shapes=[
                    pltpu.VMEM((groups, slots * rows, piece), jnp.float32),
                    pltpu.VMEM((part, rows, rows), jnp.float32),
                    pltpu.VMEM((slots * rows, piece), jnp.bfloat16),
                    pltpu.VMEM((slots, rows, HEAD_SIZE), jnp.float32),
                    pltpu.VMEM((slots, rows, HEAD_SIZE), jnp.float32),
                    pltpu.VMEM((slots, rows, 1), jnp.float32),
                    pltpu.VMEM((slots, rows, HEAD_SIZE), jnp.float32),
                    pltpu.VMEM((rows, HEAD_SIZE), jnp.float32),
                ],
            ),
            compiler_params=pltpu.CompilerParams(vmem_limit_bytes=48 * 1024 * 1024),
            out_shape=jax.ShapeDtypeStruct((query_blocks, rows + STAT_ROWS, width), jnp.float32),
            cost_estimate=pl.CostEstimate(
                flops=4 * query_blocks * part * rows * groups * piece * HEAD_SIZE,
                transcendentals=query_blocks * part * rows * groups * piece,
                bytes_accessed=2 * groups * 2 * piece * HEAD_SIZE + 4 * query_blocks * rows * width),
        )(sel_flat, home, q_all, held, own)
        got = lax.all_to_all(partial, "help", 0, 0, tiled=True)
        first_join = c == 0
        result = pl.pallas_call(
            functools.partial(join_kernel, sources=helpers, heads=part),
            grid=(1,),
            in_specs=[pl.BlockSpec((helpers, rows + STAT_ROWS, width), lambda i: (0, 0, 0)),
                      pl.BlockSpec((1, rows + STAT_ROWS, width), lambda i, c=c: (c, 0, 0))]
            + ([] if first_join else [pl.BlockSpec(memory_space=pl.ANY)]),
            out_specs=pl.BlockSpec((rows, width), lambda i, c=c: (0, c)),
            out_shape=jax.ShapeDtypeStruct((rows, heads * HEAD_SIZE), jnp.float32),
            input_output_aliases={} if first_join else {2: 0},
        )(*((got, own_part) if first_join else (got, own_part, result)))
    return result


def solution(mesh):
    in_specs = (P("help", "blk"), P("help", None), P(("blk", "help"), None), P("help", None, None))
    out_specs = P("help", "blk")
    return jax.shard_map(local, mesh=mesh, in_specs=in_specs, out_specs=out_specs, check_vma=False)
```

```python
import functools
import math

import jax
import jax.numpy as jnp
import numpy as np
from jax import lax
from jax.experimental import pallas as pl
from jax.experimental.pallas import tpu as pltpu
from jax.sharding import PartitionSpec as P

HEAD_SIZE = 128
QUERY_HEADS = 64
KEY_VALUE_HEADS = 8
BLOCK_TOKENS = 1024
QUERY_GROUP_ROWS = 128
STAT_ROWS = 8


def relayout_kernel(x_ref, q_ref, sel_ref, out_ref, q_out_ref, *, wanted, chunks, heads):
    rows = QUERY_GROUP_ROWS
    for h in range(heads):
        q_out_ref[h * rows:(h + 1) * rows] = q_ref[:, h * HEAD_SIZE:(h + 1) * HEAD_SIZE]
    q_out_ref[heads * rows:] = sel_ref[...]
    for t, kv_head in enumerate(wanted):
        for c in range(chunks):
            tokens = slice(c * HEAD_SIZE, (c + 1) * HEAD_SIZE)
            keys = x_ref[tokens, kv_head * HEAD_SIZE:(kv_head + 1) * HEAD_SIZE]
            out_ref[t, 0, c] = keys.astype(jnp.float32).T.astype(jnp.bfloat16)
            column = (KEY_VALUE_HEADS + kv_head) * HEAD_SIZE
            out_ref[t, 1, c] = x_ref[tokens, column:column + HEAD_SIZE]


def attend_kernel(sel_ref, home_ref, q_ref, kv_ref, own_ref, out_ref,
                  s_buf, own_buf, p_buf, mpart, lpart, m_scr, acc_scr, st_scr,
                  *, groups, heads, first, all_heads, blocks, chunks, factor):
    rows = QUERY_GROUP_ROWS
    slots = blocks * heads
    lanes = HEAD_SIZE
    q = q_ref[...].reshape(slots * rows, HEAD_SIZE)
    home = home_ref[0]
    mpart[...] = jnp.full(mpart.shape, -jnp.inf, jnp.float32)
    lpart[...] = jnp.zeros(lpart.shape, jnp.float32)
    acc_scr[...] = jnp.zeros(acc_scr.shape, jnp.float32)

    def on(slot, g):
        b, h = divmod(slot, heads)
        return sel_ref[(b * all_heads + first + h) * groups + g] != 0

    def fold(x, op):
        out = x[:, :lanes]
        for c in range(1, x.shape[1] // lanes):
            out = op(out, x[:, c * lanes:(c + 1) * lanes])
        return out

    def score(g, carry):
        for c in range(chunks):
            s_buf[g, :, c * HEAD_SIZE:(c + 1) * HEAD_SIZE] = jnp.dot(
                q, kv_ref[g, 0, c], preferred_element_type=jnp.float32)
        for slot in range(slots):
            @pl.when(on(slot, g))
            def _():
                mpart[slot] = jnp.maximum(
                    mpart[slot], fold(s_buf[g, slot * rows:(slot + 1) * rows], jnp.maximum))
        return carry

    lax.fori_loop(0, groups, score, 0)

    for slot in range(slots):
        m = jnp.max(mpart[slot], axis=1, keepdims=True) * factor
        m_scr[slot] = m
        mpart[slot] = jnp.broadcast_to(jnp.where(m == -jnp.inf, 0.0, m), (rows, lanes))

    def mix(g, carry):
        ons = [on(slot, g) for slot in range(slots)]
        for slot in range(slots):
            @pl.when(ons[slot])
            def _():
                p = jnp.exp2(s_buf[g, slot * rows:(slot + 1) * rows] * factor - mpart[slot][:, :1])
                lpart[slot] += fold(p, jnp.add)
                p_buf[slot * rows:(slot + 1) * rows] = p.astype(jnp.bfloat16)

        value = kv_ref[g, 1].reshape(chunks * HEAD_SIZE, HEAD_SIZE)
        pv = jnp.dot(p_buf[...], value, preferred_element_type=jnp.float32)
        for slot in range(slots):
            @pl.when(ons[slot])
            def _():
                acc_scr[slot] += pv[slot * rows:(slot + 1) * rows]
        return carry

    lax.fori_loop(0, groups, mix, 0)

    for b in range(blocks):
        st_scr[...] = jnp.zeros(st_scr.shape, jnp.float32)
        for h in range(heads):
            slot = b * heads + h
            out_ref[b, :rows, h * HEAD_SIZE:(h + 1) * HEAD_SIZE] = acc_scr[slot]
            st_scr[:, h:h + 1] = m_scr[slot]
            st_scr[:, heads + h:heads + h + 1] = jnp.sum(lpart[slot], axis=1, keepdims=True)
        out_ref[b, rows:, :HEAD_SIZE] = st_scr[...].T[:STAT_ROWS]
        if heads > 1:
            out_ref[b, rows:, HEAD_SIZE:] = jnp.zeros((STAT_ROWS, (heads - 1) * HEAD_SIZE), jnp.float32)


def own_kernel(q_ref, own_ref, out_ref, st_scr, *, heads, factor):
    rows = QUERY_GROUP_ROWS
    causal = lax.broadcasted_iota(jnp.int32, (rows, rows), 0) >= lax.broadcasted_iota(
        jnp.int32, (rows, rows), 1)
    for c in range(out_ref.shape[0]):
        st_scr[...] = jnp.zeros(st_scr.shape, jnp.float32)
        for h in range(heads):
            column = (c * heads + h) * HEAD_SIZE
            s = jnp.dot(q_ref[:, column:column + HEAD_SIZE], own_ref[0],
                        preferred_element_type=jnp.float32)
            s = jnp.where(causal, s, -jnp.inf)
            m = jnp.max(s, axis=1, keepdims=True) * factor
            p = jnp.exp2(s * factor - m)
            out_ref[c, :rows, h * HEAD_SIZE:(h + 1) * HEAD_SIZE] = jnp.dot(
                p.astype(jnp.bfloat16), own_ref[1], preferred_element_type=jnp.float32)
            st_scr[:, h:h + 1] = m
            st_scr[:, heads + h:heads + h + 1] = jnp.sum(p, axis=1, keepdims=True)
        out_ref[c, rows:, :HEAD_SIZE] = st_scr[...].T[:STAT_ROWS]
        if heads > 1:
            out_ref[c, rows:, HEAD_SIZE:] = jnp.zeros((STAT_ROWS, (heads - 1) * HEAD_SIZE), jnp.float32)


def join_kernel(got_ref, own_ref, *refs, sources, heads):
    rows = QUERY_GROUP_ROWS
    out_ref = refs[-1]
    blocks = [(got_ref, s) for s in range(sources)] + [(own_ref, 0)]
    cols = [ref[s, rows:, :HEAD_SIZE].T for ref, s in blocks]
    for h in range(heads):
        ms = [c[:, h:h + 1] for c in cols]
        top = ms[0]
        for m in ms[1:]:
            top = jnp.maximum(top, m)
        top = jnp.where(top == -jnp.inf, 0.0, top)
        total = None
        acc = None
        for (ref, s), col, m in zip(blocks, cols, ms):
            fade = jnp.exp2(m - top)
            part_total = fade * col[:, heads + h:heads + h + 1]
            part_acc = fade * ref[s, :rows, h * HEAD_SIZE:(h + 1) * HEAD_SIZE]
            total = part_total if total is None else total + part_total
            acc = part_acc if acc is None else acc + part_acc
        out_ref[:, h * HEAD_SIZE:(h + 1) * HEAD_SIZE] = acc / total


def join(a, b):
    acc_a, m_a, l_a = a
    acc_b, m_b, l_b = b
    m = jnp.maximum(m_a, m_b)
    m_safe = jnp.where(m == -jnp.inf, 0.0, m)
    f_a = jnp.exp2(m_a - m_safe)
    f_b = jnp.exp2(m_b - m_safe)
    acc = acc_a * f_a[..., None] + acc_b * f_b[..., None]
    return acc, m, l_a * f_a + l_b * f_b


def local(queries, query_key_value, cached_key_value, selected):
    rows = queries.shape[0]
    heads = queries.shape[1] // HEAD_SIZE
    head_group = QUERY_HEADS // KEY_VALUE_HEADS
    scale = 1.0 / math.sqrt(HEAD_SIZE)
    groups = lax.axis_size("blk")
    helpers = lax.axis_size("help")
    worker = lax.axis_index("blk")
    helper = lax.axis_index("help")
    piece = cached_key_value.shape[0]
    picks = selected.shape[1] * selected.shape[2]
    assert rows == QUERY_GROUP_ROWS and head_group % heads == 0 and selected.shape[0] == 1
    assert BLOCK_TOKENS % piece == 0 and piece % HEAD_SIZE == 0 and picks % HEAD_SIZE == 0
    per_group = piece * helpers // BLOCK_TOKENS
    query_blocks = helpers

    wanted = tuple((t * heads) // head_group for t in range(groups))
    chunks = piece // HEAD_SIZE
    sel_rows = selected.reshape(picks // HEAD_SIZE, HEAD_SIZE).astype(jnp.bfloat16)
    sel_pad = -(-(picks // HEAD_SIZE) // 16) * 16
    sel_rows = jnp.pad(sel_rows, ((0, sel_pad - picks // HEAD_SIZE), (0, 0)))
    send, q = pl.pallas_call(
        functools.partial(relayout_kernel, wanted=wanted, chunks=chunks, heads=heads),
        in_specs=[pl.BlockSpec(memory_space=pltpu.VMEM)] * 3,
        out_specs=[pl.BlockSpec(memory_space=pltpu.VMEM)] * 2,
        out_shape=[jax.ShapeDtypeStruct((groups, 2, chunks, HEAD_SIZE, HEAD_SIZE), jnp.bfloat16),
                   jax.ShapeDtypeStruct((heads * rows + sel_pad, HEAD_SIZE), jnp.bfloat16)],
    )(cached_key_value, queries, sel_rows)
    held = lax.all_to_all(send, "blk", 0, 0, tiled=True)

    q_all = lax.all_gather(q[None], "help", axis=0, tiled=True)
    sel_all = q_all[:, heads * rows:heads * rows + picks // HEAD_SIZE].astype(jnp.int32).reshape(
        query_blocks, selected.shape[1], selected.shape[2])

    kv_head = (worker * heads) // head_group
    own = query_key_value.reshape(rows, 2, KEY_VALUE_HEADS, HEAD_SIZE)
    own = lax.dynamic_index_in_dim(own, kv_head, axis=2, keepdims=False)
    own = jnp.stack([own[:, 0].T, own[:, 1]])

    my_heads = lax.dynamic_slice_in_dim(sel_all, worker * heads, heads, axis=1)
    piece_block = per_group * jnp.arange(groups, dtype=jnp.int32) + (helper * piece) // BLOCK_TOKENS
    hit = jnp.any(my_heads[:, :, None, :] == piece_block[None, None, :, None], axis=3)
    sel_flat = hit.astype(jnp.int32).reshape(-1)
    home = helper.reshape(1).astype(jnp.int32)

    slices = min(2, heads)
    part = heads // slices
    assert part * slices == heads and 2 * part <= STAT_ROWS
    width = part * HEAD_SIZE
    own_part = pl.pallas_call(
        functools.partial(own_kernel, heads=part, factor=scale * math.log2(math.e)),
        in_specs=[pl.BlockSpec(memory_space=pltpu.VMEM)] * 2,
        out_specs=pl.BlockSpec(memory_space=pltpu.VMEM),
        out_shape=jax.ShapeDtypeStruct((slices, rows + STAT_ROWS, width), jnp.float32),
        scratch_shapes=[pltpu.VMEM((rows, HEAD_SIZE), jnp.float32)],
    )(queries, own)
    result = None
    for c in range(slices):
        kernel = functools.partial(attend_kernel, groups=groups, heads=part, first=c * part,
                                   all_heads=heads, blocks=query_blocks, chunks=chunks,
                                   factor=scale * math.log2(math.e))
        slots = query_blocks * part
        partial = pl.pallas_call(
            kernel,
            grid_spec=pltpu.PrefetchScalarGridSpec(
                num_scalar_prefetch=2,
                grid=(1,),
                in_specs=[
                    pl.BlockSpec((query_blocks, part * rows, HEAD_SIZE),
                                 lambda i, s, h, c=c: (0, c, 0)),
                    pl.BlockSpec((groups, 2, chunks, HEAD_SIZE, HEAD_SIZE),
                                 lambda i, s, h: (0, 0, 0, 0, 0)),
                    pl.BlockSpec((2, rows, HEAD_SIZE), lambda i, s, h: (0, 0, 0)),
                ],
                out_specs=pl.BlockSpec((query_blocks, rows + STAT_ROWS, width),
                                       lambda i, s, h: (0, 0, 0)),
                scratch_shapes=[
                    pltpu.VMEM((groups, slots * rows, piece), jnp.float32),
                    pltpu.VMEM((part, rows, rows), jnp.float32),
                    pltpu.VMEM((slots * rows, piece), jnp.bfloat16),
                    pltpu.VMEM((slots, rows, HEAD_SIZE), jnp.float32),
                    pltpu.VMEM((slots, rows, HEAD_SIZE), jnp.float32),
                    pltpu.VMEM((slots, rows, 1), jnp.float32),
                    pltpu.VMEM((slots, rows, HEAD_SIZE), jnp.float32),
                    pltpu.VMEM((rows, HEAD_SIZE), jnp.float32),
                ],
            ),
            compiler_params=pltpu.CompilerParams(vmem_limit_bytes=48 * 1024 * 1024),
            out_shape=jax.ShapeDtypeStruct((query_blocks, rows + STAT_ROWS, width), jnp.float32),
            cost_estimate=pl.CostEstimate(
                flops=4 * query_blocks * part * rows * groups * piece * HEAD_SIZE,
                transcendentals=query_blocks * part * rows * groups * piece,
                bytes_accessed=2 * groups * 2 * piece * HEAD_SIZE + 4 * query_blocks * rows * width),
        )(sel_flat, home, q_all, held, own)
        got = lax.all_to_all(partial, "help", 0, 0, tiled=True)
        first_join = c == 0
        result = pl.pallas_call(
            functools.partial(join_kernel, sources=helpers, heads=part),
            grid=(1,),
            in_specs=[pl.BlockSpec((helpers, rows + STAT_ROWS, width), lambda i: (0, 0, 0)),
                      pl.BlockSpec((1, rows + STAT_ROWS, width), lambda i, c=c: (c, 0, 0))]
            + ([] if first_join else [pl.BlockSpec(memory_space=pl.ANY)]),
            out_specs=pl.BlockSpec((rows, width), lambda i, c=c: (0, c)),
            out_shape=jax.ShapeDtypeStruct((rows, heads * HEAD_SIZE), jnp.float32),
            input_output_aliases={} if first_join else {2: 0},
        )(*((got, own_part) if first_join else (got, own_part, result)))
    return result


def solution(mesh):
    in_specs = (P("help", "blk"), P("help", None), P(("blk", "help"), None), P("help", None, None))
    out_specs = P("help", "blk")
    return jax.shard_map(local, mesh=mesh, in_specs=in_specs, out_specs=out_specs, check_vma=False)
```
